32 devices in a mesh: groups: 2 (over x), stream: 8 (over z, y), section: 2 (over core).
Axes of the slice: x: 2, y: 2, z: 4, core: 2. Of those that a mesh axis runs over, the one named last changes fastest.
Arguments:
- new_frames: bfloat16 [256, 16, 1024], P(('groups', 'stream')), parts along dimension 0, may hold values from -6 to 6
- valid_counts: int32 [256], P('groups'), parts along dimension 0, may hold values from 1 to 16
- anchor: int32 [256], P('groups'), parts along dimension 0, may hold values from 0 to 127, as said below
- context_cache: bfloat16 [2, 256, 12, 2048], P('section', ('groups', 'stream')), parts along dimension 1, may hold values from -240 to 240
- conv_state: bfloat16 [2, 256, 30, 1024], P('section', ('groups', 'stream')), parts along dimension 1, may hold values from -6 to 6
- qkv_weight: bfloat16 [2, 1024, 3072], P('section'), may hold values from -0.1875 to 0.1875
- out_weight: bfloat16 [2, 1024, 1024], P('section'), may hold values from -0.1875 to 0.1875
- conv_weight: float32 [2, 31, 1024], P('section'), may hold values from -1 to 1
Outputs:
- layer_outputs: bfloat16 [2, 256, 16, 1024], P('section', ('groups', 'stream')), parts along dimension 1
The draws below stay inside these ranges and needn't reach their ends.
There are 2 independent parts, one for each index of `groups`. The reference program is written for one: setup_inputs(seed, part) draws one part's arguments, and reference() takes and returns one part's arrays. A program takes and returns all parts, laid end to end along the dimension named above; an argument that names none is the same for every part. Nothing has to cross between parts.
Inputs may be any that keep to these rules, and one draw needn't show every extreme that they name: anchor is a permutation of the 128 slots. New slot j lies on host j // 16, old slot o on host o // 16. Exactly 7 streams leave each host and 7 arrive at it; from one old host to one other new host moves at most one stream. A stream that stays on its host keeps its slot.
All inputs are finite; a program needn't handle non-finite values.
Results may differ from the reference program's by a relative error of at most 0.0094.
Values may be sent and summed in bfloat16 or wider, within the bound.
No kernel may reach another device: no remote copies, remote signals or barrier semaphores. Data moves between devices by JAX's collectives and lax.ppermute only.
A program may use at most 128 MiB of HBM per device.

```python
import jax
import jax.numpy as jnp
from jax import lax

D = 1024
HEADS = 16
KW = 31
FRAMES = 16
CTX = 12
S_DEV = 16
HOSTS = 8
MOVE = 7
STREAMS = 128
LAYERS = 2


def draw_anchor(key, part):
    key_label, key_offset, key_local = jax.random.split(jax.random.fold_in(key, 3), 3)
    relabel = jax.random.permutation(key_label, HOSTS).astype(jnp.int32)
    inverse = jnp.argsort(relabel).astype(jnp.int32)
    offsets = (jax.random.permutation(key_offset, HOSTS - 1).astype(jnp.int32) + 1)[:MOVE]
    local_keys = jax.random.randint(key_local, (HOSTS, S_DEV), 0, 1024, dtype=jnp.int32) * S_DEV + jnp.arange(S_DEV, dtype=jnp.int32)[None, :]
    movers = jnp.argsort(local_keys, axis=1).astype(jnp.int32)[:, :MOVE]
    host_ids = jnp.arange(HOSTS, dtype=jnp.int32)
    source = relabel[(inverse[:, None] - offsets[None, :]) % HOSTS]
    mover_ids = jnp.arange(MOVE, dtype=jnp.int32)[None, :]
    target_slots = host_ids[:, None] * S_DEV + movers
    source_slots = source * S_DEV + movers[source, mover_ids]
    anchor = jnp.arange(STREAMS, dtype=jnp.int32)
    anchor = anchor.at[target_slots.reshape(-1)].set(source_slots.reshape(-1).astype(jnp.int32))
    return anchor.astype(jnp.int32)


def draw_context_cache(key, part):
    key_base = jax.random.fold_in(jax.random.fold_in(key, 7), 0)
    entries = jnp.clip(jax.random.normal(key_base, (LAYERS, STREAMS, CTX, 2 * D), jnp.float32), -6.0, 6.0)
    return entries.astype(jnp.bfloat16)


def touch_ends(values, own_key, low, top_value):
    dims = values.shape
    index_at = [jax.random.randint(jax.random.fold_in(own_key, axis), (), 0, dims[axis]) for axis in range(len(dims))]
    values = values.at[tuple(index_at)].set(low)
    longest = dims.index(max(dims))
    index_at[longest] = (index_at[longest] + 1) % dims[longest]
    return values.at[tuple(index_at)].set(top_value)


def steps_of(own_key, shape, cuts, smallest, top_value):
    level, own = 1.0, jax.random.fold_in(own_key, 6)
    for axis_at, blocks in cuts:
        draws = jnp.exp(jax.random.uniform(jax.random.fold_in(own, axis_at), (blocks,), jnp.float32, smallest / len(cuts), top_value / len(cuts)))
        level = level * jnp.repeat(draws, shape[axis_at] // blocks).reshape([-1 if axis == axis_at else 1 for axis in range(len(shape))])
    return level


def normal_values(key, extent, spread, reach, cuts=(), kind=jnp.bfloat16):
    level = steps_of(key, extent, cuts, -0.22, 0.18) if cuts else 1.0
    result = jax.random.normal(key, extent, jnp.float32) * spread * level
    return jnp.minimum(jnp.maximum(result, -reach), reach).astype(kind)


def setup_inputs(seed: int = 0, part: int = 0) -> dict:
    streams_of = jax.random.split(jax.random.key(seed), 9)
    part_splits = jax.random.split(jax.random.fold_in(streams_of[8], part), 9)
    new_frames = normal_values(part_splits[0], (STREAMS, FRAMES, D), 1.0, 6.0, ((0, 8),))
    valid_counts = touch_ends(jax.random.randint(part_splits[1], (STREAMS,), 1, FRAMES + 1), jax.random.fold_in(part_splits[1], 1), 1, FRAMES).astype(jnp.int32)
    anchor = draw_anchor(jax.random.fold_in(jax.random.fold_in(streams_of[8], part), 71), part)
    context_cache = draw_context_cache(jax.random.fold_in(jax.random.fold_in(streams_of[8], part), 71), part)
    conv_state = normal_values(part_splits[4], (LAYERS, STREAMS, KW - 1, D), 1.0, 6.0, ((0, 2), (1, 8)))
    qkv_weight = normal_values(streams_of[5], (LAYERS, D, 3 * D), D ** -0.5, 0.1875, ((0, 2),))
    out_weight = normal_values(streams_of[6], (LAYERS, D, D), D ** -0.5, 0.1875, ((0, 2),))
    conv_weight = normal_values(streams_of[7], (LAYERS, KW, D), KW ** -0.5, 1.0, ((0, 2),), jnp.float32)
    return dict(new_frames=new_frames, valid_counts=valid_counts, anchor=anchor, context_cache=context_cache, conv_state=conv_state, qkv_weight=qkv_weight, out_weight=out_weight, conv_weight=conv_weight)


def encoder_layer(inputs, valid_counts, context, conv_state, qkv_weight, out_weight, conv_weight):
    stream_count, frame_count, model_width = inputs.shape
    head_size = model_width // HEADS
    live_mask = jnp.arange(frame_count, dtype=jnp.int32)[None, :] < valid_counts[:, None]
    floats = inputs.astype(jnp.float32)
    centred = floats - lax.optimization_barrier(jnp.mean(floats, axis=-1, keepdims=True))
    variance = lax.optimization_barrier(jnp.mean(centred * centred, axis=-1, keepdims=True))
    normed = (centred * lax.rsqrt(variance + 1e-05)).astype(jnp.bfloat16)
    projected = jnp.dot(normed.reshape(-1, model_width), qkv_weight, preferred_element_type=jnp.float32)
    projected = projected.reshape(stream_count, frame_count, 3 * model_width)
    queries = (projected[:, :, :model_width] * head_size ** (-0.5)).astype(jnp.bfloat16)
    new_keys = projected[:, :, model_width:2 * model_width].astype(jnp.bfloat16)
    new_values = projected[:, :, 2 * model_width:].astype(jnp.bfloat16)
    keys_all = jnp.concatenate([context[:, :, :model_width], new_keys], axis=1)
    values_all = jnp.concatenate([context[:, :, model_width:], new_values], axis=1)
    key_total = keys_all.shape[1]
    queries_split = queries.reshape(stream_count, frame_count, HEADS, head_size).astype(jnp.float32)
    keys_split = keys_all.reshape(stream_count, key_total, HEADS, head_size).astype(jnp.float32)
    values_split = values_all.reshape(stream_count, key_total, HEADS, head_size).astype(jnp.float32)
    scores = jnp.einsum('bqhd,bkhd->bhqk', queries_split, keys_split)
    key_mask = jnp.concatenate([jnp.ones((stream_count, key_total - frame_count), dtype=bool), live_mask], axis=1)
    scores = jnp.where(key_mask[:, None, None, :], scores, jnp.float32(-1e+30))
    top_score = lax.optimization_barrier(jnp.max(scores, axis=-1, keepdims=True))
    exponent = jnp.exp(scores - top_score)
    softmax_weights = (exponent / lax.optimization_barrier(jnp.sum(exponent, axis=-1, keepdims=True))).astype(jnp.bfloat16)
    attended = jnp.einsum('bhqk,bkhd->bqhd', softmax_weights.astype(jnp.float32), values_split)
    attended = attended.reshape(stream_count * frame_count, model_width).astype(jnp.bfloat16)
    mixed = jnp.dot(attended, out_weight, preferred_element_type=jnp.float32)
    residual_sum = floats + mixed.reshape(stream_count, frame_count, model_width)
    rounded = lax.optimization_barrier(residual_sum.astype(jnp.bfloat16))
    padded_input = jnp.concatenate([conv_state, rounded], axis=1).astype(jnp.float32)
    convolved = jnp.zeros((stream_count, frame_count, model_width), jnp.float32)
    for tap_index in range(conv_weight.shape[0]):
        convolved = convolved + conv_weight[tap_index][None, None, :] * padded_input[:, tap_index:tap_index + frame_count, :]
    output = (residual_sum + jax.nn.silu(convolved)) * live_mask[:, :, None].astype(jnp.float32)
    return output.astype(jnp.bfloat16)

def reference(new_frames, valid_counts, anchor, context_cache, conv_state, qkv_weight, out_weight, conv_weight):
    current = new_frames
    results = []
    for layer_index in range(LAYERS):
        moved_context = jnp.take(context_cache[layer_index], anchor, axis=0)
        moved_conv = jnp.take(conv_state[layer_index], anchor, axis=0)
        current = encoder_layer(current, valid_counts, moved_context, moved_conv, qkv_weight[layer_index], out_weight[layer_index], conv_weight[layer_index])
        results.append(current)
    return jnp.stack(results)
```

```python
import functools

import jax
import jax.numpy as jnp
from jax import lax
from jax.experimental import pallas as pl
from jax.experimental.pallas import tpu as pltpu
from jax.sharding import PartitionSpec as P

HEADS = 16


def shifted(value, axis, steps):
    count = lax.axis_size(axis)
    leading, last = (max(0, -steps), min(count, count - steps))
    return lax.ppermute(value, axis, [(source, source + steps) for source in range(leading, last)])


def layer_kernel(x_ref, klive_ref, rlive_ref, ck_ref, cv_ref, cst_ref, wq_ref, wk_ref, wv_ref,
                 wo_ref, cw_ref, out_ref, nrm_ref, acc_ref, bc_ref, bn_ref, pad_ref,
                 *, streams, frames, ctx, head_size):
    step = pl.program_id(0)
    tokens = streams * frames
    width = x_ref.shape[1]
    pair = wq_ref.shape[1]

    @pl.when(step == 0)
    def _():
        floats = x_ref[...].astype(jnp.float32)
        centred = floats - jnp.mean(floats, axis=-1, keepdims=True)
        variance = jnp.mean(centred * centred, axis=-1, keepdims=True)
        nrm_ref[...] = (centred * lax.rsqrt(variance + 1e-05)).astype(jnp.bfloat16)
        acc_ref[...] = jnp.zeros_like(acc_ref)
        q_stream = lax.broadcasted_iota(jnp.int32, (tokens, streams * ctx), 0) // frames
        c_col = lax.broadcasted_iota(jnp.int32, (tokens, streams * ctx), 1)
        same_c = (c_col >= q_stream * ctx) & (c_col < q_stream * ctx + ctx)
        bc_ref[...] = jnp.where(same_c, 0.0, -1e30).astype(jnp.float32)
        q_stream_n = lax.broadcasted_iota(jnp.int32, (tokens, tokens), 0) // frames
        k_stream_n = lax.broadcasted_iota(jnp.int32, (tokens, tokens), 1) // frames
        same_n = (q_stream_n == k_stream_n) & (klive_ref[...] > 0.0)
        bn_ref[...] = jnp.where(same_n, 0.0, -1e30).astype(jnp.float32)

    normed = nrm_ref[...]
    q = jnp.dot(normed, wq_ref[...], preferred_element_type=jnp.float32)
    q = (q * (head_size ** -0.5)).astype(jnp.bfloat16)
    k = jnp.dot(normed, wk_ref[...], preferred_element_type=jnp.float32).astype(jnp.bfloat16)
    v = jnp.dot(normed, wv_ref[...], preferred_element_type=jnp.float32).astype(jnp.bfloat16)
    ck = ck_ref[...]
    cv = cv_ref[...]
    lane = lax.broadcasted_iota(jnp.int32, (tokens, pair), 1)
    nt = (((1,), (1,)), ((), ()))
    outs = []
    for half in range(pair // head_size):
        mine = (lane >= half * head_size) & (lane < (half + 1) * head_size)
        qh = jnp.where(mine, q, jnp.zeros_like(q))
        sc = lax.dot_general(qh, ck, nt, preferred_element_type=jnp.float32) + bc_ref[...]
        sn = lax.dot_general(qh, k, nt, preferred_element_type=jnp.float32) + bn_ref[...]
        top = jnp.maximum(jnp.max(sc, axis=-1, keepdims=True), jnp.max(sn, axis=-1, keepdims=True))
        ec = jnp.exp(sc - top)
        en = jnp.exp(sn - top)
        total = jnp.sum(ec, axis=-1, keepdims=True) + jnp.sum(en, axis=-1, keepdims=True)
        pc = (ec / total).astype(jnp.bfloat16)
        pn = (en / total).astype(jnp.bfloat16)
        oh = jnp.dot(pc, cv, preferred_element_type=jnp.float32) + jnp.dot(
            pn, v, preferred_element_type=jnp.float32)
        outs.append((mine, oh))
    attended = outs[-1][1]
    for mine, oh in outs[:-1]:
        attended = jnp.where(mine, oh, attended)
    attended = attended.astype(jnp.bfloat16)
    acc_ref[...] += jnp.dot(attended, wo_ref[...], preferred_element_type=jnp.float32)

    @pl.when(step == pl.num_programs(0) - 1)
    def _():
        kept = cst_ref.shape[1]
        lead = pad_ref.shape[1] - frames - kept
        residual = x_ref[...].astype(jnp.float32) + acc_ref[...]
        acc_ref[...] = residual
        rounded = residual.astype(jnp.bfloat16).astype(jnp.float32)
        pad_ref[:, lead:lead + kept, :] = cst_ref[...].astype(jnp.float32)
        pad_ref[:, lead + kept:, :] = rounded.reshape(streams, frames, width)
        taps = cw_ref.shape[0]
        chunk = 128
        for c in range(width // chunk):
            cols = slice(c * chunk, (c + 1) * chunk)
            conv = jnp.zeros((streams, frames, chunk), jnp.float32)
            for j in range(taps):
                conv = conv + cw_ref[j:j + 1, cols].reshape(1, 1, chunk) * pad_ref[
                    :, lead + j:lead + j + frames, cols]
            res = acc_ref[:, cols].reshape(streams, frames, chunk)
            silu = conv / (1.0 + jnp.exp(-conv))
            live = rlive_ref[...].reshape(streams, frames, 1)
            out = (res + silu) * live
            out_ref[:, cols] = out.reshape(tokens, chunk).astype(out_ref.dtype)


def encoder_layer(inputs, valid_counts, context, conv_state, qkv_weight, out_weight, conv_weight):
    streams, frames, width = inputs.shape
    ctx = context.shape[1]
    kept = conv_state.shape[1]
    head_size = width // HEADS
    pair = 2 * head_size
    pairs = width // pair
    tokens = streams * frames
    live = (jnp.arange(frames, dtype=jnp.int32)[None, :] < valid_counts[:, None]).astype(jnp.float32)
    klive = live.reshape(1, tokens)
    rlive = live.reshape(tokens, 1)
    x = inputs.reshape(tokens, width)
    ctx2 = context.reshape(streams * ctx, 2 * width)
    lead = (-(kept + frames)) % 8
    kernel = functools.partial(layer_kernel, streams=streams, frames=frames, ctx=ctx,
                               head_size=head_size)
    const = lambda p: (0, 0)
    out = pl.pallas_call(
        kernel,
        out_shape=jax.ShapeDtypeStruct((tokens, width), jnp.bfloat16),
        grid=(pairs,),
        in_specs=[
            pl.BlockSpec((tokens, width), const),
            pl.BlockSpec((1, tokens), const),
            pl.BlockSpec((tokens, 1), const),
            pl.BlockSpec((streams * ctx, pair), lambda p: (0, p)),
            pl.BlockSpec((streams * ctx, pair), lambda p: (0, pairs + p)),
            pl.BlockSpec((streams, kept, width), lambda p: (0, 0, 0)),
            pl.BlockSpec((width, pair), lambda p: (0, p)),
            pl.BlockSpec((width, pair), lambda p: (0, pairs + p)),
            pl.BlockSpec((width, pair), lambda p: (0, 2 * pairs + p)),
            pl.BlockSpec((pair, width), lambda p: (p, 0)),
            pl.BlockSpec(conv_weight.shape, const),
        ],
        out_specs=pl.BlockSpec((tokens, width), const),
        scratch_shapes=[
            pltpu.VMEM((tokens, width), jnp.bfloat16),
            pltpu.VMEM((tokens, width), jnp.float32),
            pltpu.VMEM((tokens, streams * ctx), jnp.float32),
            pltpu.VMEM((tokens, tokens), jnp.float32),
            pltpu.VMEM((streams, lead + kept + frames, width), jnp.float32),
        ],
        compiler_params=pltpu.CompilerParams(dimension_semantics=("arbitrary",)),
    )(x, klive, rlive, ctx2, ctx2, conv_state, qkv_weight, qkv_weight, qkv_weight, out_weight,
      conv_weight)
    return out.reshape(streams, frames, width)


def routing(anchor, own_index, local_count):
    stream_total = anchor.shape[0]
    every_slot = jnp.arange(stream_total, dtype=jnp.int32)
    newpos = jnp.sum(
        jnp.where(anchor[None, :] == every_slot[:, None], every_slot[None, :], 0), axis=1
    )
    mine_new = lax.dynamic_slice_in_dim(newpos, own_index * local_count, local_count)
    mine_old = lax.dynamic_slice_in_dim(anchor, own_index * local_count, local_count)
    return (mine_new // local_count, mine_old // local_count, mine_new, mine_old)


def pack_rows(rows, hosts, own_index, slot_total):
    places = jnp.where(hosts == own_index, slot_total, hosts)
    return jnp.zeros((slot_total,) + rows.shape[1:], rows.dtype).at[places].set(rows, mode="drop")


def pick_rows(buffer, local_rows, hosts, own_index, local_index):
    from_buffer = jnp.take(buffer, hosts, axis=0)
    from_local = jnp.take(local_rows, local_index, axis=0)
    staying = (hosts == own_index).reshape((-1,) + (1,) * (buffer.ndim - 1))
    return jnp.where(staying, from_local, from_buffer)


def run_sections(inputs, valid_counts, context, conv_state, qkv_weight, out_weight, conv_weight):
    local_count = inputs.shape[0]
    block_total = 1
    block_rows = local_count // block_total
    section_total = lax.axis_size("section")
    section_index = lax.axis_index("section")
    inbound = jnp.zeros((block_rows,) + inputs.shape[1:], jnp.bfloat16)
    result = jnp.zeros_like(inputs)
    turn_total = block_total + section_total - 1
    for turn_index in range(turn_total):
        own_block = turn_index - section_index
        first_row = jnp.clip(own_block, 0, block_total - 1) * block_rows
        layer_input = jnp.where(section_index == 0, inputs, inbound)
        produced = encoder_layer(
            layer_input, valid_counts, context, conv_state, qkv_weight, out_weight, conv_weight
        )
        active = (own_block >= 0) & (own_block < block_total)
        previous = result
        result = jnp.where(active, produced, previous)
        if turn_index + 1 < turn_total:
            inbound = shifted(produced, "section", 1)
    return result


def body(
    new_frames, valid_counts, anchor, context_cache, conv_state, qkv_weight, out_weight, conv_weight
):
    local_count = new_frames.shape[0]
    own_index = lax.axis_index("stream")
    slot_total = lax.axis_size("stream")
    context_here = context_cache[0]
    conv_here = conv_state[0]
    target_host, source_host, mine_new, mine_old = routing(anchor, own_index, local_count)
    old_local = jnp.clip(mine_old - own_index * local_count, 0, local_count - 1)
    outgoing = (
        pack_rows(context_here, target_host, own_index, slot_total),
        pack_rows(conv_here, target_host, own_index, slot_total),
    )
    got_context, got_conv = (
        lax.all_to_all(outgoing[0], "stream", split_axis=0, concat_axis=0, tiled=True),
        lax.all_to_all(outgoing[1], "stream", split_axis=0, concat_axis=0, tiled=True),
    )
    valid_here = lax.dynamic_slice_in_dim(valid_counts, own_index * local_count, local_count)
    context_new = pick_rows(got_context, context_here, source_host, own_index, old_local)
    conv_new = pick_rows(got_conv, conv_here, source_host, own_index, old_local)
    section_output = run_sections(
        new_frames, valid_here, context_new, conv_new, qkv_weight[0], out_weight[0], conv_weight[0]
    )
    return section_output[None]


def solution(mesh):
    return jax.shard_map(
        body,
        mesh=mesh,
        in_specs=(
            P(("groups", "stream"), None, None),
            P("groups"),
            P("groups"),
            P("section", ("groups", "stream"), None, None),
            P("section", ("groups", "stream"), None, None),
            P("section", None, None),
            P("section", None, None),
            P("section", None, None),
        ),
        out_specs=P("section", ("groups", "stream"), None, None),
        check_vma=False,
    )
```

```python
import functools

import jax
import jax.numpy as jnp
from jax import lax
from jax.experimental import pallas as pl
from jax.experimental.pallas import tpu as pltpu
from jax.sharding import PartitionSpec as P

HEADS = 16
GROUP = 8


def shifted(value, axis, steps):
    count = lax.axis_size(axis)
    leading, last = (max(0, -steps), min(count, count - steps))
    return lax.ppermute(value, axis, [(source, source + steps) for source in range(leading, last)])


def layer_kernel(sel_ref, x_ref, klive_ref, rlive_ref, cw_ref, wqkv_hbm, wo_hbm, ctxl_hbm,
                 ctxr_hbm, cstl_hbm, cstr_hbm, out_ref, wbuf, ctxv, cstv, qkv, acc_ref, pad_ref,
                 wsem, gsem, *, streams, frames, ctx, head_size):
    tokens = streams * frames
    width = x_ref.shape[1]
    slot = ctxv.shape[0] // streams
    copies = [
        pltpu.make_async_copy(wqkv_hbm.at[:, pl.ds(i * width, width)], wbuf.at[i], wsem.at[i])
        for i in range(3)
    ]
    copies.append(pltpu.make_async_copy(wo_hbm, wbuf.at[3], wsem.at[3]))
    for c in copies:
        c.start()
    for j in range(streams):
        kind = sel_ref[j]
        idx = sel_ref[streams + j]

        @pl.when(kind == 0)
        def _():
            pltpu.make_async_copy(ctxl_hbm.at[idx], ctxv.at[pl.ds(slot * j, slot)],
                                  gsem.at[0, j]).start()
            pltpu.make_async_copy(cstl_hbm.at[idx], cstv.at[j], gsem.at[1, j]).start()

        @pl.when(kind != 0)
        def _():
            pltpu.make_async_copy(ctxr_hbm.at[idx], ctxv.at[pl.ds(slot * j, slot)],
                                  gsem.at[0, j]).start()
            pltpu.make_async_copy(cstr_hbm.at[idx], cstv.at[j], gsem.at[1, j]).start()

    floats = x_ref[...].astype(jnp.float32)
    centred = floats - jnp.mean(floats, axis=-1, keepdims=True)
    variance = jnp.mean(centred * centred, axis=-1, keepdims=True)
    normed = (centred * lax.rsqrt(variance + 1e-05)).astype(jnp.bfloat16)
    for i in range(3):
        copies[i].wait()
        part = jnp.dot(normed, wbuf[i], preferred_element_type=jnp.float32)
        if i == 0:
            part = part * (head_size ** -0.5)
        qkv[i] = part.astype(jnp.bfloat16)
    for j in range(streams):
        pltpu.make_async_copy(ctxl_hbm.at[0], ctxv.at[pl.ds(slot * j, slot)], gsem.at[0, j]).wait()

    rows_g = GROUP * frames
    cols_g = GROUP * slot
    q_stream = lax.broadcasted_iota(jnp.int32, (rows_g, cols_g), 0) // frames
    c_col = lax.broadcasted_iota(jnp.int32, (rows_g, cols_g), 1)
    bias_c = jnp.where((c_col // slot == q_stream) & (c_col % slot < ctx), 0.0, -1e30)
    k_stream = lax.broadcasted_iota(jnp.int32, (rows_g, rows_g), 1) // frames
    q_stream_n = lax.broadcasted_iota(jnp.int32, (rows_g, rows_g), 0) // frames
    same_n = q_stream_n == k_stream
    pair = 2 * head_size
    lane = lax.broadcasted_iota(jnp.int32, (rows_g, pair), 1)
    nt = (((1,), (1,)), ((), ()))
    for g in range(streams // GROUP):
        rows = pl.ds(g * rows_g, rows_g)
        crow = pl.ds(g * cols_g, cols_g)
        bias_n = jnp.where(same_n & (klive_ref[:, pl.ds(g * rows_g, rows_g)] > 0.0), 0.0, -1e30)
        def head_pair(p, carry):
            cols = pl.ds(pl.multiple_of(p * pair, pair), pair)
            q = qkv[0, rows, cols]
            k = qkv[1, rows, cols]
            v = qkv[2, rows, cols]
            ck = ctxv[crow, cols]
            cv = ctxv[crow, pl.ds(pl.multiple_of(width + p * pair, pair), pair)]
            attended = None
            for half in range(pair // head_size):
                mine = (lane >= half * head_size) & (lane < (half + 1) * head_size)
                qh = jnp.where(mine, q, jnp.zeros_like(q))
                sc = lax.dot_general(qh, ck, nt, preferred_element_type=jnp.float32) + bias_c
                sn = lax.dot_general(qh, k, nt, preferred_element_type=jnp.float32) + bias_n
                top = jnp.maximum(jnp.max(sc, axis=-1, keepdims=True),
                                  jnp.max(sn, axis=-1, keepdims=True))
                ec = jnp.exp(sc - top)
                en = jnp.exp(sn - top)
                total = jnp.sum(ec, axis=-1, keepdims=True) + jnp.sum(en, axis=-1, keepdims=True)
                pc = (ec / total).astype(jnp.bfloat16)
                pn = (en / total).astype(jnp.bfloat16)
                oh = jnp.dot(pc, cv, preferred_element_type=jnp.float32) + jnp.dot(
                    pn, v, preferred_element_type=jnp.float32)
                attended = oh if attended is None else jnp.where(mine, oh, attended)
            qkv[0, rows, cols] = attended.astype(jnp.bfloat16)
            return carry

        lax.fori_loop(0, width // pair, head_pair, 0)

    copies[3].wait()
    mixed = jnp.dot(qkv[0], wbuf[3], preferred_element_type=jnp.float32)
    residual = x_ref[...].astype(jnp.float32) + mixed
    acc_ref[...] = residual
    for j in range(streams):
        pltpu.make_async_copy(cstl_hbm.at[0], cstv.at[j], gsem.at[1, j]).wait()
    kept = cstv.shape[1]
    lead = pad_ref.shape[1] - frames - kept
    rounded = residual.astype(jnp.bfloat16).astype(jnp.float32)
    pad_ref[:, lead:lead + kept, :] = cstv[...].astype(jnp.float32)
    pad_ref[:, lead + kept:, :] = rounded.reshape(streams, frames, width)
    taps = cw_ref.shape[0]
    chunk = 128
    live = rlive_ref[...].reshape(streams, frames, 1)
    def conv_chunk(c, carry):
        cols = pl.ds(pl.multiple_of(c * chunk, chunk), chunk)
        conv = jnp.zeros((streams, frames, chunk), jnp.float32)
        for j in range(taps):
            conv = conv + cw_ref[pl.ds(j, 1), cols].reshape(1, 1, chunk) * pad_ref[
                :, pl.ds(lead + j, frames), cols]
        res = acc_ref[:, cols].reshape(streams, frames, chunk)
        silu = conv / (1.0 + jnp.exp(-conv))
        out = (res + silu) * live
        out_ref[:, cols] = out.reshape(tokens, chunk).astype(out_ref.dtype)
        return carry

    lax.fori_loop(0, width // chunk, conv_chunk, 0)


def encoder_layer(inputs, valid_counts, sel, ctx_local, ctx_recv, cst_local, cst_recv,
                  qkv_weight, out_weight, conv_weight, ctx):
    streams, frames, width = inputs.shape
    kept = cst_local.shape[1]
    head_size = width // HEADS
    tokens = streams * frames
    slot = -(-ctx // 16) * 16
    live = (jnp.arange(frames, dtype=jnp.int32)[None, :] < valid_counts[:, None]).astype(jnp.float32)
    klive = live.reshape(1, tokens)
    rlive = live.reshape(tokens, 1)
    x = inputs.reshape(tokens, width)
    lead = (-(kept + frames)) % 8
    kernel = functools.partial(layer_kernel, streams=streams, frames=frames, ctx=ctx,
                               head_size=head_size)
    vmem = pl.BlockSpec(memory_space=pltpu.VMEM)
    hbm = pl.BlockSpec(memory_space=pl.ANY)
    out = pl.pallas_call(
        kernel,
        out_shape=jax.ShapeDtypeStruct((tokens, width), jnp.bfloat16),
        in_specs=[pl.BlockSpec(memory_space=pltpu.SMEM), vmem, vmem, vmem, vmem,
                  hbm, hbm, hbm, hbm, hbm, hbm],
        out_specs=vmem,
        scratch_shapes=[
            pltpu.VMEM((4, width, width), jnp.bfloat16),
            pltpu.VMEM((streams * slot, 2 * width), jnp.bfloat16),
            pltpu.VMEM((streams, kept, width), jnp.bfloat16),
            pltpu.VMEM((3, tokens, width), jnp.bfloat16),
            pltpu.VMEM((tokens, width), jnp.float32),
            pltpu.VMEM((streams, lead + kept + frames, width), jnp.float32),
            pltpu.SemaphoreType.DMA((4,)),
            pltpu.SemaphoreType.DMA((2, streams)),
        ],
    )(sel, x, klive, rlive, conv_weight, qkv_weight, out_weight, ctx_local, ctx_recv, cst_local,
      cst_recv)
    return out.reshape(streams, frames, width)


def migrate(anchor, own, count, local_count, ctx_local, cst_local):
    total = anchor.shape[0]
    every_slot = jnp.arange(total, dtype=jnp.int32)
    newpos = jnp.sum(jnp.where(anchor[None, :] == every_slot[:, None], every_slot[None, :], 0),
                     axis=1)
    mine_new = lax.dynamic_slice_in_dim(newpos, own * local_count, local_count)
    target = mine_new // local_count
    shifts = jnp.arange(1, count, dtype=jnp.int32)
    dest = (own + shifts) % count
    match = target[None, :] == dest[:, None]
    send_slot = jnp.sum(jnp.where(match, jnp.arange(local_count, dtype=jnp.int32)[None, :], 0),
                        axis=1)
    ctx_recv, cst_recv = [], []
    for k in range(1, count):
        perm = [(i, (i + k) % count) for i in range(count)]
        row = send_slot[k - 1]
        ctx_recv.append(lax.ppermute(ctx_local[row], "stream", perm))
        cst_recv.append(lax.ppermute(cst_local[row], "stream", perm))
    mine_old = lax.dynamic_slice_in_dim(anchor, own * local_count, local_count)
    source = mine_old // local_count
    staying = source == own
    local_idx = jnp.clip(mine_old - own * local_count, 0, local_count - 1)
    recv_idx = jnp.clip((own - source) % count - 1, 0, count - 2)
    sel = jnp.concatenate([jnp.where(staying, 0, 1), jnp.where(staying, local_idx, recv_idx)])
    return sel.astype(jnp.int32), jnp.stack(ctx_recv), jnp.stack(cst_recv)


def body(
    new_frames, valid_counts, anchor, context_cache, conv_state, qkv_weight, out_weight, conv_weight
):
    local_count = new_frames.shape[0]
    own = lax.axis_index("stream")
    count = lax.axis_size("stream")
    ctx = context_cache.shape[2]
    slot = -(-ctx // 16) * 16
    ctx_local = jnp.pad(context_cache[0], ((0, 0), (0, slot - ctx), (0, 0)))
    cst_local = conv_state[0]
    sel, ctx_recv, cst_recv = migrate(anchor, own, count, local_count, ctx_local, cst_local)
    valid_here = lax.dynamic_slice_in_dim(valid_counts, own * local_count, local_count)
    section_index = lax.axis_index("section")
    layer = functools.partial(encoder_layer, valid_counts=valid_here, sel=sel, ctx_local=ctx_local,
                              ctx_recv=ctx_recv, cst_local=cst_local, cst_recv=cst_recv,
                              qkv_weight=qkv_weight[0], out_weight=out_weight[0],
                              conv_weight=conv_weight[0], ctx=ctx)
    first = layer(new_frames)
    inbound = shifted(first, "section", 1)
    second = layer(inbound)
    result = jnp.where(section_index == 0, first, second)
    return result[None]


def solution(mesh):
    return jax.shard_map(
        body,
        mesh=mesh,
        in_specs=(
            P(("groups", "stream"), None, None),
            P("groups"),
            P("groups"),
            P("section", ("groups", "stream"), None, None),
            P("section", ("groups", "stream"), None, None),
            P("section", None, None),
            P("section", None, None),
            P("section", None, None),
        ),
        out_specs=P("section", ("groups", "stream"), None, None),
        check_vma=False,
    )
```

```python
import functools

import jax
import jax.numpy as jnp
from jax import lax
from jax.experimental import pallas as pl
from jax.experimental.pallas import tpu as pltpu
from jax.sharding import PartitionSpec as P

HEADS = 16
GROUP = 16
CHUNK_ROWS = 128


def shifted(value, axis, steps):
    count = lax.axis_size(axis)
    leading, last = (max(0, -steps), min(count, count - steps))
    return lax.ppermute(value, axis, [(source, source + steps) for source in range(leading, last)])


def layer_kernel(sel_ref, x_ref, klive_ref, rlive_ref, cw_ref, wqkv_hbm, wo_hbm, ctxl_hbm,
                 ctxr_hbm, cstl_hbm, cstr_hbm, out_ref, wbuf, wobuf, ctxv, cstv, qkv, conv_ref,
                 pad_ref, res_ref, wsem, gsem, *, streams, frames, ctx, head_size):
    tokens = streams * frames
    width = x_ref.shape[1]
    slot = ctxv.shape[0] // streams
    kept = cstv.shape[1]
    lead = pad_ref.shape[1] - frames - kept
    taps = cw_ref.shape[0]
    chunk = 128

    def gather(j, which):
        kind = sel_ref[j]
        idx = sel_ref[streams + j]
        if which == 0:
            dst, local, remote = cstv.at[j], cstl_hbm, cstr_hbm
        else:
            dst, local, remote = ctxv.at[pl.ds(slot * j, slot)], ctxl_hbm, ctxr_hbm

        @pl.when(kind == 0)
        def _():
            pltpu.make_async_copy(local.at[idx], dst, gsem.at[which, j]).start()

        @pl.when(kind != 0)
        def _():
            pltpu.make_async_copy(remote.at[idx], dst, gsem.at[which, j]).start()

    def gather_wait(j, which):
        if which == 0:
            pltpu.make_async_copy(cstl_hbm.at[0], cstv.at[j], gsem.at[0, j]).wait()
        else:
            pltpu.make_async_copy(ctxl_hbm.at[0], ctxv.at[pl.ds(slot * j, slot)],
                                  gsem.at[1, j]).wait()

    for j in range(streams):
        gather(j, 0)
    for j in range(streams):
        gather(j, 1)
    rows_w = wqkv_hbm.shape[0]
    copies = []
    for r in range(rows_w // CHUNK_ROWS):
        part = pl.ds(r * CHUNK_ROWS, CHUNK_ROWS)
        copies.append(pltpu.make_async_copy(wqkv_hbm.at[part], wbuf.at[part], wsem.at[0, r]))
    for r in range(rows_w // CHUNK_ROWS):
        part = pl.ds(r * CHUNK_ROWS, CHUNK_ROWS)
        copies.append(pltpu.make_async_copy(wo_hbm.at[part], wobuf.at[part], wsem.at[1, r]))
    for c in copies:
        c.start()

    floats = x_ref[...].astype(jnp.float32)
    centred = floats - jnp.mean(floats, axis=-1, keepdims=True)
    variance = jnp.mean(centred * centred, axis=-1, keepdims=True)
    normed = (centred * lax.rsqrt(variance + 1e-05)).astype(jnp.bfloat16)

    for j in range(streams):
        gather_wait(j, 0)
    pad_ref[:, 0:lead, :] = jnp.zeros((streams, lead, width), jnp.float32)
    pad_ref[:, lead:lead + kept, :] = cstv[...].astype(jnp.float32)
    pad_ref[:, lead + kept:, :] = jnp.zeros((streams, frames, width), jnp.float32)

    def conv_taps(first):
        def conv_chunk(c, carry):
            cols = pl.ds(pl.multiple_of(c * chunk, chunk), chunk)
            conv = conv_ref[:, :, cols]
            for j in range(first, taps):
                conv = conv + cw_ref[pl.ds(j, 1), cols].reshape(1, 1, chunk) * pad_ref[
                    :, pl.ds(lead + j, frames), cols]
            conv_ref[:, :, cols] = conv
            return carry

        lax.fori_loop(0, width // chunk, conv_chunk, 0)

    conv_ref[...] = jnp.zeros_like(conv_ref)
    conv_taps(0)

    for c in copies[:rows_w // CHUNK_ROWS]:
        c.wait()
    for i in range(3):
        part = jnp.dot(normed, wbuf[:, pl.ds(i * width, width)], preferred_element_type=jnp.float32)
        if i == 0:
            part = part * (head_size ** -0.5)
        qkv[i] = part.astype(jnp.bfloat16)
    for j in range(streams):
        gather_wait(j, 1)

    rows_g = GROUP * frames
    cols_g = GROUP * slot
    q_stream = lax.broadcasted_iota(jnp.int32, (rows_g, cols_g), 0) // frames
    c_col = lax.broadcasted_iota(jnp.int32, (rows_g, cols_g), 1)
    bias_c = jnp.where((c_col // slot == q_stream) & (c_col % slot < ctx), 0.0, -1e30)
    k_stream = lax.broadcasted_iota(jnp.int32, (rows_g, rows_g), 1) // frames
    q_stream_n = lax.broadcasted_iota(jnp.int32, (rows_g, rows_g), 0) // frames
    same_n = q_stream_n == k_stream
    pair = 2 * head_size
    lane = lax.broadcasted_iota(jnp.int32, (rows_g, pair), 1)
    nt = (((1,), (1,)), ((), ()))
    for g in range(streams // GROUP):
        rows = pl.ds(g * rows_g, rows_g)
        crow = pl.ds(g * cols_g, cols_g)
        bias_n = jnp.where(same_n & (klive_ref[:, pl.ds(g * rows_g, rows_g)] > 0.0), 0.0, -1e30)

        def head_pair(p, carry):
            cols = pl.ds(pl.multiple_of(p * pair, pair), pair)
            q = qkv[0, rows, cols]
            k = qkv[1, rows, cols]
            v = qkv[2, rows, cols]
            ck = ctxv[crow, cols]
            cv = ctxv[crow, pl.ds(pl.multiple_of(width + p * pair, pair), pair)]
            attended = None
            for half in range(pair // head_size):
                mine = (lane >= half * head_size) & (lane < (half + 1) * head_size)
                qh = jnp.where(mine, q, jnp.zeros_like(q))
                sc = lax.dot_general(qh, ck, nt, preferred_element_type=jnp.float32) + bias_c
                sn = lax.dot_general(qh, k, nt, preferred_element_type=jnp.float32) + bias_n
                top = jnp.maximum(jnp.max(sc, axis=-1, keepdims=True),
                                  jnp.max(sn, axis=-1, keepdims=True))
                ec = jnp.exp(sc - top)
                en = jnp.exp(sn - top)
                total = jnp.sum(ec, axis=-1, keepdims=True) + jnp.sum(en, axis=-1, keepdims=True)
                pc = (ec / total).astype(jnp.bfloat16)
                pn = (en / total).astype(jnp.bfloat16)
                oh = jnp.dot(pc, cv, preferred_element_type=jnp.float32) + jnp.dot(
                    pn, v, preferred_element_type=jnp.float32)
                attended = oh if attended is None else jnp.where(mine, oh, attended)
            qkv[0, rows, cols] = attended.astype(jnp.bfloat16)
            return carry

        lax.fori_loop(0, width // pair, head_pair, 0)

    for c in copies[rows_w // CHUNK_ROWS:]:
        c.wait()
    mixed = jnp.dot(qkv[0], wobuf[...], preferred_element_type=jnp.float32)
    residual = x_ref[...].astype(jnp.float32) + mixed
    res_ref[...] = residual
    pad_ref[:, lead:lead + kept, :] = jnp.zeros((streams, kept, width), jnp.float32)
    pad_ref[:, lead + kept:, :] = residual.astype(jnp.bfloat16).astype(jnp.float32).reshape(
        streams, frames, width)
    first = taps - frames
    conv_taps(first)
    live = rlive_ref[...].reshape(streams, frames, 1)

    def finish(c, carry):
        cols = pl.ds(pl.multiple_of(c * chunk, chunk), chunk)
        conv = conv_ref[:, :, cols]
        res = res_ref[:, cols]
        silu = conv / (1.0 + jnp.exp(-conv))
        out = (res.reshape(streams, frames, chunk) + silu) * live
        out_ref[:, cols] = out.reshape(tokens, chunk).astype(out_ref.dtype)
        return carry

    lax.fori_loop(0, width // chunk, finish, 0)


def encoder_layer(inputs, valid_counts, sel, ctx_local, ctx_recv, cst_local, cst_recv,
                  qkv_weight, out_weight, conv_weight, ctx):
    streams, frames, width = inputs.shape
    kept = cst_local.shape[1]
    head_size = width // HEADS
    tokens = streams * frames
    slot = -(-ctx // 16) * 16
    live = (jnp.arange(frames, dtype=jnp.int32)[None, :] < valid_counts[:, None]).astype(jnp.float32)
    klive = live.reshape(1, tokens)
    rlive = live.reshape(tokens, 1)
    x = inputs.reshape(tokens, width)
    lead = (-(kept + frames)) % 8
    kernel = functools.partial(layer_kernel, streams=streams, frames=frames, ctx=ctx,
                               head_size=head_size)
    vmem = pl.BlockSpec(memory_space=pltpu.VMEM)
    hbm = pl.BlockSpec(memory_space=pl.ANY)
    out = pl.pallas_call(
        kernel,
        out_shape=jax.ShapeDtypeStruct((tokens, width), jnp.bfloat16),
        in_specs=[pl.BlockSpec(memory_space=pltpu.SMEM), vmem, vmem, vmem, vmem,
                  hbm, hbm, hbm, hbm, hbm, hbm],
        out_specs=vmem,
        scratch_shapes=[
            pltpu.VMEM((width, 3 * width), jnp.bfloat16),
            pltpu.VMEM((width, width), jnp.bfloat16),
            pltpu.VMEM((streams * slot, 2 * width), jnp.bfloat16),
            pltpu.VMEM((streams, kept, width), jnp.bfloat16),
            pltpu.VMEM((3, tokens, width), jnp.bfloat16),
            pltpu.VMEM((streams, frames, width), jnp.float32),
            pltpu.VMEM((streams, lead + kept + frames, width), jnp.float32),
            pltpu.VMEM((tokens, width), jnp.float32),
            pltpu.SemaphoreType.DMA((2, width // CHUNK_ROWS)),
            pltpu.SemaphoreType.DMA((2, streams)),
        ],
    )(sel, x, klive, rlive, conv_weight, qkv_weight, out_weight, ctx_local, ctx_recv, cst_local,
      cst_recv)
    return out.reshape(streams, frames, width)


def migrate(anchor, own, count, local_count, ctx_local, cst_local):
    total = anchor.shape[0]
    every_slot = jnp.arange(total, dtype=jnp.int32)
    newpos = jnp.sum(jnp.where(anchor[None, :] == every_slot[:, None], every_slot[None, :], 0),
                     axis=1)
    mine_new = lax.dynamic_slice_in_dim(newpos, own * local_count, local_count)
    target = mine_new // local_count
    hosts = jnp.arange(count, dtype=jnp.int32)
    match = target[None, :] == hosts[:, None]
    send_slot = jnp.sum(jnp.where(match, jnp.arange(local_count, dtype=jnp.int32)[None, :], 0),
                        axis=1)
    ctx_recv = lax.all_to_all(jnp.take(ctx_local, send_slot, axis=0), "stream", 0, 0, tiled=True)
    cst_recv = lax.all_to_all(jnp.take(cst_local, send_slot, axis=0), "stream", 0, 0, tiled=True)
    mine_old = lax.dynamic_slice_in_dim(anchor, own * local_count, local_count)
    source = mine_old // local_count
    staying = source == own
    local_idx = jnp.clip(mine_old - own * local_count, 0, local_count - 1)
    recv_idx = jnp.clip(source, 0, count - 1)
    sel = jnp.concatenate([jnp.where(staying, 0, 1), jnp.where(staying, local_idx, recv_idx)])
    return sel.astype(jnp.int32), ctx_recv, cst_recv


def body(
    new_frames, valid_counts, anchor, context_cache, conv_state, qkv_weight, out_weight, conv_weight
):
    local_count = new_frames.shape[0]
    own = lax.axis_index("stream")
    count = lax.axis_size("stream")
    ctx = context_cache.shape[2]
    slot = -(-ctx // 16) * 16
    ctx_local = jnp.pad(context_cache[0], ((0, 0), (0, slot - ctx), (0, 0)))
    cst_local = conv_state[0]
    sel, ctx_recv, cst_recv = migrate(anchor, own, count, local_count, ctx_local, cst_local)
    valid_here = lax.dynamic_slice_in_dim(valid_counts, own * local_count, local_count)
    section_index = lax.axis_index("section")
    layer = functools.partial(encoder_layer, valid_counts=valid_here, sel=sel, ctx_local=ctx_local,
                              ctx_recv=ctx_recv, cst_local=cst_local, cst_recv=cst_recv,
                              qkv_weight=qkv_weight[0], out_weight=out_weight[0],
                              conv_weight=conv_weight[0], ctx=ctx)
    first = layer(new_frames)
    inbound = shifted(first, "section", 1)
    second = layer(inbound)
    result = jnp.where(section_index == 0, first, second)
    return result[None]


def solution(mesh):
    return jax.shard_map(
        body,
        mesh=mesh,
        in_specs=(
            P(("groups", "stream"), None, None),
            P("groups"),
            P("groups"),
            P("section", ("groups", "stream"), None, None),
            P("section", ("groups", "stream"), None, None),
            P("section", None, None),
            P("section", None, None),
            P("section", None, None),
        ),
        out_specs=P("section", ("groups", "stream"), None, None),
        check_vma=False,
    )
```

```python
import functools

import jax
import jax.numpy as jnp
from jax import lax
from jax.experimental import pallas as pl
from jax.experimental.pallas import tpu as pltpu
from jax.sharding import PartitionSpec as P

HEADS = 16
GROUP = 16
CHUNK_ROWS = 128


def shifted(value, axis, steps):
    count = lax.axis_size(axis)
    leading, last = (max(0, -steps), min(count, count - steps))
    return lax.ppermute(value, axis, [(source, source + steps) for source in range(leading, last)])


def layer_kernel(sel_ref, x_ref, klive_ref, rlive_ref, cw_ref, wqkv_hbm, wo_hbm, state_hbm,
                 recv_hbm, out_ref, wbuf, wobuf, stv, qkv, conv_ref, pad_ref, res_ref, wsem, gsem,
                 *, streams, frames, ctx, head_size):
    tokens = streams * frames
    width = x_ref.shape[1]
    slot = -(-ctx // 16) * 16
    kept = pad_ref.shape[1] - frames
    taps = cw_ref.shape[0]
    chunk = 128

    for j in range(streams):
        kind = sel_ref[j]
        idx = sel_ref[streams + j]

        @pl.when(kind == 0)
        def _():
            pltpu.make_async_copy(state_hbm.at[idx], stv.at[j], gsem.at[j]).start()

        @pl.when(kind != 0)
        def _():
            pltpu.make_async_copy(recv_hbm.at[idx], stv.at[j], gsem.at[j]).start()

    rows_w = wqkv_hbm.shape[0]
    copies = []
    for r in range(rows_w // CHUNK_ROWS):
        part = pl.ds(r * CHUNK_ROWS, CHUNK_ROWS)
        copies.append(pltpu.make_async_copy(wqkv_hbm.at[part], wbuf.at[part], wsem.at[0, r]))
    for r in range(rows_w // CHUNK_ROWS):
        part = pl.ds(r * CHUNK_ROWS, CHUNK_ROWS)
        copies.append(pltpu.make_async_copy(wo_hbm.at[part], wobuf.at[part], wsem.at[1, r]))
    for c in copies:
        c.start()

    floats = x_ref[...].astype(jnp.float32)
    centred = floats - jnp.mean(floats, axis=-1, keepdims=True)
    variance = jnp.mean(centred * centred, axis=-1, keepdims=True)
    normed = (centred * lax.rsqrt(variance + 1e-05)).astype(jnp.bfloat16)

    for j in range(streams):
        pltpu.make_async_copy(state_hbm.at[0], stv.at[j], gsem.at[j]).wait()
    pad_ref[:, 0:kept, :] = stv[:, pl.ds(2 * slot, kept), :].astype(jnp.float32)
    pad_ref[:, kept:, :] = jnp.zeros((streams, frames, width), jnp.float32)

    def conv_taps(first):
        def conv_chunk(c, carry):
            cols = pl.ds(pl.multiple_of(c * chunk, chunk), chunk)
            conv = conv_ref[:, :, cols]
            for j in range(first, taps):
                conv = conv + cw_ref[pl.ds(j, 1), cols].reshape(1, 1, chunk) * pad_ref[
                    :, pl.ds(kept - taps + 1 + j, frames), cols]
            conv_ref[:, :, cols] = conv
            return carry

        lax.fori_loop(0, width // chunk, conv_chunk, 0)

    conv_ref[...] = jnp.zeros_like(conv_ref)
    conv_taps(0)

    for c in copies[:rows_w // CHUNK_ROWS]:
        c.wait()
    for i in range(3):
        part = jnp.dot(normed, wbuf[:, pl.ds(i * width, width)], preferred_element_type=jnp.float32)
        if i == 0:
            part = part * (head_size ** -0.5)
        qkv[i] = part.astype(jnp.bfloat16)

    rows_g = GROUP * frames
    cols_g = GROUP * slot
    q_stream = lax.broadcasted_iota(jnp.int32, (rows_g, cols_g), 0) // frames
    c_col = lax.broadcasted_iota(jnp.int32, (rows_g, cols_g), 1)
    bias_c = jnp.where((c_col // slot == q_stream) & (c_col % slot < ctx), 0.0, -1e30)
    k_stream = lax.broadcasted_iota(jnp.int32, (rows_g, rows_g), 1) // frames
    q_stream_n = lax.broadcasted_iota(jnp.int32, (rows_g, rows_g), 0) // frames
    same_n = q_stream_n == k_stream
    pair = 2 * head_size
    lane = lax.broadcasted_iota(jnp.int32, (rows_g, pair), 1)
    nt = (((1,), (1,)), ((), ()))
    for g in range(streams // GROUP):
        rows = pl.ds(g * rows_g, rows_g)
        srow = pl.ds(g * GROUP, GROUP)
        bias_n = jnp.where(same_n & (klive_ref[:, pl.ds(g * rows_g, rows_g)] > 0.0), 0.0, -1e30)

        def head_pair(p, carry):
            cols = pl.ds(pl.multiple_of(p * pair, pair), pair)
            q = qkv[0, rows, cols]
            k = qkv[1, rows, cols]
            v = qkv[2, rows, cols]
            ck = stv[srow, pl.ds(0, slot), cols].reshape(cols_g, pair)
            cv = stv[srow, pl.ds(slot, slot), cols].reshape(cols_g, pair)
            attended = None
            for half in range(pair // head_size):
                mine = (lane >= half * head_size) & (lane < (half + 1) * head_size)
                qh = jnp.where(mine, q, jnp.zeros_like(q))
                sc = lax.dot_general(qh, ck, nt, preferred_element_type=jnp.float32) + bias_c
                sn = lax.dot_general(qh, k, nt, preferred_element_type=jnp.float32) + bias_n
                top = jnp.maximum(jnp.max(sc, axis=-1, keepdims=True),
                                  jnp.max(sn, axis=-1, keepdims=True))
                ec = jnp.exp(sc - top)
                en = jnp.exp(sn - top)
                total = jnp.sum(ec, axis=-1, keepdims=True) + jnp.sum(en, axis=-1, keepdims=True)
                pc = (ec / total).astype(jnp.bfloat16)
                pn = (en / total).astype(jnp.bfloat16)
                oh = jnp.dot(pc, cv, preferred_element_type=jnp.float32) + jnp.dot(
                    pn, v, preferred_element_type=jnp.float32)
                attended = oh if attended is None else jnp.where(mine, oh, attended)
            qkv[0, rows, cols] = attended.astype(jnp.bfloat16)
            return carry

        lax.fori_loop(0, width // pair, head_pair, 0)

    for c in copies[rows_w // CHUNK_ROWS:]:
        c.wait()
    mixed = jnp.dot(qkv[0], wobuf[...], preferred_element_type=jnp.float32)
    residual = x_ref[...].astype(jnp.float32) + mixed
    res_ref[...] = residual
    pad_ref[:, 0:kept, :] = jnp.zeros((streams, kept, width), jnp.float32)
    pad_ref[:, kept:, :] = residual.astype(jnp.bfloat16).astype(jnp.float32).reshape(
        streams, frames, width)
    first = taps - frames
    conv_taps(first)
    live = rlive_ref[...].reshape(streams, frames, 1)

    def finish(c, carry):
        cols = pl.ds(pl.multiple_of(c * chunk, chunk), chunk)
        conv = conv_ref[:, :, cols]
        res = res_ref[:, cols]
        silu = conv / (1.0 + jnp.exp(-conv))
        out = (res.reshape(streams, frames, chunk) + silu) * live
        out_ref[:, cols] = out.reshape(tokens, chunk).astype(out_ref.dtype)
        return carry

    lax.fori_loop(0, width // chunk, finish, 0)


def encoder_layer(inputs, valid_counts, sel, state, recv, qkv_weight, out_weight, conv_weight,
                  ctx):
    streams, frames, width = inputs.shape
    taps = conv_weight.shape[0]
    head_size = width // HEADS
    tokens = streams * frames
    slot = -(-ctx // 16) * 16
    live = (jnp.arange(frames, dtype=jnp.int32)[None, :] < valid_counts[:, None]).astype(jnp.float32)
    klive = live.reshape(1, tokens)
    rlive = live.reshape(tokens, 1)
    x = inputs.reshape(tokens, width)
    kept = state.shape[1] - 2 * slot
    kernel = functools.partial(layer_kernel, streams=streams, frames=frames, ctx=ctx,
                               head_size=head_size)
    vmem = pl.BlockSpec(memory_space=pltpu.VMEM)
    hbm = pl.BlockSpec(memory_space=pl.ANY)
    out = pl.pallas_call(
        kernel,
        out_shape=jax.ShapeDtypeStruct((tokens, width), jnp.bfloat16),
        in_specs=[pl.BlockSpec(memory_space=pltpu.SMEM), vmem, vmem, vmem, vmem,
                  hbm, hbm, hbm, hbm],
        out_specs=vmem,
        scratch_shapes=[
            pltpu.VMEM((width, 3 * width), jnp.bfloat16),
            pltpu.VMEM((width, width), jnp.bfloat16),
            pltpu.VMEM((streams,) + state.shape[1:], jnp.bfloat16),
            pltpu.VMEM((3, tokens, width), jnp.bfloat16),
            pltpu.VMEM((streams, frames, width), jnp.float32),
            pltpu.VMEM((streams, kept + frames, width), jnp.float32),
            pltpu.VMEM((tokens, width), jnp.float32),
            pltpu.SemaphoreType.DMA((2, width // CHUNK_ROWS)),
            pltpu.SemaphoreType.DMA((streams,)),
        ],
    )(sel, x, klive, rlive, conv_weight, qkv_weight, out_weight, state, recv)
    return out.reshape(streams, frames, width)


def migrate(anchor, own, count, local_count, state):
    total = anchor.shape[0]
    every_slot = jnp.arange(total, dtype=jnp.int32)
    newpos = jnp.sum(jnp.where(anchor[None, :] == every_slot[:, None], every_slot[None, :], 0),
                     axis=1)
    mine_new = lax.dynamic_slice_in_dim(newpos, own * local_count, local_count)
    target = mine_new // local_count
    hosts = jnp.arange(count, dtype=jnp.int32)
    match = target[None, :] == hosts[:, None]
    send_slot = jnp.sum(jnp.where(match, jnp.arange(local_count, dtype=jnp.int32)[None, :], 0),
                        axis=1)
    recv = lax.all_to_all(jnp.take(state, send_slot, axis=0), "stream", 0, 0, tiled=True)
    mine_old = lax.dynamic_slice_in_dim(anchor, own * local_count, local_count)
    source = mine_old // local_count
    staying = source == own
    local_idx = jnp.clip(mine_old - own * local_count, 0, local_count - 1)
    recv_idx = jnp.clip(source, 0, count - 1)
    sel = jnp.concatenate([jnp.where(staying, 0, 1), jnp.where(staying, local_idx, recv_idx)])
    return sel.astype(jnp.int32), recv


def body(
    new_frames, valid_counts, anchor, context_cache, conv_state, qkv_weight, out_weight, conv_weight
):
    local_count = new_frames.shape[0]
    own = lax.axis_index("stream")
    count = lax.axis_size("stream")
    ctx = context_cache.shape[2]
    width = conv_state.shape[3]
    slot = -(-ctx // 16) * 16
    kept = conv_state.shape[2]
    lead = (-kept) % 16
    context = context_cache[0]
    state = jnp.concatenate([
        jnp.pad(context[:, :, :width], ((0, 0), (0, slot - ctx), (0, 0))),
        jnp.pad(context[:, :, width:], ((0, 0), (0, slot - ctx), (0, 0))),
        jnp.pad(conv_state[0], ((0, 0), (lead, 0), (0, 0))),
    ], axis=1)
    sel, recv = migrate(anchor, own, count, local_count, state)
    valid_here = lax.dynamic_slice_in_dim(valid_counts, own * local_count, local_count)
    section_index = lax.axis_index("section")
    layer = functools.partial(encoder_layer, valid_counts=valid_here, sel=sel, state=state,
                              recv=recv, qkv_weight=qkv_weight[0], out_weight=out_weight[0],
                              conv_weight=conv_weight[0], ctx=ctx)
    first = layer(new_frames)
    inbound = shifted(first, "section", 1)
    second = layer(inbound)
    result = jnp.where(section_index == 0, first, second)
    return result[None]


def solution(mesh):
    return jax.shard_map(
        body,
        mesh=mesh,
        in_specs=(
            P(("groups", "stream"), None, None),
            P("groups"),
            P("groups"),
            P("section", ("groups", "stream"), None, None),
            P("section", ("groups", "stream"), None, None),
            P("section", None, None),
            P("section", None, None),
            P("section", None, None),
        ),
        out_specs=P("section", ("groups", "stream"), None, None),
        check_vma=False,
    )
```

```python
import functools

import jax
import jax.numpy as jnp
from jax import lax
from jax.experimental import pallas as pl
from jax.experimental.pallas import tpu as pltpu
from jax.sharding import PartitionSpec as P

HEADS = 16
GROUP = 16
CHUNK_ROWS = 128


def shifted(value, axis, steps):
    count = lax.axis_size(axis)
    leading, last = (max(0, -steps), min(count, count - steps))
    return lax.ppermute(value, axis, [(source, source + steps) for source in range(leading, last)])


def projection_kernel(x_ref, w_ref, out_ref, nrm_ref, *, head_size):
    step = pl.program_id(0)

    @pl.when(step == 0)
    def _():
        floats = x_ref[...].astype(jnp.float32)
        centred = floats - jnp.mean(floats, axis=-1, keepdims=True)
        variance = jnp.mean(centred * centred, axis=-1, keepdims=True)
        nrm_ref[...] = (centred * lax.rsqrt(variance + 1e-05)).astype(jnp.bfloat16)

    part = jnp.dot(nrm_ref[...], w_ref[...], preferred_element_type=jnp.float32)
    scale = jnp.where(step == 0, head_size ** -0.5, 1.0).astype(jnp.float32)
    out_ref[0] = (part * scale).astype(out_ref.dtype)


def layer_kernel(sel_ref, x_ref, klive_ref, rlive_ref, cw_ref, qkv_hbm, wo_hbm, state_hbm,
                 recv_hbm, out_ref, wobuf, stv, qkv, conv_ref, pad_ref, res_ref, wsem, gsem,
                 *, streams, frames, ctx, head_size):
    tokens = streams * frames
    width = x_ref.shape[1]
    slot = -(-ctx // 16) * 16
    kept = pad_ref.shape[1] - frames
    taps = cw_ref.shape[0]
    chunk = 128

    for j in range(streams):
        kind = sel_ref[j]
        idx = sel_ref[streams + j]

        @pl.when(kind == 0)
        def _():
            pltpu.make_async_copy(state_hbm.at[idx], stv.at[j], gsem.at[j]).start()

        @pl.when(kind != 0)
        def _():
            pltpu.make_async_copy(recv_hbm.at[idx], stv.at[j], gsem.at[j]).start()

    rows_w = wo_hbm.shape[0]
    copies = [pltpu.make_async_copy(qkv_hbm, qkv, wsem.at[0, 0])]
    for r in range(rows_w // CHUNK_ROWS):
        part = pl.ds(r * CHUNK_ROWS, CHUNK_ROWS)
        copies.append(pltpu.make_async_copy(wo_hbm.at[part], wobuf.at[part], wsem.at[1, r]))
    for c in copies:
        c.start()

    for j in range(streams):
        pltpu.make_async_copy(state_hbm.at[0], stv.at[j], gsem.at[j]).wait()
    pad_ref[:, 0:kept, :] = stv[:, pl.ds(2 * slot, kept), :].astype(jnp.float32)
    pad_ref[:, kept:, :] = jnp.zeros((streams, frames, width), jnp.float32)

    def conv_taps(first):
        def conv_chunk(c, carry):
            cols = pl.ds(pl.multiple_of(c * chunk, chunk), chunk)
            conv = conv_ref[:, :, cols]
            for j in range(first, taps):
                conv = conv + cw_ref[pl.ds(j, 1), cols].reshape(1, 1, chunk) * pad_ref[
                    :, pl.ds(kept - taps + 1 + j, frames), cols]
            conv_ref[:, :, cols] = conv
            return carry

        lax.fori_loop(0, width // chunk, conv_chunk, 0)

    conv_ref[...] = jnp.zeros_like(conv_ref)
    conv_taps(0)

    copies[0].wait()

    rows_g = GROUP * frames
    cols_g = GROUP * slot
    q_stream = lax.broadcasted_iota(jnp.int32, (rows_g, cols_g), 0) // frames
    c_col = lax.broadcasted_iota(jnp.int32, (rows_g, cols_g), 1)
    bias_c = jnp.where((c_col // slot == q_stream) & (c_col % slot < ctx), 0.0, -1e30)
    k_stream = lax.broadcasted_iota(jnp.int32, (rows_g, rows_g), 1) // frames
    q_stream_n = lax.broadcasted_iota(jnp.int32, (rows_g, rows_g), 0) // frames
    same_n = q_stream_n == k_stream
    pair = 2 * head_size
    lane = lax.broadcasted_iota(jnp.int32, (rows_g, pair), 1)
    nt = (((1,), (1,)), ((), ()))
    for g in range(streams // GROUP):
        rows = pl.ds(g * rows_g, rows_g)
        srow = pl.ds(g * GROUP, GROUP)
        bias_n = jnp.where(same_n & (klive_ref[:, pl.ds(g * rows_g, rows_g)] > 0.0), 0.0, -1e30)

        def head_pair(p, carry):
            cols = pl.ds(pl.multiple_of(p * pair, pair), pair)
            q = qkv[0, rows, cols]
            k = qkv[1, rows, cols]
            v = qkv[2, rows, cols]
            ck = stv[srow, pl.ds(0, slot), cols].reshape(cols_g, pair)
            cv = stv[srow, pl.ds(slot, slot), cols].reshape(cols_g, pair)
            attended = None
            for half in range(pair // head_size):
                mine = (lane >= half * head_size) & (lane < (half + 1) * head_size)
                qh = jnp.where(mine, q, jnp.zeros_like(q))
                sc = lax.dot_general(qh, ck, nt, preferred_element_type=jnp.float32) + bias_c
                sn = lax.dot_general(qh, k, nt, preferred_element_type=jnp.float32) + bias_n
                top = jnp.maximum(jnp.max(sc, axis=-1, keepdims=True),
                                  jnp.max(sn, axis=-1, keepdims=True))
                ec = jnp.exp(sc - top)
                en = jnp.exp(sn - top)
                total = jnp.sum(ec, axis=-1, keepdims=True) + jnp.sum(en, axis=-1, keepdims=True)
                pc = (ec / total).astype(jnp.bfloat16)
                pn = (en / total).astype(jnp.bfloat16)
                oh = jnp.dot(pc, cv, preferred_element_type=jnp.float32) + jnp.dot(
                    pn, v, preferred_element_type=jnp.float32)
                attended = oh if attended is None else jnp.where(mine, oh, attended)
            qkv[0, rows, cols] = attended.astype(jnp.bfloat16)
            return carry

        lax.fori_loop(0, width // pair, head_pair, 0)

    for c in copies[1:]:
        c.wait()
    mixed = jnp.dot(qkv[0], wobuf[...], preferred_element_type=jnp.float32)
    residual = x_ref[...].astype(jnp.float32) + mixed
    res_ref[...] = residual
    pad_ref[:, 0:kept, :] = jnp.zeros((streams, kept, width), jnp.float32)
    pad_ref[:, kept:, :] = residual.astype(jnp.bfloat16).astype(jnp.float32).reshape(
        streams, frames, width)
    first = taps - frames
    conv_taps(first)
    live = rlive_ref[...].reshape(streams, frames, 1)

    def finish(c, carry):
        cols = pl.ds(pl.multiple_of(c * chunk, chunk), chunk)
        conv = conv_ref[:, :, cols]
        res = res_ref[:, cols]
        silu = conv / (1.0 + jnp.exp(-conv))
        out = (res.reshape(streams, frames, chunk) + silu) * live
        out_ref[:, cols] = out.reshape(tokens, chunk).astype(out_ref.dtype)
        return carry

    lax.fori_loop(0, width // chunk, finish, 0)


def project(inputs, qkv_weight):
    streams, frames, width = inputs.shape
    tokens = streams * frames
    x = inputs.reshape(tokens, width)
    kernel = functools.partial(projection_kernel, head_size=width // HEADS)
    return pl.pallas_call(
        kernel,
        out_shape=jax.ShapeDtypeStruct((3, tokens, width), jnp.bfloat16),
        grid=(3,),
        in_specs=[pl.BlockSpec((tokens, width), lambda i: (0, 0)),
                  pl.BlockSpec((width, width), lambda i: (0, i))],
        out_specs=pl.BlockSpec((1, tokens, width), lambda i: (i, 0, 0)),
        scratch_shapes=[pltpu.VMEM((tokens, width), jnp.bfloat16)],
        compiler_params=pltpu.CompilerParams(dimension_semantics=("arbitrary",)),
    )(x, qkv_weight)


def encoder_layer(inputs, valid_counts, sel, state, recv, qkv_weight, out_weight, conv_weight,
                  ctx):
    streams, frames, width = inputs.shape
    taps = conv_weight.shape[0]
    head_size = width // HEADS
    tokens = streams * frames
    slot = -(-ctx // 16) * 16
    live = (jnp.arange(frames, dtype=jnp.int32)[None, :] < valid_counts[:, None]).astype(jnp.float32)
    klive = live.reshape(1, tokens)
    rlive = live.reshape(tokens, 1)
    x = inputs.reshape(tokens, width)
    kept = state.shape[1] - 2 * slot
    kernel = functools.partial(layer_kernel, streams=streams, frames=frames, ctx=ctx,
                               head_size=head_size)
    vmem = pl.BlockSpec(memory_space=pltpu.VMEM)
    hbm = pl.BlockSpec(memory_space=pl.ANY)
    out = pl.pallas_call(
        kernel,
        out_shape=jax.ShapeDtypeStruct((tokens, width), jnp.bfloat16),
        in_specs=[pl.BlockSpec(memory_space=pltpu.SMEM), vmem, vmem, vmem, vmem,
                  hbm, hbm, hbm, hbm],
        out_specs=vmem,
        scratch_shapes=[
            pltpu.VMEM((width, width), jnp.bfloat16),
            pltpu.VMEM((streams,) + state.shape[1:], jnp.bfloat16),
            pltpu.VMEM((3, tokens, width), jnp.bfloat16),
            pltpu.VMEM((streams, frames, width), jnp.float32),
            pltpu.VMEM((streams, kept + frames, width), jnp.float32),
            pltpu.VMEM((tokens, width), jnp.float32),
            pltpu.SemaphoreType.DMA((2, width // CHUNK_ROWS)),
            pltpu.SemaphoreType.DMA((streams,)),
        ],
    )(sel, x, klive, rlive, conv_weight, project(inputs, qkv_weight), out_weight, state, recv)
    return out.reshape(streams, frames, width)


def migrate(anchor, own, count, local_count, state):
    total = anchor.shape[0]
    every_slot = jnp.arange(total, dtype=jnp.int32)
    newpos = jnp.sum(jnp.where(anchor[None, :] == every_slot[:, None], every_slot[None, :], 0),
                     axis=1)
    mine_new = lax.dynamic_slice_in_dim(newpos, own * local_count, local_count)
    target = mine_new // local_count
    hosts = jnp.arange(count, dtype=jnp.int32)
    match = target[None, :] == hosts[:, None]
    send_slot = jnp.sum(jnp.where(match, jnp.arange(local_count, dtype=jnp.int32)[None, :], 0),
                        axis=1)
    recv = lax.all_to_all(jnp.take(state, send_slot, axis=0), "stream", 0, 0, tiled=True)
    mine_old = lax.dynamic_slice_in_dim(anchor, own * local_count, local_count)
    source = mine_old // local_count
    staying = source == own
    local_idx = jnp.clip(mine_old - own * local_count, 0, local_count - 1)
    recv_idx = jnp.clip(source, 0, count - 1)
    sel = jnp.concatenate([jnp.where(staying, 0, 1), jnp.where(staying, local_idx, recv_idx)])
    return sel.astype(jnp.int32), recv


def body(
    new_frames, valid_counts, anchor, context_cache, conv_state, qkv_weight, out_weight, conv_weight
):
    local_count = new_frames.shape[0]
    own = lax.axis_index("stream")
    count = lax.axis_size("stream")
    ctx = context_cache.shape[2]
    width = conv_state.shape[3]
    slot = -(-ctx // 16) * 16
    kept = conv_state.shape[2]
    lead = (-kept) % 16
    context = context_cache[0]
    state = jnp.concatenate([
        jnp.pad(context[:, :, :width], ((0, 0), (0, slot - ctx), (0, 0))),
        jnp.pad(context[:, :, width:], ((0, 0), (0, slot - ctx), (0, 0))),
        jnp.pad(conv_state[0], ((0, 0), (lead, 0), (0, 0))),
    ], axis=1)
    sel, recv = migrate(anchor, own, count, local_count, state)
    valid_here = lax.dynamic_slice_in_dim(valid_counts, own * local_count, local_count)
    section_index = lax.axis_index("section")
    layer = functools.partial(encoder_layer, valid_counts=valid_here, sel=sel, state=state,
                              recv=recv, qkv_weight=qkv_weight[0], out_weight=out_weight[0],
                              conv_weight=conv_weight[0], ctx=ctx)
    first = layer(new_frames)
    inbound = shifted(first, "section", 1)
    second = layer(inbound)
    result = jnp.where(section_index == 0, first, second)
    return result[None]


def solution(mesh):
    return jax.shard_map(
        body,
        mesh=mesh,
        in_specs=(
            P(("groups", "stream"), None, None),
            P("groups"),
            P("groups"),
            P("section", ("groups", "stream"), None, None),
            P("section", ("groups", "stream"), None, None),
            P("section", None, None),
            P("section", None, None),
            P("section", None, None),
        ),
        out_specs=P("section", ("groups", "stream"), None, None),
        check_vma=False,
    )
```

```python
import functools

import jax
import jax.numpy as jnp
from jax import lax
from jax.experimental import pallas as pl
from jax.experimental.pallas import tpu as pltpu
from jax.sharding import PartitionSpec as P

HEADS = 16
GROUP = 16
CHUNK_ROWS = 128


def shifted(value, axis, steps):
    count = lax.axis_size(axis)
    leading, last = (max(0, -steps), min(count, count - steps))
    return lax.ppermute(value, axis, [(source, source + steps) for source in range(leading, last)])


def projection_kernel(x_ref, w_ref, out_ref, nrm_ref, *, head_size):
    step = pl.program_id(0)

    @pl.when(step == 0)
    def _():
        floats = x_ref[...].astype(jnp.float32)
        centred = floats - jnp.mean(floats, axis=-1, keepdims=True)
        variance = jnp.mean(centred * centred, axis=-1, keepdims=True)
        nrm_ref[...] = (centred * lax.rsqrt(variance + 1e-05)).astype(jnp.bfloat16)

    part = jnp.dot(nrm_ref[...], w_ref[...], preferred_element_type=jnp.float32)
    scale = jnp.where(step == 0, head_size ** -0.5, 1.0).astype(jnp.float32)
    out_ref[0] = (part * scale).astype(out_ref.dtype)


def conv_rows(conv_ref, pad_ref, cw_ref, tap_rows, frames, origin):
    width = cw_ref.shape[1]
    chunk = 128

    def conv_chunk(c, carry):
        cols = pl.ds(pl.multiple_of(c * chunk, chunk), chunk)
        for lo in range(0, frames, 8):
            conv = conv_ref[:, pl.ds(lo, 8), cols]
            for j, rows in enumerate(tap_rows):
                if lo in rows:
                    conv = conv + cw_ref[pl.ds(j, 1), cols].reshape(1, 1, chunk) * pad_ref[
                        :, pl.ds(origin + j + lo, 8), cols]
            conv_ref[:, pl.ds(lo, 8), cols] = conv
        return carry

    lax.fori_loop(0, width // chunk, conv_chunk, 0)


def kept_taps(taps, kept, frames):
    return [[lo for lo in range(0, frames, 8) if lo < kept - j] for j in range(taps)]


def new_taps(taps, kept, frames):
    return [[lo for lo in range(0, frames, 8) if lo + 7 >= kept - j] for j in range(taps)]


def kept_conv_kernel(sel_ref, cw_ref, state_hbm, recv_hbm, out_ref, stv, pad_ref, gsem, *,
                     streams, frames, slot, kept):
    width = cw_ref.shape[1]
    rows = pad_ref.shape[1] - frames
    for j in range(streams):
        kind = sel_ref[j]
        idx = sel_ref[streams + j]

        @pl.when(kind == 0)
        def _():
            pltpu.make_async_copy(state_hbm.at[idx, pl.ds(2 * slot, rows)], stv.at[j],
                                  gsem.at[j]).start()

        @pl.when(kind != 0)
        def _():
            pltpu.make_async_copy(recv_hbm.at[idx, pl.ds(2 * slot, rows)], stv.at[j],
                                  gsem.at[j]).start()

    for j in range(streams):
        pltpu.make_async_copy(state_hbm.at[0, pl.ds(2 * slot, rows)], stv.at[j], gsem.at[j]).wait()
    pad_ref[:, 0:rows, :] = stv[...].astype(jnp.float32)
    pad_ref[:, rows:, :] = jnp.zeros((streams, frames, width), jnp.float32)
    out_ref[...] = jnp.zeros_like(out_ref)
    taps = cw_ref.shape[0]
    conv_rows(out_ref, pad_ref, cw_ref, kept_taps(taps, kept, frames), frames, rows - kept)


def kept_conv(sel, state, recv, conv_weight, streams, frames, ctx, kept):
    slot = -(-ctx // 16) * 16
    rows = state.shape[1] - 2 * slot
    width = state.shape[2]
    kernel = functools.partial(kept_conv_kernel, streams=streams, frames=frames, slot=slot,
                               kept=kept)
    vmem = pl.BlockSpec(memory_space=pltpu.VMEM)
    hbm = pl.BlockSpec(memory_space=pl.ANY)
    return pl.pallas_call(
        kernel,
        out_shape=jax.ShapeDtypeStruct((streams, frames, width), jnp.float32),
        in_specs=[pl.BlockSpec(memory_space=pltpu.SMEM), vmem, hbm, hbm],
        out_specs=vmem,
        scratch_shapes=[
            pltpu.VMEM((streams, rows, width), jnp.bfloat16),
            pltpu.VMEM((streams, rows + frames, width), jnp.float32),
            pltpu.SemaphoreType.DMA((streams,)),
        ],
    )(sel, conv_weight, state, recv)


def layer_kernel(sel_ref, x_ref, klive_ref, rlive_ref, cw_ref, qkv_hbm, wo_hbm, state_hbm,
                 recv_hbm, *rest, streams, frames, ctx, head_size, kept_real, early):
    if early:
        conv_in_ref, out_ref, wobuf, stv, qkv, conv_ref, pad_ref, res_ref, wsem, gsem = rest
    else:
        out_ref, wobuf, stv, qkv, conv_ref, pad_ref, res_ref, wsem, gsem = rest
    tokens = streams * frames
    width = x_ref.shape[1]
    slot = -(-ctx // 16) * 16
    kept = pad_ref.shape[1] - frames
    taps = cw_ref.shape[0]
    chunk = 128

    for j in range(streams):
        kind = sel_ref[j]
        idx = sel_ref[streams + j]

        @pl.when(kind == 0)
        def _():
            pltpu.make_async_copy(state_hbm.at[idx], stv.at[j], gsem.at[j]).start()

        @pl.when(kind != 0)
        def _():
            pltpu.make_async_copy(recv_hbm.at[idx], stv.at[j], gsem.at[j]).start()

    rows_w = wo_hbm.shape[0]
    copies = [pltpu.make_async_copy(qkv_hbm, qkv, wsem.at[0, 0])]
    for r in range(rows_w // CHUNK_ROWS):
        part = pl.ds(r * CHUNK_ROWS, CHUNK_ROWS)
        copies.append(pltpu.make_async_copy(wo_hbm.at[part], wobuf.at[part], wsem.at[1, r]))
    for c in copies:
        c.start()

    for j in range(streams):
        pltpu.make_async_copy(state_hbm.at[0], stv.at[j], gsem.at[j]).wait()

    copies[0].wait()

    rows_g = GROUP * frames
    cols_g = GROUP * slot
    q_stream = lax.broadcasted_iota(jnp.int32, (rows_g, cols_g), 0) // frames
    c_col = lax.broadcasted_iota(jnp.int32, (rows_g, cols_g), 1)
    bias_c = jnp.where((c_col // slot == q_stream) & (c_col % slot < ctx), 0.0, -1e30)
    k_stream = lax.broadcasted_iota(jnp.int32, (rows_g, rows_g), 1) // frames
    q_stream_n = lax.broadcasted_iota(jnp.int32, (rows_g, rows_g), 0) // frames
    same_n = q_stream_n == k_stream
    pair = 2 * head_size
    lane = lax.broadcasted_iota(jnp.int32, (rows_g, pair), 1)
    nt = (((1,), (1,)), ((), ()))
    for g in range(streams // GROUP):
        rows = pl.ds(g * rows_g, rows_g)
        srow = pl.ds(g * GROUP, GROUP)
        bias_n = jnp.where(same_n & (klive_ref[:, pl.ds(g * rows_g, rows_g)] > 0.0), 0.0, -1e30)

        def head_pair(p, carry):
            cols = pl.ds(pl.multiple_of(p * pair, pair), pair)
            q = qkv[0, rows, cols]
            k = qkv[1, rows, cols]
            v = qkv[2, rows, cols]
            ck = stv[srow, pl.ds(0, slot), cols].reshape(cols_g, pair)
            cv = stv[srow, pl.ds(slot, slot), cols].reshape(cols_g, pair)
            attended = None
            for half in range(pair // head_size):
                mine = (lane >= half * head_size) & (lane < (half + 1) * head_size)
                qh = jnp.where(mine, q, jnp.zeros_like(q))
                sc = lax.dot_general(qh, ck, nt, preferred_element_type=jnp.float32) + bias_c
                sn = lax.dot_general(qh, k, nt, preferred_element_type=jnp.float32) + bias_n
                top = jnp.maximum(jnp.max(sc, axis=-1, keepdims=True),
                                  jnp.max(sn, axis=-1, keepdims=True))
                ec = jnp.exp(sc - top)
                en = jnp.exp(sn - top)
                total = jnp.sum(ec, axis=-1, keepdims=True) + jnp.sum(en, axis=-1, keepdims=True)
                inv = 1.0 / total
                pc = (ec * inv).astype(jnp.bfloat16)
                pn = (en * inv).astype(jnp.bfloat16)
                oh = jnp.dot(pc, cv, preferred_element_type=jnp.float32) + jnp.dot(
                    pn, v, preferred_element_type=jnp.float32)
                attended = oh if attended is None else jnp.where(mine, oh, attended)
            qkv[0, rows, cols] = attended.astype(jnp.bfloat16)
            return carry

        lax.fori_loop(0, width // pair, head_pair, 0)

    for c in copies[1:]:
        c.wait()
    mixed = jnp.dot(qkv[0], wobuf[...], preferred_element_type=jnp.float32)
    residual = x_ref[...].astype(jnp.float32) + mixed
    res_ref[...] = residual
    rounded = residual.astype(jnp.bfloat16).astype(jnp.float32).reshape(streams, frames, width)
    origin = kept - kept_real
    if early:
        pad_ref[:, 0:kept, :] = jnp.zeros((streams, kept, width), jnp.float32)
        pad_ref[:, kept:, :] = rounded
        conv_ref[...] = conv_in_ref[...]
        conv_rows(conv_ref, pad_ref, cw_ref, new_taps(taps, kept_real, frames), frames, origin)
    else:
        pad_ref[:, 0:kept, :] = stv[:, pl.ds(2 * slot, kept), :].astype(jnp.float32)
        pad_ref[:, kept:, :] = rounded
        conv_ref[...] = jnp.zeros_like(conv_ref)
        every = [list(range(0, frames, 8))] * taps
        conv_rows(conv_ref, pad_ref, cw_ref, every, frames, origin)
    live = rlive_ref[...].reshape(streams, frames, 1)

    def finish(c, carry):
        cols = pl.ds(pl.multiple_of(c * chunk, chunk), chunk)
        conv = conv_ref[:, :, cols]
        res = res_ref[:, cols]
        silu = conv / (1.0 + jnp.exp(-conv))
        out = (res.reshape(streams, frames, chunk) + silu) * live
        out_ref[:, cols] = out.reshape(tokens, chunk).astype(out_ref.dtype)
        return carry

    lax.fori_loop(0, width // chunk, finish, 0)


def project(inputs, qkv_weight):
    streams, frames, width = inputs.shape
    tokens = streams * frames
    x = inputs.reshape(tokens, width)
    kernel = functools.partial(projection_kernel, head_size=width // HEADS)
    return pl.pallas_call(
        kernel,
        out_shape=jax.ShapeDtypeStruct((3, tokens, width), jnp.bfloat16),
        grid=(3,),
        in_specs=[pl.BlockSpec((tokens, width), lambda i: (0, 0)),
                  pl.BlockSpec((width, width), lambda i: (0, i))],
        out_specs=pl.BlockSpec((1, tokens, width), lambda i: (i, 0, 0)),
        scratch_shapes=[pltpu.VMEM((tokens, width), jnp.bfloat16)],
        compiler_params=pltpu.CompilerParams(dimension_semantics=("arbitrary",)),
    )(x, qkv_weight)


def encoder_layer(inputs, valid_counts, sel, state, recv, qkv_weight, out_weight, conv_weight,
                  ctx, kept_real, conv_in=None):
    streams, frames, width = inputs.shape
    taps = conv_weight.shape[0]
    head_size = width // HEADS
    tokens = streams * frames
    slot = -(-ctx // 16) * 16
    live = (jnp.arange(frames, dtype=jnp.int32)[None, :] < valid_counts[:, None]).astype(jnp.float32)
    klive = live.reshape(1, tokens)
    rlive = live.reshape(tokens, 1)
    x = inputs.reshape(tokens, width)
    kept = state.shape[1] - 2 * slot
    early = conv_in is not None
    kernel = functools.partial(layer_kernel, streams=streams, frames=frames, ctx=ctx,
                               head_size=head_size, kept_real=kept_real, early=early)
    vmem = pl.BlockSpec(memory_space=pltpu.VMEM)
    hbm = pl.BlockSpec(memory_space=pl.ANY)
    extra = [conv_in] if early else []
    out = pl.pallas_call(
        kernel,
        out_shape=jax.ShapeDtypeStruct((tokens, width), jnp.bfloat16),
        in_specs=[pl.BlockSpec(memory_space=pltpu.SMEM), vmem, vmem, vmem, vmem,
                  hbm, hbm, hbm, hbm] + [vmem] * len(extra),
        out_specs=vmem,
        scratch_shapes=[
            pltpu.VMEM((width, width), jnp.bfloat16),
            pltpu.VMEM((streams,) + state.shape[1:], jnp.bfloat16),
            pltpu.VMEM((3, tokens, width), jnp.bfloat16),
            pltpu.VMEM((streams, frames, width), jnp.float32),
            pltpu.VMEM((streams, kept + frames, width), jnp.float32),
            pltpu.VMEM((tokens, width), jnp.float32),
            pltpu.SemaphoreType.DMA((2, width // CHUNK_ROWS)),
            pltpu.SemaphoreType.DMA((streams,)),
        ],
    )(sel, x, klive, rlive, conv_weight, project(inputs, qkv_weight), out_weight, state, recv, *extra)
    return out.reshape(streams, frames, width)


def migrate(anchor, own, count, local_count, state):
    total = anchor.shape[0]
    every_slot = jnp.arange(total, dtype=jnp.int32)
    newpos = jnp.sum(jnp.where(anchor[None, :] == every_slot[:, None], every_slot[None, :], 0),
                     axis=1)
    mine_new = lax.dynamic_slice_in_dim(newpos, own * local_count, local_count)
    target = mine_new // local_count
    hosts = jnp.arange(count, dtype=jnp.int32)
    match = target[None, :] == hosts[:, None]
    send_slot = jnp.sum(jnp.where(match, jnp.arange(local_count, dtype=jnp.int32)[None, :], 0),
                        axis=1)
    recv = lax.all_to_all(jnp.take(state, send_slot, axis=0), "stream", 0, 0, tiled=True)
    mine_old = lax.dynamic_slice_in_dim(anchor, own * local_count, local_count)
    source = mine_old // local_count
    staying = source == own
    local_idx = jnp.clip(mine_old - own * local_count, 0, local_count - 1)
    recv_idx = jnp.clip(source, 0, count - 1)
    sel = jnp.concatenate([jnp.where(staying, 0, 1), jnp.where(staying, local_idx, recv_idx)])
    return sel.astype(jnp.int32), recv


def body(
    new_frames, valid_counts, anchor, context_cache, conv_state, qkv_weight, out_weight, conv_weight
):
    local_count = new_frames.shape[0]
    own = lax.axis_index("stream")
    count = lax.axis_size("stream")
    ctx = context_cache.shape[2]
    width = conv_state.shape[3]
    slot = -(-ctx // 16) * 16
    kept = conv_state.shape[2]
    lead = (-kept) % 16
    context = context_cache[0]
    state = jnp.concatenate([
        jnp.pad(context[:, :, :width], ((0, 0), (0, slot - ctx), (0, 0))),
        jnp.pad(context[:, :, width:], ((0, 0), (0, slot - ctx), (0, 0))),
        jnp.pad(conv_state[0], ((0, 0), (lead, 0), (0, 0))),
    ], axis=1)
    sel, recv = migrate(anchor, own, count, local_count, state)
    valid_here = lax.dynamic_slice_in_dim(valid_counts, own * local_count, local_count)
    section_index = lax.axis_index("section")
    layer = functools.partial(encoder_layer, valid_counts=valid_here, sel=sel, state=state,
                              recv=recv, qkv_weight=qkv_weight[0], out_weight=out_weight[0],
                              conv_weight=conv_weight[0], ctx=ctx, kept_real=kept)
    first = layer(new_frames)
    inbound = shifted(first, "section", 1)
    early = kept_conv(sel, state, recv, conv_weight[0], local_count, new_frames.shape[1], ctx, kept)
    second = layer(inbound, conv_in=early)
    result = jnp.where(section_index == 0, first, second)
    return result[None]


def solution(mesh):
    return jax.shard_map(
        body,
        mesh=mesh,
        in_specs=(
            P(("groups", "stream"), None, None),
            P("groups"),
            P("groups"),
            P("section", ("groups", "stream"), None, None),
            P("section", ("groups", "stream"), None, None),
            P("section", None, None),
            P("section", None, None),
            P("section", None, None),
        ),
        out_specs=P("section", ("groups", "stream"), None, None),
        check_vma=False,
    )
```

```python
import functools

import jax
import jax.numpy as jnp
from jax import lax
from jax.experimental import pallas as pl
from jax.experimental.pallas import tpu as pltpu
from jax.sharding import PartitionSpec as P

HEADS = 16
GROUP = 16
CHUNK_ROWS = 128


def shifted(value, axis, steps):
    count = lax.axis_size(axis)
    leading, last = (max(0, -steps), min(count, count - steps))
    return lax.ppermute(value, axis, [(source, source + steps) for source in range(leading, last)])


def projection_kernel(x_ref, w_ref, out_ref, nrm_ref, *, head_size):
    step = pl.program_id(0)

    @pl.when(step == 0)
    def _():
        floats = x_ref[...].astype(jnp.float32)
        centred = floats - jnp.mean(floats, axis=-1, keepdims=True)
        variance = jnp.mean(centred * centred, axis=-1, keepdims=True)
        nrm_ref[...] = (centred * lax.rsqrt(variance + 1e-05)).astype(jnp.bfloat16)

    part = jnp.dot(nrm_ref[...], w_ref[...], preferred_element_type=jnp.float32)
    scale = jnp.where(step == 0, head_size ** -0.5, 1.0).astype(jnp.float32)
    out_ref[0] = (part * scale).astype(out_ref.dtype)


def conv_rows(conv_ref, pad_ref, cw_ref, tap_rows, frames, origin):
    width = cw_ref.shape[1]
    chunk = 128

    def conv_chunk(c, carry):
        cols = pl.ds(pl.multiple_of(c * chunk, chunk), chunk)
        for lo in range(0, frames, 8):
            conv = conv_ref[:, pl.ds(lo, 8), cols]
            for j, rows in enumerate(tap_rows):
                if lo in rows:
                    conv = conv + cw_ref[pl.ds(j, 1), cols].reshape(1, 1, chunk) * pad_ref[
                        :, pl.ds(origin + j + lo, 8), cols]
            conv_ref[:, pl.ds(lo, 8), cols] = conv
        return carry

    lax.fori_loop(0, width // chunk, conv_chunk, 0)


def kept_taps(taps, kept, frames):
    return [[lo for lo in range(0, frames, 8) if lo < kept - j] for j in range(taps)]


def new_taps(taps, kept, frames):
    return [[lo for lo in range(0, frames, 8) if lo + 7 >= kept - j] for j in range(taps)]


def kept_conv_kernel(sel_ref, cw_ref, state_hbm, recv_hbm, out_ref, stv, pad_ref, gsem, *,
                     streams, frames, slot, kept):
    width = cw_ref.shape[1]
    rows = pad_ref.shape[1] - frames
    for j in range(streams):
        kind = sel_ref[j]
        idx = sel_ref[streams + j]

        @pl.when(kind == 0)
        def _():
            pltpu.make_async_copy(state_hbm.at[idx, pl.ds(2 * slot, rows)], stv.at[j],
                                  gsem.at[j]).start()

        @pl.when(kind != 0)
        def _():
            pltpu.make_async_copy(recv_hbm.at[idx, pl.ds(2 * slot, rows)], stv.at[j],
                                  gsem.at[j]).start()

    for j in range(streams):
        pltpu.make_async_copy(state_hbm.at[0, pl.ds(2 * slot, rows)], stv.at[j], gsem.at[j]).wait()
    pad_ref[:, 0:rows, :] = stv[...].astype(jnp.float32)
    pad_ref[:, rows:, :] = jnp.zeros((streams, frames, width), jnp.float32)
    out_ref[...] = jnp.zeros_like(out_ref)
    taps = cw_ref.shape[0]
    conv_rows(out_ref, pad_ref, cw_ref, kept_taps(taps, kept, frames), frames, rows - kept)


def kept_conv(sel, state, recv, conv_weight, streams, frames, ctx, kept):
    slot = -(-ctx // 16) * 16
    rows = state.shape[1] - 2 * slot
    width = state.shape[2]
    kernel = functools.partial(kept_conv_kernel, streams=streams, frames=frames, slot=slot,
                               kept=kept)
    vmem = pl.BlockSpec(memory_space=pltpu.VMEM)
    hbm = pl.BlockSpec(memory_space=pl.ANY)
    return pl.pallas_call(
        kernel,
        out_shape=jax.ShapeDtypeStruct((streams, frames, width), jnp.float32),
        in_specs=[pl.BlockSpec(memory_space=pltpu.SMEM), vmem, hbm, hbm],
        out_specs=vmem,
        scratch_shapes=[
            pltpu.VMEM((streams, rows, width), jnp.bfloat16),
            pltpu.VMEM((streams, rows + frames, width), jnp.float32),
            pltpu.SemaphoreType.DMA((streams,)),
        ],
    )(sel, conv_weight, state, recv)


def layer_kernel(sel_ref, x_ref, klive_ref, rlive_ref, cw_ref, qkv_hbm, wo_hbm, state_hbm,
                 recv_hbm, *rest, streams, frames, ctx, head_size, kept_real, early):
    if early:
        conv_in_ref, out_ref, wobuf, stv, qkv, conv_ref, pad_ref, res_ref, wsem, gsem = rest
    else:
        out_ref, wobuf, stv, qkv, conv_ref, pad_ref, res_ref, wsem, gsem = rest
    tokens = streams * frames
    width = x_ref.shape[1]
    slot = -(-ctx // 16) * 16
    kept = pad_ref.shape[1] - frames
    taps = cw_ref.shape[0]
    chunk = 128

    for j in range(streams):
        kind = sel_ref[j]
        idx = sel_ref[streams + j]

        @pl.when(kind == 0)
        def _():
            pltpu.make_async_copy(state_hbm.at[idx], stv.at[j], gsem.at[j]).start()

        @pl.when(kind != 0)
        def _():
            pltpu.make_async_copy(recv_hbm.at[idx], stv.at[j], gsem.at[j]).start()

    rows_w = wo_hbm.shape[0]
    copies = [pltpu.make_async_copy(qkv_hbm, qkv, wsem.at[0, 0])]
    for r in range(rows_w // CHUNK_ROWS):
        part = pl.ds(r * CHUNK_ROWS, CHUNK_ROWS)
        copies.append(pltpu.make_async_copy(wo_hbm.at[part], wobuf.at[part], wsem.at[1, r]))
    for c in copies:
        c.start()

    for j in range(streams):
        pltpu.make_async_copy(state_hbm.at[0], stv.at[j], gsem.at[j]).wait()

    copies[0].wait()

    rows_g = GROUP * frames
    cols_g = GROUP * slot
    q_stream = lax.broadcasted_iota(jnp.int32, (rows_g, cols_g), 0) // frames
    c_col = lax.broadcasted_iota(jnp.int32, (rows_g, cols_g), 1)
    bias_c = jnp.where((c_col // slot == q_stream) & (c_col % slot < ctx), 0.0, -1e30)
    k_stream = lax.broadcasted_iota(jnp.int32, (rows_g, rows_g), 1) // frames
    q_stream_n = lax.broadcasted_iota(jnp.int32, (rows_g, rows_g), 0) // frames
    same_n = q_stream_n == k_stream
    pair = 2 * head_size
    lane = lax.broadcasted_iota(jnp.int32, (rows_g, pair), 1)
    nt = (((1,), (1,)), ((), ()))
    for g in range(streams // GROUP):
        rows = pl.ds(g * rows_g, rows_g)
        srow = pl.ds(g * GROUP, GROUP)
        bias_n = jnp.where(same_n & (klive_ref[:, pl.ds(g * rows_g, rows_g)] > 0.0), 0.0, -1e30)

        def head_pair(p, carry):
            cols = pl.ds(pl.multiple_of(p * pair, pair), pair)
            q = qkv[0, rows, cols]
            k = qkv[1, rows, cols]
            v = qkv[2, rows, cols]
            ck = stv[srow, pl.ds(0, slot), cols].reshape(cols_g, pair)
            cv = stv[srow, pl.ds(slot, slot), cols].reshape(cols_g, pair)
            attended = None
            for half in range(pair // head_size):
                mine = (lane >= half * head_size) & (lane < (half + 1) * head_size)
                qh = jnp.where(mine, q, jnp.zeros_like(q))
                sc = lax.dot_general(qh, ck, nt, preferred_element_type=jnp.float32) + bias_c
                sn = lax.dot_general(qh, k, nt, preferred_element_type=jnp.float32) + bias_n
                top = jnp.maximum(jnp.max(sc, axis=-1, keepdims=True),
                                  jnp.max(sn, axis=-1, keepdims=True))
                ec = jnp.exp(sc - top)
                en = jnp.exp(sn - top)
                total = jnp.sum(ec, axis=-1, keepdims=True) + jnp.sum(en, axis=-1, keepdims=True)
                inv = 1.0 / total
                pc = (ec * inv).astype(jnp.bfloat16)
                pn = (en * inv).astype(jnp.bfloat16)
                oh = jnp.dot(pc, cv, preferred_element_type=jnp.float32) + jnp.dot(
                    pn, v, preferred_element_type=jnp.float32)
                attended = oh if attended is None else jnp.where(mine, oh, attended)
            qkv[0, rows, cols] = attended.astype(jnp.bfloat16)
            return carry

        lax.fori_loop(0, width // pair, head_pair, 0)

    for c in copies[1:]:
        c.wait()
    mixed = jnp.dot(qkv[0], wobuf[...], preferred_element_type=jnp.float32)
    residual = x_ref[...].astype(jnp.float32) + mixed
    res_ref[...] = residual
    rounded = residual.astype(jnp.bfloat16).astype(jnp.float32).reshape(streams, frames, width)
    origin = kept - kept_real
    if early:
        pad_ref[:, 0:kept, :] = jnp.zeros((streams, kept, width), jnp.float32)
        pad_ref[:, kept:, :] = rounded
        conv_ref[...] = conv_in_ref[...]
        conv_rows(conv_ref, pad_ref, cw_ref, new_taps(taps, kept_real, frames), frames, origin)
    else:
        pad_ref[:, 0:kept, :] = stv[:, pl.ds(2 * slot, kept), :].astype(jnp.float32)
        pad_ref[:, kept:, :] = rounded
        conv_ref[...] = jnp.zeros_like(conv_ref)
        every = [list(range(0, frames, 8))] * taps
        conv_rows(conv_ref, pad_ref, cw_ref, every, frames, origin)
    live = rlive_ref[...].reshape(streams, frames, 1)

    def finish(c, carry):
        cols = pl.ds(pl.multiple_of(c * chunk, chunk), chunk)
        conv = conv_ref[:, :, cols]
        res = res_ref[:, cols]
        silu = conv / (1.0 + jnp.exp(-conv))
        out = (res.reshape(streams, frames, chunk) + silu) * live
        out_ref[:, cols] = out.reshape(tokens, chunk).astype(out_ref.dtype)
        return carry

    lax.fori_loop(0, width // chunk, finish, 0)


def project(inputs, qkv_weight):
    streams, frames, width = inputs.shape
    tokens = streams * frames
    x = inputs.reshape(tokens, width)
    kernel = functools.partial(projection_kernel, head_size=width // HEADS)
    return pl.pallas_call(
        kernel,
        out_shape=jax.ShapeDtypeStruct((3, tokens, width), jnp.bfloat16),
        grid=(3,),
        in_specs=[pl.BlockSpec((tokens, width), lambda i: (0, 0)),
                  pl.BlockSpec((width, width), lambda i: (0, i))],
        out_specs=pl.BlockSpec((1, tokens, width), lambda i: (i, 0, 0)),
        scratch_shapes=[pltpu.VMEM((tokens, width), jnp.bfloat16)],
        compiler_params=pltpu.CompilerParams(dimension_semantics=("arbitrary",)),
    )(x, qkv_weight)


def encoder_layer(inputs, valid_counts, sel, state, recv, qkv_weight, out_weight, conv_weight,
                  ctx, kept_real, conv_in=None, projected=None):
    streams, frames, width = inputs.shape
    taps = conv_weight.shape[0]
    head_size = width // HEADS
    tokens = streams * frames
    slot = -(-ctx // 16) * 16
    live = (jnp.arange(frames, dtype=jnp.int32)[None, :] < valid_counts[:, None]).astype(jnp.float32)
    klive = live.reshape(1, tokens)
    rlive = live.reshape(tokens, 1)
    x = inputs.reshape(tokens, width)
    kept = state.shape[1] - 2 * slot
    early = conv_in is not None
    kernel = functools.partial(layer_kernel, streams=streams, frames=frames, ctx=ctx,
                               head_size=head_size, kept_real=kept_real, early=early)
    vmem = pl.BlockSpec(memory_space=pltpu.VMEM)
    hbm = pl.BlockSpec(memory_space=pl.ANY)
    extra = [conv_in] if early else []
    out = pl.pallas_call(
        kernel,
        out_shape=jax.ShapeDtypeStruct((tokens, width), jnp.bfloat16),
        in_specs=[pl.BlockSpec(memory_space=pltpu.SMEM), vmem, vmem, vmem, vmem,
                  hbm, hbm, hbm, hbm] + [vmem] * len(extra),
        out_specs=vmem,
        scratch_shapes=[
            pltpu.VMEM((width, width), jnp.bfloat16),
            pltpu.VMEM((streams,) + state.shape[1:], jnp.bfloat16),
            pltpu.VMEM((3, tokens, width), jnp.bfloat16),
            pltpu.VMEM((streams, frames, width), jnp.float32),
            pltpu.VMEM((streams, kept + frames, width), jnp.float32),
            pltpu.VMEM((tokens, width), jnp.float32),
            pltpu.SemaphoreType.DMA((2, width // CHUNK_ROWS)),
            pltpu.SemaphoreType.DMA((streams,)),
        ],
    )(sel, x, klive, rlive, conv_weight, project(inputs, qkv_weight) if projected is None else projected,
      out_weight, state, recv, *extra)
    return out.reshape(streams, frames, width)


def migrate(anchor, own, count, local_count, state):
    total = anchor.shape[0]
    every_slot = jnp.arange(total, dtype=jnp.int32)
    newpos = jnp.sum(jnp.where(anchor[None, :] == every_slot[:, None], every_slot[None, :], 0),
                     axis=1)
    mine_new = lax.dynamic_slice_in_dim(newpos, own * local_count, local_count)
    target = mine_new // local_count
    hosts = jnp.arange(count, dtype=jnp.int32)
    match = target[None, :] == hosts[:, None]
    send_slot = jnp.sum(jnp.where(match, jnp.arange(local_count, dtype=jnp.int32)[None, :], 0),
                        axis=1)
    recv = lax.all_to_all(jnp.take(state, send_slot, axis=0), "stream", 0, 0, tiled=True)
    mine_old = lax.dynamic_slice_in_dim(anchor, own * local_count, local_count)
    source = mine_old // local_count
    staying = source == own
    local_idx = jnp.clip(mine_old - own * local_count, 0, local_count - 1)
    recv_idx = jnp.clip(source, 0, count - 1)
    sel = jnp.concatenate([jnp.where(staying, 0, 1), jnp.where(staying, local_idx, recv_idx)])
    return sel.astype(jnp.int32), recv


def body(
    new_frames, valid_counts, anchor, context_cache, conv_state, qkv_weight, out_weight, conv_weight
):
    local_count = new_frames.shape[0]
    own = lax.axis_index("stream")
    count = lax.axis_size("stream")
    ctx = context_cache.shape[2]
    width = conv_state.shape[3]
    slot = -(-ctx // 16) * 16
    kept = conv_state.shape[2]
    lead = (-kept) % 16
    context = context_cache[0]
    state = jnp.concatenate([
        jnp.pad(context[:, :, :width], ((0, 0), (0, slot - ctx), (0, 0))),
        jnp.pad(context[:, :, width:], ((0, 0), (0, slot - ctx), (0, 0))),
        jnp.pad(conv_state[0], ((0, 0), (lead, 0), (0, 0))),
    ], axis=1)
    sel, recv = migrate(anchor, own, count, local_count, state)
    valid_here = lax.dynamic_slice_in_dim(valid_counts, own * local_count, local_count)
    section_index = lax.axis_index("section")
    layer = functools.partial(encoder_layer, valid_counts=valid_here, sel=sel, state=state,
                              recv=recv, qkv_weight=qkv_weight[0], out_weight=out_weight[0],
                              conv_weight=conv_weight[0], ctx=ctx, kept_real=kept)
    on_first = section_index == 0
    frames = new_frames.shape[1]
    like = lambda shape, dtype: (lambda: jnp.zeros(shape, dtype))
    projected = lax.cond(on_first, lambda: project(new_frames, qkv_weight[0]),
                         like((3, local_count * frames, width), jnp.bfloat16))
    first = lax.cond(on_first, lambda: layer(new_frames, projected=projected),
                     like(new_frames.shape, new_frames.dtype))
    early = lax.cond(on_first, like(new_frames.shape, jnp.float32),
                     lambda: kept_conv(sel, state, recv, conv_weight[0], local_count, frames, ctx,
                                       kept))
    inbound = shifted(first, "section", 1)
    second = lax.cond(on_first, like(new_frames.shape, new_frames.dtype),
                      lambda: layer(inbound, conv_in=early))
    result = jnp.where(on_first, first, second)
    return result[None]


def solution(mesh):
    return jax.shard_map(
        body,
        mesh=mesh,
        in_specs=(
            P(("groups", "stream"), None, None),
            P("groups"),
            P("groups"),
            P("section", ("groups", "stream"), None, None),
            P("section", ("groups", "stream"), None, None),
            P("section", None, None),
            P("section", None, None),
            P("section", None, None),
        ),
        out_specs=P("section", ("groups", "stream"), None, None),
        check_vma=False,
    )
```

```python
import functools

import jax
import jax.numpy as jnp
from jax import lax
from jax.experimental import pallas as pl
from jax.experimental.pallas import tpu as pltpu
from jax.sharding import PartitionSpec as P

HEADS = 16
GROUP = 16
CHUNK_ROWS = 128


def shifted(value, axis, steps):
    count = lax.axis_size(axis)
    leading, last = (max(0, -steps), min(count, count - steps))
    return lax.ppermute(value, axis, [(source, source + steps) for source in range(leading, last)])


def projection_kernel(x_ref, w_ref, out_ref, nrm_ref, *, head_size):
    step = pl.program_id(0)

    @pl.when(step == 0)
    def _():
        floats = x_ref[...].astype(jnp.float32)
        centred = floats - jnp.mean(floats, axis=-1, keepdims=True)
        variance = jnp.mean(centred * centred, axis=-1, keepdims=True)
        nrm_ref[...] = (centred * lax.rsqrt(variance + 1e-05)).astype(jnp.bfloat16)

    part = jnp.dot(nrm_ref[...], w_ref[...], preferred_element_type=jnp.float32)
    scale = jnp.where(step == 0, head_size ** -0.5, 1.0).astype(jnp.float32)
    out_ref[0] = (part * scale).astype(out_ref.dtype)


def conv_rows(conv_ref, pad_ref, cw_ref, tap_rows, frames, origin):
    width = cw_ref.shape[1]
    chunk = 128

    def conv_chunk(c, carry):
        cols = pl.ds(pl.multiple_of(c * chunk, chunk), chunk)
        for lo in range(0, frames, 8):
            conv = conv_ref[:, pl.ds(lo, 8), cols]
            for j, rows in enumerate(tap_rows):
                if lo in rows:
                    conv = conv + cw_ref[pl.ds(j, 1), cols].reshape(1, 1, chunk) * pad_ref[
                        :, pl.ds(origin + j + lo, 8), cols]
            conv_ref[:, pl.ds(lo, 8), cols] = conv
        return carry

    lax.fori_loop(0, width // chunk, conv_chunk, 0)


def kept_taps(taps, kept, frames):
    return [[lo for lo in range(0, frames, 8) if lo < kept - j] for j in range(taps)]


def new_taps(taps, kept, frames):
    return [[lo for lo in range(0, frames, 8) if lo + 7 >= kept - j] for j in range(taps)]


def kept_conv_kernel(sel_ref, cw_ref, state_hbm, recv_hbm, out_ref, stv, pad_ref, gsem, *,
                     streams, frames, slot, kept):
    width = cw_ref.shape[1]
    rows = pad_ref.shape[1] - frames
    for j in range(streams):
        kind = sel_ref[j]
        idx = sel_ref[streams + j]

        @pl.when(kind == 0)
        def _():
            pltpu.make_async_copy(state_hbm.at[idx, pl.ds(2 * slot, rows)], stv.at[j],
                                  gsem.at[j]).start()

        @pl.when(kind != 0)
        def _():
            pltpu.make_async_copy(recv_hbm.at[idx, pl.ds(2 * slot, rows)], stv.at[j],
                                  gsem.at[j]).start()

    for j in range(streams):
        pltpu.make_async_copy(state_hbm.at[0, pl.ds(2 * slot, rows)], stv.at[j], gsem.at[j]).wait()
    pad_ref[:, 0:rows, :] = stv[...].astype(jnp.float32)
    pad_ref[:, rows:, :] = jnp.zeros((streams, frames, width), jnp.float32)
    out_ref[...] = jnp.zeros_like(out_ref)
    taps = cw_ref.shape[0]
    conv_rows(out_ref, pad_ref, cw_ref, kept_taps(taps, kept, frames), frames, rows - kept)


def kept_conv(sel, state, recv, conv_weight, streams, frames, ctx, kept):
    slot = -(-ctx // 16) * 16
    rows = state.shape[1] - 2 * slot
    width = state.shape[2]
    kernel = functools.partial(kept_conv_kernel, streams=streams, frames=frames, slot=slot,
                               kept=kept)
    vmem = pl.BlockSpec(memory_space=pltpu.VMEM)
    hbm = pl.BlockSpec(memory_space=pl.ANY)
    return pl.pallas_call(
        kernel,
        out_shape=jax.ShapeDtypeStruct((streams, frames, width), jnp.float32),
        in_specs=[pl.BlockSpec(memory_space=pltpu.SMEM), vmem, hbm, hbm],
        out_specs=vmem,
        scratch_shapes=[
            pltpu.VMEM((streams, rows, width), jnp.bfloat16),
            pltpu.VMEM((streams, rows + frames, width), jnp.float32),
            pltpu.SemaphoreType.DMA((streams,)),
        ],
    )(sel, conv_weight, state, recv)


def layer_kernel(sel_ref, x_ref, klive_ref, rlive_ref, cw_ref, qkv_hbm, wo_hbm, state_hbm,
                 recv_hbm, *rest, streams, frames, ctx, head_size, kept_real, early):
    if early:
        conv_in_ref, out_ref, wobuf, stv, qkv, conv_ref, pad_ref, res_ref, wsem, gsem = rest
    else:
        out_ref, wobuf, stv, qkv, conv_ref, pad_ref, res_ref, wsem, gsem = rest
    tokens = streams * frames
    width = x_ref.shape[1]
    slot = -(-ctx // 16) * 16
    kept = pad_ref.shape[1] - frames
    taps = cw_ref.shape[0]
    chunk = 128

    for j in range(streams):
        kind = sel_ref[j]
        idx = sel_ref[streams + j]

        @pl.when(kind == 0)
        def _():
            pltpu.make_async_copy(state_hbm.at[idx], stv.at[j], gsem.at[j]).start()

        @pl.when(kind != 0)
        def _():
            pltpu.make_async_copy(recv_hbm.at[idx], stv.at[j], gsem.at[j]).start()

    rows_w = wo_hbm.shape[0]
    copies = [pltpu.make_async_copy(qkv_hbm, qkv, wsem.at[0, 0])]
    for r in range(rows_w // CHUNK_ROWS):
        part = pl.ds(r * CHUNK_ROWS, CHUNK_ROWS)
        copies.append(pltpu.make_async_copy(wo_hbm.at[part], wobuf.at[part], wsem.at[1, r]))
    for c in copies:
        c.start()

    for j in range(streams):
        pltpu.make_async_copy(state_hbm.at[0], stv.at[j], gsem.at[j]).wait()

    copies[0].wait()

    rows_g = GROUP * frames
    cols_g = GROUP * slot
    q_stream = lax.broadcasted_iota(jnp.int32, (rows_g, cols_g), 0) // frames
    c_col = lax.broadcasted_iota(jnp.int32, (rows_g, cols_g), 1)
    bias_c = jnp.where((c_col // slot == q_stream) & (c_col % slot < ctx), 0.0, -1e30)
    k_stream = lax.broadcasted_iota(jnp.int32, (rows_g, rows_g), 1) // frames
    q_stream_n = lax.broadcasted_iota(jnp.int32, (rows_g, rows_g), 0) // frames
    same_n = q_stream_n == k_stream
    pair = 2 * head_size
    lane = lax.broadcasted_iota(jnp.int32, (rows_g, pair), 1)
    nt = (((1,), (1,)), ((), ()))
    for g in range(streams // GROUP):
        rows = pl.ds(g * rows_g, rows_g)
        srow = pl.ds(g * GROUP, GROUP)
        bias_n = jnp.where(same_n & (klive_ref[:, pl.ds(g * rows_g, rows_g)] > 0.0), 0.0, -1e30)

        def head_pair(p, carry):
            cols = pl.ds(pl.multiple_of(p * pair, pair), pair)
            q = qkv[0, rows, cols]
            k = qkv[1, rows, cols]
            v = qkv[2, rows, cols]
            ck = stv[srow, pl.ds(0, slot), cols].reshape(cols_g, pair)
            cv = stv[srow, pl.ds(slot, slot), cols].reshape(cols_g, pair)
            attended = None
            for half in range(pair // head_size):
                mine = (lane >= half * head_size) & (lane < (half + 1) * head_size)
                qh = jnp.where(mine, q, jnp.zeros_like(q))
                sc = lax.dot_general(qh, ck, nt, preferred_element_type=jnp.float32) + bias_c
                sn = lax.dot_general(qh, k, nt, preferred_element_type=jnp.float32) + bias_n
                top = jnp.maximum(jnp.max(sc, axis=-1, keepdims=True),
                                  jnp.max(sn, axis=-1, keepdims=True))
                ec = jnp.exp(sc - top)
                en = jnp.exp(sn - top)
                total = jnp.sum(ec, axis=-1, keepdims=True) + jnp.sum(en, axis=-1, keepdims=True)
                inv = 1.0 / total
                pc = (ec * inv).astype(jnp.bfloat16)
                pn = (en * inv).astype(jnp.bfloat16)
                oh = jnp.dot(pc, cv, preferred_element_type=jnp.float32) + jnp.dot(
                    pn, v, preferred_element_type=jnp.float32)
                attended = oh if attended is None else jnp.where(mine, oh, attended)
            qkv[0, rows, cols] = attended.astype(jnp.bfloat16)
            return carry

        lax.fori_loop(0, width // pair, head_pair, 0)

    for c in copies[1:]:
        c.wait()
    mixed = jnp.dot(qkv[0], wobuf[...], preferred_element_type=jnp.float32)
    residual = x_ref[...].astype(jnp.float32) + mixed
    res_ref[...] = residual
    rounded = residual.astype(jnp.bfloat16).astype(jnp.float32).reshape(streams, frames, width)
    origin = kept - kept_real
    if early:
        pad_ref[:, 0:kept, :] = jnp.zeros((streams, kept, width), jnp.float32)
        pad_ref[:, kept:, :] = rounded
        conv_ref[...] = conv_in_ref[...]
        conv_rows(conv_ref, pad_ref, cw_ref, new_taps(taps, kept_real, frames), frames, origin)
    else:
        pad_ref[:, 0:kept, :] = stv[:, pl.ds(2 * slot, kept), :].astype(jnp.float32)
        pad_ref[:, kept:, :] = rounded
        conv_ref[...] = jnp.zeros_like(conv_ref)
        every = [list(range(0, frames, 8))] * taps
        conv_rows(conv_ref, pad_ref, cw_ref, every, frames, origin)
    live = rlive_ref[...].reshape(streams, frames, 1)

    def finish(c, carry):
        cols = pl.ds(pl.multiple_of(c * chunk, chunk), chunk)
        conv = conv_ref[:, :, cols]
        res = res_ref[:, cols]
        silu = conv / (1.0 + jnp.exp(-conv))
        out = (res.reshape(streams, frames, chunk) + silu) * live
        out_ref[:, cols] = out.reshape(tokens, chunk).astype(out_ref.dtype)
        return carry

    lax.fori_loop(0, width // chunk, finish, 0)


def project(inputs, qkv_weight):
    streams, frames, width = inputs.shape
    tokens = streams * frames
    x = inputs.reshape(tokens, width)
    kernel = functools.partial(projection_kernel, head_size=width // HEADS)
    return pl.pallas_call(
        kernel,
        out_shape=jax.ShapeDtypeStruct((3, tokens, width), jnp.bfloat16),
        grid=(3,),
        in_specs=[pl.BlockSpec((tokens, width), lambda i: (0, 0)),
                  pl.BlockSpec((width, width), lambda i: (0, i))],
        out_specs=pl.BlockSpec((1, tokens, width), lambda i: (i, 0, 0)),
        scratch_shapes=[pltpu.VMEM((tokens, width), jnp.bfloat16)],
        compiler_params=pltpu.CompilerParams(dimension_semantics=("arbitrary",)),
    )(x, qkv_weight)


def encoder_layer(inputs, valid_counts, sel, state, recv, qkv_weight, out_weight, conv_weight,
                  ctx, kept_real, conv_in=None, projected=None):
    streams, frames, width = inputs.shape
    taps = conv_weight.shape[0]
    head_size = width // HEADS
    tokens = streams * frames
    slot = -(-ctx // 16) * 16
    live = (jnp.arange(frames, dtype=jnp.int32)[None, :] < valid_counts[:, None]).astype(jnp.float32)
    klive = live.reshape(1, tokens)
    rlive = live.reshape(tokens, 1)
    x = inputs.reshape(tokens, width)
    kept = state.shape[1] - 2 * slot
    early = conv_in is not None
    kernel = functools.partial(layer_kernel, streams=streams, frames=frames, ctx=ctx,
                               head_size=head_size, kept_real=kept_real, early=early)
    vmem = pl.BlockSpec(memory_space=pltpu.VMEM)
    hbm = pl.BlockSpec(memory_space=pl.ANY)
    extra = [conv_in] if early else []
    out = pl.pallas_call(
        kernel,
        out_shape=jax.ShapeDtypeStruct((tokens, width), jnp.bfloat16),
        in_specs=[pl.BlockSpec(memory_space=pltpu.SMEM), vmem, vmem, vmem, vmem,
                  hbm, hbm, hbm, hbm] + [vmem] * len(extra),
        out_specs=vmem,
        scratch_shapes=[
            pltpu.VMEM((width, width), jnp.bfloat16),
            pltpu.VMEM((streams,) + state.shape[1:], jnp.bfloat16),
            pltpu.VMEM((3, tokens, width), jnp.bfloat16),
            pltpu.VMEM((streams, frames, width), jnp.float32),
            pltpu.VMEM((streams, kept + frames, width), jnp.float32),
            pltpu.VMEM((tokens, width), jnp.float32),
            pltpu.SemaphoreType.DMA((2, width // CHUNK_ROWS)),
            pltpu.SemaphoreType.DMA((streams,)),
        ],
    )(sel, x, klive, rlive, conv_weight, project(inputs, qkv_weight) if projected is None else projected,
      out_weight, state, recv, *extra)
    return out.reshape(streams, frames, width)


def migrate(anchor, own, count, local_count, packed):
    total = anchor.shape[0]
    every_slot = jnp.arange(total, dtype=jnp.int32)
    newpos = jnp.sum(jnp.where(anchor[None, :] == every_slot[:, None], every_slot[None, :], 0),
                     axis=1)
    mine_new = lax.dynamic_slice_in_dim(newpos, own * local_count, local_count)
    target = mine_new // local_count
    hosts = jnp.arange(count, dtype=jnp.int32)
    match = target[None, :] == hosts[:, None]
    send_slot = jnp.sum(jnp.where(match, jnp.arange(local_count, dtype=jnp.int32)[None, :], 0),
                        axis=1)
    recv = lax.all_to_all(jnp.take(packed, send_slot, axis=0), "stream", 0, 0, tiled=True)
    mine_old = lax.dynamic_slice_in_dim(anchor, own * local_count, local_count)
    source = mine_old // local_count
    staying = source == own
    local_idx = jnp.clip(mine_old - own * local_count, 0, local_count - 1)
    recv_idx = jnp.clip(source, 0, count - 1)
    sel = jnp.concatenate([jnp.where(staying, 0, 1), jnp.where(staying, local_idx, recv_idx)])
    return sel.astype(jnp.int32), recv


def body(
    new_frames, valid_counts, anchor, context_cache, conv_state, qkv_weight, out_weight, conv_weight
):
    local_count = new_frames.shape[0]
    own = lax.axis_index("stream")
    count = lax.axis_size("stream")
    ctx = context_cache.shape[2]
    width = conv_state.shape[3]
    slot = -(-ctx // 16) * 16
    kept = conv_state.shape[2]
    lead = (-kept) % 16
    context = context_cache[0]
    state = jnp.concatenate([
        jnp.pad(context[:, :, :width], ((0, 0), (0, slot - ctx), (0, 0))),
        jnp.pad(context[:, :, width:], ((0, 0), (0, slot - ctx), (0, 0))),
        jnp.pad(conv_state[0], ((0, 0), (lead, 0), (0, 0))),
    ], axis=1)
    packed = jnp.concatenate([context[:, :, :width], context[:, :, width:], conv_state[0]], axis=1)
    sel, recv = migrate(anchor, own, count, local_count, packed)
    recv = jnp.concatenate([
        jnp.pad(recv[:, :ctx], ((0, 0), (0, slot - ctx), (0, 0))),
        jnp.pad(recv[:, ctx:2 * ctx], ((0, 0), (0, slot - ctx), (0, 0))),
        jnp.pad(recv[:, 2 * ctx:], ((0, 0), (lead, 0), (0, 0))),
    ], axis=1)
    valid_here = lax.dynamic_slice_in_dim(valid_counts, own * local_count, local_count)
    section_index = lax.axis_index("section")
    layer = functools.partial(encoder_layer, valid_counts=valid_here, sel=sel, state=state,
                              recv=recv, qkv_weight=qkv_weight[0], out_weight=out_weight[0],
                              conv_weight=conv_weight[0], ctx=ctx, kept_real=kept)
    on_first = section_index == 0
    frames = new_frames.shape[1]
    like = lambda shape, dtype: (lambda: jnp.zeros(shape, dtype))
    projected = lax.cond(on_first, lambda: project(new_frames, qkv_weight[0]),
                         like((3, local_count * frames, width), jnp.bfloat16))
    first = lax.cond(on_first, lambda: layer(new_frames, projected=projected),
                     like(new_frames.shape, new_frames.dtype))
    early = lax.cond(on_first, like(new_frames.shape, jnp.float32),
                     lambda: kept_conv(sel, state, recv, conv_weight[0], local_count, frames, ctx,
                                       kept))
    inbound = shifted(first, "section", 1)
    result = lax.cond(on_first, lambda: first, lambda: layer(inbound, conv_in=early))
    return result[None]


def solution(mesh):
    return jax.shard_map(
        body,
        mesh=mesh,
        in_specs=(
            P(("groups", "stream"), None, None),
            P("groups"),
            P("groups"),
            P("section", ("groups", "stream"), None, None),
            P("section", ("groups", "stream"), None, None),
            P("section", None, None),
            P("section", None, None),
            P("section", None, None),
        ),
        out_specs=P("section", ("groups", "stream"), None, None),
        check_vma=False,
    )
```

```python
import functools

import jax
import jax.numpy as jnp
from jax import lax
from jax.experimental import pallas as pl
from jax.experimental.pallas import tpu as pltpu
from jax.sharding import PartitionSpec as P

HEADS = 16
GROUP = 16
CHUNK_ROWS = 128


def shifted(value, axis, steps):
    count = lax.axis_size(axis)
    leading, last = (max(0, -steps), min(count, count - steps))
    return lax.ppermute(value, axis, [(source, source + steps) for source in range(leading, last)])


def projection_kernel(x_ref, w_ref, out_ref, nrm_ref, *, head_size):
    step = pl.program_id(0)

    @pl.when(step == 0)
    def _():
        floats = x_ref[...].astype(jnp.float32)
        centred = floats - jnp.mean(floats, axis=-1, keepdims=True)
        variance = jnp.mean(centred * centred, axis=-1, keepdims=True)
        nrm_ref[...] = (centred * lax.rsqrt(variance + 1e-05)).astype(jnp.bfloat16)

    part = jnp.dot(nrm_ref[...], w_ref[...], preferred_element_type=jnp.float32)
    scale = jnp.where(step == 0, head_size ** -0.5, 1.0).astype(jnp.float32)
    out_ref[0] = (part * scale).astype(out_ref.dtype)


def conv_rows(conv_ref, pad_ref, cw_ref, tap_rows, frames, origin):
    width = cw_ref.shape[1]
    chunk = 128

    def conv_chunk(c, carry):
        cols = pl.ds(pl.multiple_of(c * chunk, chunk), chunk)
        for lo in range(0, frames, 8):
            conv = conv_ref[:, pl.ds(lo, 8), cols]
            for j, rows in enumerate(tap_rows):
                if lo in rows:
                    conv = conv + cw_ref[pl.ds(j, 1), cols].reshape(1, 1, chunk) * pad_ref[
                        :, pl.ds(origin + j + lo, 8), cols]
            conv_ref[:, pl.ds(lo, 8), cols] = conv
        return carry

    lax.fori_loop(0, width // chunk, conv_chunk, 0)


def kept_taps(taps, kept, frames):
    return [[lo for lo in range(0, frames, 8) if lo < kept - j] for j in range(taps)]


def new_taps(taps, kept, frames):
    return [[lo for lo in range(0, frames, 8) if lo + 7 >= kept - j] for j in range(taps)]


def kept_conv_kernel(sel_ref, cw_ref, state_hbm, recv_hbm, out_ref, stv, pad_ref, gsem, *,
                     streams, frames, slot, kept):
    width = cw_ref.shape[1]
    rows = pad_ref.shape[1] - frames
    for j in range(streams):
        kind = sel_ref[j]
        idx = sel_ref[streams + j]

        @pl.when(kind == 0)
        def _():
            pltpu.make_async_copy(state_hbm.at[idx, pl.ds(2 * slot, rows)], stv.at[j],
                                  gsem.at[j]).start()

        @pl.when(kind != 0)
        def _():
            pltpu.make_async_copy(recv_hbm.at[idx, pl.ds(2 * slot, rows)], stv.at[j],
                                  gsem.at[j]).start()

    for j in range(streams):
        pltpu.make_async_copy(state_hbm.at[0, pl.ds(2 * slot, rows)], stv.at[j], gsem.at[j]).wait()
    pad_ref[:, 0:rows, :] = stv[...].astype(jnp.float32)
    pad_ref[:, rows:, :] = jnp.zeros((streams, frames, width), jnp.float32)
    out_ref[...] = jnp.zeros_like(out_ref)
    taps = cw_ref.shape[0]
    conv_rows(out_ref, pad_ref, cw_ref, kept_taps(taps, kept, frames), frames, rows - kept)


def kept_conv(sel, state, recv, conv_weight, streams, frames, ctx, kept):
    slot = -(-ctx // 16) * 16
    rows = state.shape[1] - 2 * slot
    width = state.shape[2]
    kernel = functools.partial(kept_conv_kernel, streams=streams, frames=frames, slot=slot,
                               kept=kept)
    vmem = pl.BlockSpec(memory_space=pltpu.VMEM)
    hbm = pl.BlockSpec(memory_space=pl.ANY)
    return pl.pallas_call(
        kernel,
        out_shape=jax.ShapeDtypeStruct((streams, frames, width), jnp.float32),
        in_specs=[pl.BlockSpec(memory_space=pltpu.SMEM), vmem, hbm, hbm],
        out_specs=vmem,
        scratch_shapes=[
            pltpu.VMEM((streams, rows, width), jnp.bfloat16),
            pltpu.VMEM((streams, rows + frames, width), jnp.float32),
            pltpu.SemaphoreType.DMA((streams,)),
        ],
    )(sel, conv_weight, state, recv)


def layer_kernel(sel_ref, x_ref, klive_ref, rlive_ref, cw_ref, qkv_hbm, wo_hbm, state_hbm,
                 recv_hbm, *rest, streams, frames, ctx, head_size, kept_real, early):
    if early:
        conv_in_ref, out_ref, wobuf, stv, qkv, conv_ref, pad_ref, res_ref, wsem, gsem = rest
    else:
        out_ref, wobuf, stv, qkv, conv_ref, pad_ref, res_ref, wsem, gsem = rest
    tokens = streams * frames
    width = x_ref.shape[1]
    slot = -(-ctx // 16) * 16
    kept = pad_ref.shape[1] - frames
    taps = cw_ref.shape[0]
    chunk = 128

    for j in range(streams):
        kind = sel_ref[j]
        idx = sel_ref[streams + j]

        @pl.when(kind == 0)
        def _():
            pltpu.make_async_copy(state_hbm.at[idx], stv.at[j], gsem.at[j]).start()

        @pl.when(kind != 0)
        def _():
            pltpu.make_async_copy(recv_hbm.at[idx], stv.at[j], gsem.at[j]).start()

    rows_w = wo_hbm.shape[0]
    copies = [pltpu.make_async_copy(qkv_hbm, qkv, wsem.at[0, 0])]
    for r in range(rows_w // CHUNK_ROWS):
        part = pl.ds(r * CHUNK_ROWS, CHUNK_ROWS)
        copies.append(pltpu.make_async_copy(wo_hbm.at[part], wobuf.at[part], wsem.at[1, r]))
    for c in copies:
        c.start()

    for j in range(streams):
        pltpu.make_async_copy(state_hbm.at[0], stv.at[j], gsem.at[j]).wait()

    copies[0].wait()

    rows_g = GROUP * frames
    cols_g = GROUP * slot
    q_stream = lax.broadcasted_iota(jnp.int32, (rows_g, cols_g), 0) // frames
    c_col = lax.broadcasted_iota(jnp.int32, (rows_g, cols_g), 1)
    bias_c = jnp.where((c_col // slot == q_stream) & (c_col % slot < ctx), 0.0, -1e30)
    k_stream = lax.broadcasted_iota(jnp.int32, (rows_g, rows_g), 1) // frames
    q_stream_n = lax.broadcasted_iota(jnp.int32, (rows_g, rows_g), 0) // frames
    same_n = q_stream_n == k_stream
    pair = 2 * head_size
    lane = lax.broadcasted_iota(jnp.int32, (rows_g, pair), 1)
    nt = (((1,), (1,)), ((), ()))
    for g in range(streams // GROUP):
        rows = pl.ds(g * rows_g, rows_g)
        srow = pl.ds(g * GROUP, GROUP)
        bias_n = jnp.where(same_n & (klive_ref[:, pl.ds(g * rows_g, rows_g)] > 0.0), 0.0, -1e30)

        def head_pair(p, carry):
            cols = pl.ds(pl.multiple_of(p * pair, pair), pair)
            q = qkv[0, rows, cols]
            k = qkv[1, rows, cols]
            v = qkv[2, rows, cols]
            ck = stv[srow, pl.ds(0, slot), cols].reshape(cols_g, pair)
            cv = stv[srow, pl.ds(slot, slot), cols].reshape(cols_g, pair)
            attended = None
            for half in range(pair // head_size):
                mine = (lane >= half * head_size) & (lane < (half + 1) * head_size)
                qh = jnp.where(mine, q, jnp.zeros_like(q))
                sc = lax.dot_general(qh, ck, nt, preferred_element_type=jnp.float32) + bias_c
                sn = lax.dot_general(qh, k, nt, preferred_element_type=jnp.float32) + bias_n
                top = jnp.maximum(jnp.max(sc, axis=-1, keepdims=True),
                                  jnp.max(sn, axis=-1, keepdims=True))
                ec = jnp.exp(sc - top)
                en = jnp.exp(sn - top)
                total = jnp.sum(ec, axis=-1, keepdims=True) + jnp.sum(en, axis=-1, keepdims=True)
                inv = 1.0 / total
                pc = (ec * inv).astype(jnp.bfloat16)
                pn = (en * inv).astype(jnp.bfloat16)
                oh = jnp.dot(pc, cv, preferred_element_type=jnp.float32) + jnp.dot(
                    pn, v, preferred_element_type=jnp.float32)
                attended = oh if attended is None else jnp.where(mine, oh, attended)
            qkv[0, rows, cols] = attended.astype(jnp.bfloat16)
            return carry

        lax.fori_loop(0, width // pair, head_pair, 0)

    for c in copies[1:]:
        c.wait()
    mixed = jnp.dot(qkv[0], wobuf[...], preferred_element_type=jnp.float32)
    residual = x_ref[...].astype(jnp.float32) + mixed
    res_ref[...] = residual
    rounded = residual.astype(jnp.bfloat16).astype(jnp.float32).reshape(streams, frames, width)
    origin = kept - kept_real
    if early:
        pad_ref[:, 0:kept, :] = jnp.zeros((streams, kept, width), jnp.float32)
        pad_ref[:, kept:, :] = rounded
        conv_ref[...] = conv_in_ref[...]
        conv_rows(conv_ref, pad_ref, cw_ref, new_taps(taps, kept_real, frames), frames, origin)
    else:
        pad_ref[:, 0:kept, :] = stv[:, pl.ds(2 * slot, kept), :].astype(jnp.float32)
        pad_ref[:, kept:, :] = rounded
        conv_ref[...] = jnp.zeros_like(conv_ref)
        every = [list(range(0, frames, 8))] * taps
        conv_rows(conv_ref, pad_ref, cw_ref, every, frames, origin)
    live = rlive_ref[...].reshape(streams, frames, 1)

    def finish(c, carry):
        cols = pl.ds(pl.multiple_of(c * chunk, chunk), chunk)
        conv = conv_ref[:, :, cols]
        res = res_ref[:, cols]
        silu = conv / (1.0 + jnp.exp(-conv))
        out = (res.reshape(streams, frames, chunk) + silu) * live
        out_ref[:, cols] = out.reshape(tokens, chunk).astype(out_ref.dtype)
        return carry

    lax.fori_loop(0, width // chunk, finish, 0)


def project(inputs, qkv_weight):
    streams, frames, width = inputs.shape
    tokens = streams * frames
    x = inputs.reshape(tokens, width)
    kernel = functools.partial(projection_kernel, head_size=width // HEADS)
    return pl.pallas_call(
        kernel,
        out_shape=jax.ShapeDtypeStruct((3, tokens, width), jnp.bfloat16),
        grid=(3,),
        in_specs=[pl.BlockSpec((tokens, width), lambda i: (0, 0)),
                  pl.BlockSpec((width, width), lambda i: (0, i))],
        out_specs=pl.BlockSpec((1, tokens, width), lambda i: (i, 0, 0)),
        scratch_shapes=[pltpu.VMEM((tokens, width), jnp.bfloat16)],
        compiler_params=pltpu.CompilerParams(dimension_semantics=("arbitrary",)),
    )(x, qkv_weight)


def encoder_layer(inputs, valid_counts, sel, state, recv, qkv_weight, out_weight, conv_weight,
                  ctx, kept_real, conv_in=None, projected=None):
    streams, frames, width = inputs.shape
    taps = conv_weight.shape[0]
    head_size = width // HEADS
    tokens = streams * frames
    slot = -(-ctx // 16) * 16
    live = (jnp.arange(frames, dtype=jnp.int32)[None, :] < valid_counts[:, None]).astype(jnp.float32)
    klive = live.reshape(1, tokens)
    rlive = live.reshape(tokens, 1)
    x = inputs.reshape(tokens, width)
    kept = state.shape[1] - 2 * slot
    early = conv_in is not None
    kernel = functools.partial(layer_kernel, streams=streams, frames=frames, ctx=ctx,
                               head_size=head_size, kept_real=kept_real, early=early)
    vmem = pl.BlockSpec(memory_space=pltpu.VMEM)
    hbm = pl.BlockSpec(memory_space=pl.ANY)
    extra = [conv_in] if early else []
    out = pl.pallas_call(
        kernel,
        out_shape=jax.ShapeDtypeStruct((tokens, width), jnp.bfloat16),
        in_specs=[pl.BlockSpec(memory_space=pltpu.SMEM), vmem, vmem, vmem, vmem,
                  hbm, hbm, hbm, hbm] + [vmem] * len(extra),
        out_specs=vmem,
        scratch_shapes=[
            pltpu.VMEM((width, width), jnp.bfloat16),
            pltpu.VMEM((streams,) + state.shape[1:], jnp.bfloat16),
            pltpu.VMEM((3, tokens, width), jnp.bfloat16),
            pltpu.VMEM((streams, frames, width), jnp.float32),
            pltpu.VMEM((streams, kept + frames, width), jnp.float32),
            pltpu.VMEM((tokens, width), jnp.float32),
            pltpu.SemaphoreType.DMA((2, width // CHUNK_ROWS)),
            pltpu.SemaphoreType.DMA((streams,)),
        ],
    )(sel, x, klive, rlive, conv_weight, project(inputs, qkv_weight) if projected is None else projected,
      out_weight, state, recv, *extra)
    return out.reshape(streams, frames, width)


def migrate(anchor, own, count, local_count, state):
    total = anchor.shape[0]
    every_slot = jnp.arange(total, dtype=jnp.int32)
    newpos = jnp.sum(jnp.where(anchor[None, :] == every_slot[:, None], every_slot[None, :], 0),
                     axis=1)
    mine_new = lax.dynamic_slice_in_dim(newpos, own * local_count, local_count)
    target = mine_new // local_count
    hosts = jnp.arange(count, dtype=jnp.int32)
    match = target[None, :] == hosts[:, None]
    send_slot = jnp.sum(jnp.where(match, jnp.arange(local_count, dtype=jnp.int32)[None, :], 0),
                        axis=1)
    send = jnp.take(state, jnp.clip(send_slot, 0, local_count - 1), axis=0)
    mine_old = lax.dynamic_slice_in_dim(anchor, own * local_count, local_count)
    source = mine_old // local_count
    staying = source == own
    local_idx = jnp.clip(mine_old - own * local_count, 0, local_count - 1)
    recv_idx = jnp.clip(source, 0, count - 1)
    sel = jnp.concatenate([jnp.where(staying, 0, 1), jnp.where(staying, local_idx, recv_idx)])
    return sel.astype(jnp.int32), send


def exchange(send):
    return lax.all_to_all(send, "stream", 0, 0, tiled=True)


def body(
    new_frames, valid_counts, anchor, context_cache, conv_state, qkv_weight, out_weight, conv_weight
):
    local_count = new_frames.shape[0]
    own = lax.axis_index("stream")
    count = lax.axis_size("stream")
    ctx = context_cache.shape[2]
    width = conv_state.shape[3]
    slot = -(-ctx // 16) * 16
    kept = conv_state.shape[2]
    lead = (-kept) % 16
    context = context_cache[0]
    state = jnp.concatenate([
        jnp.pad(context[:, :, :width], ((0, 0), (0, slot - ctx), (0, 0))),
        jnp.pad(context[:, :, width:], ((0, 0), (0, slot - ctx), (0, 0))),
        jnp.pad(conv_state[0], ((0, 0), (lead, 0), (0, 0))),
    ], axis=1)
    sel, send = migrate(anchor, own, count, local_count, state)
    valid_here = lax.dynamic_slice_in_dim(valid_counts, own * local_count, local_count)
    section_index = lax.axis_index("section")
    layer = functools.partial(encoder_layer, valid_counts=valid_here, sel=sel, state=state,
                              qkv_weight=qkv_weight[0], out_weight=out_weight[0],
                              conv_weight=conv_weight[0], ctx=ctx, kept_real=kept)
    on_first = section_index == 0
    frames = new_frames.shape[1]
    like = lambda shape, dtype: (lambda: jnp.zeros(shape, dtype))

    def early_branch():
        return exchange(send), project(new_frames, qkv_weight[0])

    recv0, projected = lax.cond(
        on_first, early_branch,
        lambda: (jnp.zeros_like(send), jnp.zeros((3, local_count * frames, width), jnp.bfloat16)))
    token = shifted(recv0[:1, :8], "section", 1)
    zero = jnp.where(on_first, 0.0, jnp.sum(token.astype(jnp.float32)) * 0.0)
    sel0 = sel + zero.astype(sel.dtype)
    first = lax.cond(on_first,
                     lambda: layer(new_frames, sel=sel0, recv=recv0, projected=projected),
                     like(new_frames.shape, new_frames.dtype))

    def late_branch():
        recv1 = exchange(send + zero.astype(send.dtype))
        return recv1, kept_conv(sel, state, recv1, conv_weight[0], local_count, frames, ctx, kept)

    recv1, early = lax.cond(on_first, lambda: (jnp.zeros_like(send),
                                               jnp.zeros(new_frames.shape, jnp.float32)),
                            late_branch)
    inbound = shifted(first, "section", 1)
    result = lax.cond(on_first, lambda: first,
                      lambda: layer(inbound, recv=recv1, conv_in=early))
    return result[None]


def solution(mesh):
    return jax.shard_map(
        body,
        mesh=mesh,
        in_specs=(
            P(("groups", "stream"), None, None),
            P("groups"),
            P("groups"),
            P("section", ("groups", "stream"), None, None),
            P("section", ("groups", "stream"), None, None),
            P("section", None, None),
            P("section", None, None),
            P("section", None, None),
        ),
        out_specs=P("section", ("groups", "stream"), None, None),
        check_vma=False,
    )
```

```python
import functools

import jax
import jax.numpy as jnp
from jax import lax
from jax.experimental import pallas as pl
from jax.experimental.pallas import tpu as pltpu
from jax.sharding import PartitionSpec as P

HEADS = 16
GROUP = 16
CHUNK_ROWS = 128


def shifted(value, axis, steps):
    count = lax.axis_size(axis)
    leading, last = (max(0, -steps), min(count, count - steps))
    return lax.ppermute(value, axis, [(source, source + steps) for source in range(leading, last)])


def projection_kernel(x_ref, w_ref, out_ref, nrm_ref, *, head_size):
    step = pl.program_id(0)

    @pl.when(step == 0)
    def _():
        floats = x_ref[...].astype(jnp.float32)
        centred = floats - jnp.mean(floats, axis=-1, keepdims=True)
        variance = jnp.mean(centred * centred, axis=-1, keepdims=True)
        nrm_ref[...] = (centred * lax.rsqrt(variance + 1e-05)).astype(jnp.bfloat16)

    part = jnp.dot(nrm_ref[...], w_ref[...], preferred_element_type=jnp.float32)
    scale = jnp.where(step == 0, head_size ** -0.5, 1.0).astype(jnp.float32)
    out_ref[0] = (part * scale).astype(out_ref.dtype)


def conv_rows(conv_ref, pad_ref, cw_ref, tap_rows, frames, origin):
    width = cw_ref.shape[1]
    chunk = 128

    def conv_chunk(c, carry):
        cols = pl.ds(pl.multiple_of(c * chunk, chunk), chunk)
        for lo in range(0, frames, 8):
            conv = conv_ref[:, pl.ds(lo, 8), cols]
            for j, rows in enumerate(tap_rows):
                if lo in rows:
                    conv = conv + cw_ref[pl.ds(j, 1), cols].reshape(1, 1, chunk) * pad_ref[
                        :, pl.ds(origin + j + lo, 8), cols]
            conv_ref[:, pl.ds(lo, 8), cols] = conv
        return carry

    lax.fori_loop(0, width // chunk, conv_chunk, 0)


def kept_taps(taps, kept, frames):
    return [[lo for lo in range(0, frames, 8) if lo < kept - j] for j in range(taps)]


def new_taps(taps, kept, frames):
    return [[lo for lo in range(0, frames, 8) if lo + 7 >= kept - j] for j in range(taps)]


def kept_conv_kernel(sel_ref, cw_ref, state_hbm, recv_hbm, out_ref, stv, pad_ref, gsem, *,
                     streams, frames, slot, kept):
    width = cw_ref.shape[1]
    rows = pad_ref.shape[1] - frames
    for j in range(streams):
        kind = sel_ref[j]
        idx = sel_ref[streams + j]

        @pl.when(kind == 0)
        def _():
            pltpu.make_async_copy(state_hbm.at[idx, pl.ds(2 * slot, rows)], stv.at[j],
                                  gsem.at[j]).start()

        @pl.when(kind != 0)
        def _():
            pltpu.make_async_copy(recv_hbm.at[idx, pl.ds(2 * slot, rows)], stv.at[j],
                                  gsem.at[j]).start()

    for j in range(streams):
        pltpu.make_async_copy(state_hbm.at[0, pl.ds(2 * slot, rows)], stv.at[j], gsem.at[j]).wait()
    pad_ref[:, 0:rows, :] = stv[...].astype(jnp.float32)
    pad_ref[:, rows:, :] = jnp.zeros((streams, frames, width), jnp.float32)
    out_ref[...] = jnp.zeros_like(out_ref)
    taps = cw_ref.shape[0]
    conv_rows(out_ref, pad_ref, cw_ref, kept_taps(taps, kept, frames), frames, rows - kept)


def kept_conv(sel, state, recv, conv_weight, streams, frames, ctx, kept):
    slot = -(-ctx // 16) * 16
    rows = state.shape[1] - 2 * slot
    width = state.shape[2]
    kernel = functools.partial(kept_conv_kernel, streams=streams, frames=frames, slot=slot,
                               kept=kept)
    vmem = pl.BlockSpec(memory_space=pltpu.VMEM)
    hbm = pl.BlockSpec(memory_space=pl.ANY)
    return pl.pallas_call(
        kernel,
        out_shape=jax.ShapeDtypeStruct((streams, frames, width), jnp.float32),
        in_specs=[pl.BlockSpec(memory_space=pltpu.SMEM), vmem, hbm, hbm],
        out_specs=vmem,
        scratch_shapes=[
            pltpu.VMEM((streams, rows, width), jnp.bfloat16),
            pltpu.VMEM((streams, rows + frames, width), jnp.float32),
            pltpu.SemaphoreType.DMA((streams,)),
        ],
    )(sel, conv_weight, state, recv)


def layer_kernel(sel_ref, x_ref, klive_ref, rlive_ref, cw_ref, qkv_hbm, wo_hbm, state_hbm,
                 recv_hbm, *rest, streams, frames, ctx, head_size, kept_real, early):
    if early:
        conv_in_ref, out_ref, wobuf, stv, qkv, conv_ref, pad_ref, res_ref, wsem, gsem = rest
    else:
        out_ref, wobuf, stv, qkv, conv_ref, pad_ref, res_ref, wsem, gsem = rest
    tokens = streams * frames
    width = x_ref.shape[1]
    slot = -(-ctx // 16) * 16
    kept = pad_ref.shape[1] - frames
    taps = cw_ref.shape[0]
    chunk = 128

    for j in range(streams):
        kind = sel_ref[j]
        idx = sel_ref[streams + j]

        @pl.when(kind == 0)
        def _():
            pltpu.make_async_copy(state_hbm.at[idx], stv.at[j], gsem.at[j]).start()

        @pl.when(kind != 0)
        def _():
            pltpu.make_async_copy(recv_hbm.at[idx], stv.at[j], gsem.at[j]).start()

    rows_w = wo_hbm.shape[0]
    copies = [pltpu.make_async_copy(qkv_hbm, qkv, wsem.at[0, 0])]
    for r in range(rows_w // CHUNK_ROWS):
        part = pl.ds(r * CHUNK_ROWS, CHUNK_ROWS)
        copies.append(pltpu.make_async_copy(wo_hbm.at[part], wobuf.at[part], wsem.at[1, r]))
    for c in copies:
        c.start()

    for j in range(streams):
        pltpu.make_async_copy(state_hbm.at[0], stv.at[j], gsem.at[j]).wait()

    copies[0].wait()

    rows_g = GROUP * frames
    cols_g = GROUP * slot
    q_stream = lax.broadcasted_iota(jnp.int32, (rows_g, cols_g), 0) // frames
    c_col = lax.broadcasted_iota(jnp.int32, (rows_g, cols_g), 1)
    bias_c = jnp.where((c_col // slot == q_stream) & (c_col % slot < ctx), 0.0, -1e30)
    k_stream = lax.broadcasted_iota(jnp.int32, (rows_g, rows_g), 1) // frames
    q_stream_n = lax.broadcasted_iota(jnp.int32, (rows_g, rows_g), 0) // frames
    same_n = q_stream_n == k_stream
    pair = 2 * head_size
    lane = lax.broadcasted_iota(jnp.int32, (rows_g, pair), 1)
    nt = (((1,), (1,)), ((), ()))
    for g in range(streams // GROUP):
        rows = pl.ds(g * rows_g, rows_g)
        srow = pl.ds(g * GROUP, GROUP)
        bias_n = jnp.where(same_n & (klive_ref[:, pl.ds(g * rows_g, rows_g)] > 0.0), 0.0, -1e30)

        def head_pair(p, carry):
            cols = pl.ds(pl.multiple_of(p * pair, pair), pair)
            q = qkv[0, rows, cols]
            k = qkv[1, rows, cols]
            v = qkv[2, rows, cols]
            ck = stv[srow, pl.ds(0, slot), cols].reshape(cols_g, pair)
            cv = stv[srow, pl.ds(slot, slot), cols].reshape(cols_g, pair)
            attended = None
            for half in range(pair // head_size):
                mine = (lane >= half * head_size) & (lane < (half + 1) * head_size)
                qh = jnp.where(mine, q, jnp.zeros_like(q))
                sc = lax.dot_general(qh, ck, nt, preferred_element_type=jnp.float32) + bias_c
                sn = lax.dot_general(qh, k, nt, preferred_element_type=jnp.float32) + bias_n
                top = jnp.maximum(jnp.max(sc, axis=-1, keepdims=True),
                                  jnp.max(sn, axis=-1, keepdims=True))
                ec = jnp.exp(sc - top)
                en = jnp.exp(sn - top)
                total = jnp.sum(ec, axis=-1, keepdims=True) + jnp.sum(en, axis=-1, keepdims=True)
                inv = 1.0 / total
                pc = (ec * inv).astype(jnp.bfloat16)
                pn = (en * inv).astype(jnp.bfloat16)
                oh = jnp.dot(pc, cv, preferred_element_type=jnp.float32) + jnp.dot(
                    pn, v, preferred_element_type=jnp.float32)
                attended = oh if attended is None else jnp.where(mine, oh, attended)
            qkv[0, rows, cols] = attended.astype(jnp.bfloat16)
            return carry

        lax.fori_loop(0, width // pair, head_pair, 0)

    for c in copies[1:]:
        c.wait()
    mixed = jnp.dot(qkv[0], wobuf[...], preferred_element_type=jnp.float32)
    residual = x_ref[...].astype(jnp.float32) + mixed
    res_ref[...] = residual
    rounded = residual.astype(jnp.bfloat16).astype(jnp.float32).reshape(streams, frames, width)
    origin = kept - kept_real
    if early:
        pad_ref[:, 0:kept, :] = jnp.zeros((streams, kept, width), jnp.float32)
        pad_ref[:, kept:, :] = rounded
        conv_ref[...] = conv_in_ref[...]
        conv_rows(conv_ref, pad_ref, cw_ref, new_taps(taps, kept_real, frames), frames, origin)
    else:
        pad_ref[:, 0:kept, :] = stv[:, pl.ds(2 * slot, kept), :].astype(jnp.float32)
        pad_ref[:, kept:, :] = rounded
        conv_ref[...] = jnp.zeros_like(conv_ref)
        every = [list(range(0, frames, 8))] * taps
        conv_rows(conv_ref, pad_ref, cw_ref, every, frames, origin)
    live = rlive_ref[...].reshape(streams, frames, 1)

    def finish(c, carry):
        cols = pl.ds(pl.multiple_of(c * chunk, chunk), chunk)
        conv = conv_ref[:, :, cols]
        res = res_ref[:, cols]
        silu = conv / (1.0 + jnp.exp(-conv))
        out = (res.reshape(streams, frames, chunk) + silu) * live
        out_ref[:, cols] = out.reshape(tokens, chunk).astype(out_ref.dtype)
        return carry

    lax.fori_loop(0, width // chunk, finish, 0)


def project(inputs, qkv_weight):
    streams, frames, width = inputs.shape
    tokens = streams * frames
    x = inputs.reshape(tokens, width)
    kernel = functools.partial(projection_kernel, head_size=width // HEADS)
    return pl.pallas_call(
        kernel,
        out_shape=jax.ShapeDtypeStruct((3, tokens, width), jnp.bfloat16),
        grid=(3,),
        in_specs=[pl.BlockSpec((tokens, width), lambda i: (0, 0)),
                  pl.BlockSpec((width, width), lambda i: (0, i))],
        out_specs=pl.BlockSpec((1, tokens, width), lambda i: (i, 0, 0)),
        scratch_shapes=[pltpu.VMEM((tokens, width), jnp.bfloat16)],
        compiler_params=pltpu.CompilerParams(dimension_semantics=("arbitrary",)),
    )(x, qkv_weight)


def encoder_layer(inputs, valid_counts, sel, state, recv, qkv_weight, out_weight, conv_weight,
                  ctx, kept_real, conv_in=None, projected=None):
    streams, frames, width = inputs.shape
    taps = conv_weight.shape[0]
    head_size = width // HEADS
    tokens = streams * frames
    slot = -(-ctx // 16) * 16
    live = (jnp.arange(frames, dtype=jnp.int32)[None, :] < valid_counts[:, None]).astype(jnp.float32)
    klive = live.reshape(1, tokens)
    rlive = live.reshape(tokens, 1)
    x = inputs.reshape(tokens, width)
    kept = state.shape[1] - 2 * slot
    early = conv_in is not None
    kernel = functools.partial(layer_kernel, streams=streams, frames=frames, ctx=ctx,
                               head_size=head_size, kept_real=kept_real, early=early)
    vmem = pl.BlockSpec(memory_space=pltpu.VMEM)
    hbm = pl.BlockSpec(memory_space=pl.ANY)
    extra = [conv_in] if early else []
    out = pl.pallas_call(
        kernel,
        out_shape=jax.ShapeDtypeStruct((tokens, width), jnp.bfloat16),
        in_specs=[pl.BlockSpec(memory_space=pltpu.SMEM), vmem, vmem, vmem, vmem,
                  hbm, hbm, hbm, hbm] + [vmem] * len(extra),
        out_specs=vmem,
        scratch_shapes=[
            pltpu.VMEM((width, width), jnp.bfloat16),
            pltpu.VMEM((streams,) + state.shape[1:], jnp.bfloat16),
            pltpu.VMEM((3, tokens, width), jnp.bfloat16),
            pltpu.VMEM((streams, frames, width), jnp.float32),
            pltpu.VMEM((streams, kept + frames, width), jnp.float32),
            pltpu.VMEM((tokens, width), jnp.float32),
            pltpu.SemaphoreType.DMA((2, width // CHUNK_ROWS)),
            pltpu.SemaphoreType.DMA((streams,)),
        ],
    )(sel, x, klive, rlive, conv_weight, project(inputs, qkv_weight) if projected is None else projected,
      out_weight, state, recv, *extra)
    return out.reshape(streams, frames, width)


def migrate(anchor, own, count, local_count, state):
    total = anchor.shape[0]
    every_slot = jnp.arange(total, dtype=jnp.int32)
    newpos = jnp.sum(jnp.where(anchor[None, :] == every_slot[:, None], every_slot[None, :], 0),
                     axis=1)
    mine_new = lax.dynamic_slice_in_dim(newpos, own * local_count, local_count)
    target = mine_new // local_count
    hosts = jnp.arange(count, dtype=jnp.int32)
    match = target[None, :] == hosts[:, None]
    send_slot = jnp.sum(jnp.where(match, jnp.arange(local_count, dtype=jnp.int32)[None, :], 0),
                        axis=1)
    send = jnp.take(state, jnp.clip(send_slot, 0, local_count - 1), axis=0, mode="clip")
    mine_old = lax.dynamic_slice_in_dim(anchor, own * local_count, local_count)
    source = mine_old // local_count
    staying = source == own
    local_idx = jnp.clip(mine_old - own * local_count, 0, local_count - 1)
    recv_idx = jnp.clip(source, 0, count - 1)
    sel = jnp.concatenate([jnp.where(staying, 0, 1), jnp.where(staying, local_idx, recv_idx)])
    return sel.astype(jnp.int32), send


def exchange(send):
    return lax.all_to_all(send, "stream", 0, 0, tiled=True)


def body(
    new_frames, valid_counts, anchor, context_cache, conv_state, qkv_weight, out_weight, conv_weight
):
    local_count = new_frames.shape[0]
    own = lax.axis_index("stream")
    count = lax.axis_size("stream")
    ctx = context_cache.shape[2]
    width = conv_state.shape[3]
    slot = -(-ctx // 16) * 16
    kept = conv_state.shape[2]
    lead = (-kept) % 16
    context = context_cache[0]
    state = jnp.concatenate([
        jnp.pad(context[:, :, :width], ((0, 0), (0, slot - ctx), (0, 0))),
        jnp.pad(context[:, :, width:], ((0, 0), (0, slot - ctx), (0, 0))),
        jnp.pad(conv_state[0], ((0, 0), (lead, 0), (0, 0))),
    ], axis=1)
    sel, send = migrate(anchor, own, count, local_count, state)
    valid_here = lax.dynamic_slice_in_dim(valid_counts, own * local_count, local_count)
    section_index = lax.axis_index("section")
    layer = functools.partial(encoder_layer, valid_counts=valid_here, sel=sel, state=state,
                              qkv_weight=qkv_weight[0], out_weight=out_weight[0],
                              conv_weight=conv_weight[0], ctx=ctx, kept_real=kept)
    on_first = section_index == 0
    frames = new_frames.shape[1]
    like = lambda shape, dtype: (lambda: jnp.zeros(shape, dtype))

    def early_branch():
        return exchange(send), project(new_frames, qkv_weight[0])

    recv0, projected = lax.cond(
        on_first, early_branch,
        lambda: (jnp.zeros_like(send), jnp.zeros((3, local_count * frames, width), jnp.bfloat16)))
    token = shifted(recv0[:1, :8], "section", 1)
    zero = jnp.where(on_first, 0.0, jnp.sum(token.astype(jnp.float32)) * 0.0)
    sel0 = sel + zero.astype(sel.dtype)
    first = lax.cond(on_first,
                     lambda: layer(new_frames, sel=sel0, recv=recv0, projected=projected),
                     like(new_frames.shape, new_frames.dtype))

    recv1 = lax.cond(on_first, lambda: jnp.zeros_like(send),
                     lambda: exchange(send + zero.astype(send.dtype)))
    inbound = shifted(first, "section", 1)
    result = lax.cond(on_first, lambda: first, lambda: layer(inbound, recv=recv1))
    return result[None]


def solution(mesh):
    return jax.shard_map(
        body,
        mesh=mesh,
        in_specs=(
            P(("groups", "stream"), None, None),
            P("groups"),
            P("groups"),
            P("section", ("groups", "stream"), None, None),
            P("section", ("groups", "stream"), None, None),
            P("section", None, None),
            P("section", None, None),
            P("section", None, None),
        ),
        out_specs=P("section", ("groups", "stream"), None, None),
        check_vma=False,
    )
```

```python
import functools

import jax
import jax.numpy as jnp
from jax import lax
from jax.experimental import pallas as pl
from jax.experimental.pallas import tpu as pltpu
from jax.sharding import PartitionSpec as P

HEADS = 16
GROUP = 16
CHUNK_ROWS = 128


def shifted(value, axis, steps):
    count = lax.axis_size(axis)
    leading, last = (max(0, -steps), min(count, count - steps))
    return lax.ppermute(value, axis, [(source, source + steps) for source in range(leading, last)])


def projection_kernel(x_ref, w_ref, out_ref, nrm_ref, *, head_size):
    step = pl.program_id(0)

    @pl.when(step == 0)
    def _():
        floats = x_ref[...].astype(jnp.float32)
        centred = floats - jnp.mean(floats, axis=-1, keepdims=True)
        variance = jnp.mean(centred * centred, axis=-1, keepdims=True)
        nrm_ref[...] = (centred * lax.rsqrt(variance + 1e-05)).astype(jnp.bfloat16)

    part = jnp.dot(nrm_ref[...], w_ref[...], preferred_element_type=jnp.float32)
    scale = jnp.where(step == 0, head_size ** -0.5, 1.0).astype(jnp.float32)
    out_ref[0] = (part * scale).astype(out_ref.dtype)


def conv_rows(conv_ref, pad_ref, cw_ref, tap_rows, frames, origin):
    width = cw_ref.shape[1]
    chunk = 128

    def conv_chunk(c, carry):
        cols = pl.ds(pl.multiple_of(c * chunk, chunk), chunk)
        for lo in range(0, frames, 8):
            conv = conv_ref[:, pl.ds(lo, 8), cols]
            for j, rows in enumerate(tap_rows):
                if lo in rows:
                    conv = conv + cw_ref[pl.ds(j, 1), cols].reshape(1, 1, chunk) * pad_ref[
                        :, pl.ds(origin + j + lo, 8), cols]
            conv_ref[:, pl.ds(lo, 8), cols] = conv
        return carry

    lax.fori_loop(0, width // chunk, conv_chunk, 0)


def kept_taps(taps, kept, frames):
    return [[lo for lo in range(0, frames, 8) if lo < kept - j] for j in range(taps)]


def new_taps(taps, kept, frames):
    return [[lo for lo in range(0, frames, 8) if lo + 7 >= kept - j] for j in range(taps)]


def kept_conv_kernel(sel_ref, cw_ref, state_hbm, recv_hbm, out_ref, stv, pad_ref, gsem, *,
                     streams, frames, slot, kept):
    width = cw_ref.shape[1]
    rows = pad_ref.shape[1] - frames
    for j in range(streams):
        kind = sel_ref[j]
        idx = sel_ref[streams + j]

        @pl.when(kind == 0)
        def _():
            pltpu.make_async_copy(state_hbm.at[idx, pl.ds(2 * slot, rows)], stv.at[j],
                                  gsem.at[j]).start()

        @pl.when(kind != 0)
        def _():
            pltpu.make_async_copy(recv_hbm.at[idx, pl.ds(2 * slot, rows)], stv.at[j],
                                  gsem.at[j]).start()

    for j in range(streams):
        pltpu.make_async_copy(state_hbm.at[0, pl.ds(2 * slot, rows)], stv.at[j], gsem.at[j]).wait()
    pad_ref[:, 0:rows, :] = stv[...].astype(jnp.float32)
    pad_ref[:, rows:, :] = jnp.zeros((streams, frames, width), jnp.float32)
    out_ref[...] = jnp.zeros_like(out_ref)
    taps = cw_ref.shape[0]
    conv_rows(out_ref, pad_ref, cw_ref, kept_taps(taps, kept, frames), frames, rows - kept)


def kept_conv(sel, state, recv, conv_weight, streams, frames, ctx, kept):
    slot = -(-ctx // 16) * 16
    rows = state.shape[1] - 2 * slot
    width = state.shape[2]
    kernel = functools.partial(kept_conv_kernel, streams=streams, frames=frames, slot=slot,
                               kept=kept)
    vmem = pl.BlockSpec(memory_space=pltpu.VMEM)
    hbm = pl.BlockSpec(memory_space=pl.ANY)
    return pl.pallas_call(
        kernel,
        out_shape=jax.ShapeDtypeStruct((streams, frames, width), jnp.float32),
        in_specs=[pl.BlockSpec(memory_space=pltpu.SMEM), vmem, hbm, hbm],
        out_specs=vmem,
        scratch_shapes=[
            pltpu.VMEM((streams, rows, width), jnp.bfloat16),
            pltpu.VMEM((streams, rows + frames, width), jnp.float32),
            pltpu.SemaphoreType.DMA((streams,)),
        ],
    )(sel, conv_weight, state, recv)


def layer_kernel(sel_ref, x_ref, klive_ref, rlive_ref, cw_ref, qkv_hbm, wo_hbm, state_hbm,
                 recv_hbm, *rest, streams, frames, ctx, head_size, kept_real, early):
    if early:
        conv_in_ref, out_ref, wobuf, stv, qkv, conv_ref, pad_ref, res_ref, wsem, gsem = rest
    else:
        out_ref, wobuf, stv, qkv, conv_ref, pad_ref, res_ref, wsem, gsem = rest
    tokens = streams * frames
    width = x_ref.shape[1]
    slot = -(-ctx // 16) * 16
    kept = pad_ref.shape[1] - frames
    taps = cw_ref.shape[0]
    chunk = 128

    for j in range(streams):
        kind = sel_ref[j]
        idx = sel_ref[streams + j]

        @pl.when(kind == 0)
        def _():
            pltpu.make_async_copy(state_hbm.at[idx], stv.at[j], gsem.at[j]).start()

        @pl.when(kind != 0)
        def _():
            pltpu.make_async_copy(recv_hbm.at[idx], stv.at[j], gsem.at[j]).start()

    rows_w = wo_hbm.shape[0]
    copies = [pltpu.make_async_copy(qkv_hbm, qkv, wsem.at[0, 0])]
    for r in range(rows_w // CHUNK_ROWS):
        part = pl.ds(r * CHUNK_ROWS, CHUNK_ROWS)
        copies.append(pltpu.make_async_copy(wo_hbm.at[part], wobuf.at[part], wsem.at[1, r]))
    for c in copies:
        c.start()

    for j in range(streams):
        pltpu.make_async_copy(state_hbm.at[0], stv.at[j], gsem.at[j]).wait()

    copies[0].wait()

    rows_g = GROUP * frames
    cols_g = GROUP * slot
    q_stream = lax.broadcasted_iota(jnp.int32, (rows_g, cols_g), 0) // frames
    c_col = lax.broadcasted_iota(jnp.int32, (rows_g, cols_g), 1)
    bias_c = jnp.where((c_col // slot == q_stream) & (c_col % slot < ctx), 0.0, -1e30)
    k_stream = lax.broadcasted_iota(jnp.int32, (rows_g, rows_g), 1) // frames
    q_stream_n = lax.broadcasted_iota(jnp.int32, (rows_g, rows_g), 0) // frames
    same_n = q_stream_n == k_stream
    pair = 2 * head_size
    lane = lax.broadcasted_iota(jnp.int32, (rows_g, pair), 1)
    nt = (((1,), (1,)), ((), ()))
    for g in range(streams // GROUP):
        rows = pl.ds(g * rows_g, rows_g)
        srow = pl.ds(g * GROUP, GROUP)
        bias_n = jnp.where(same_n & (klive_ref[:, pl.ds(g * rows_g, rows_g)] > 0.0), 0.0, -1e30)

        def head_pair(p, carry):
            cols = pl.ds(pl.multiple_of(p * pair, pair), pair)
            q = qkv[0, rows, cols]
            k = qkv[1, rows, cols]
            v = qkv[2, rows, cols]
            ck = stv[srow, pl.ds(0, slot), cols].reshape(cols_g, pair)
            cv = stv[srow, pl.ds(slot, slot), cols].reshape(cols_g, pair)
            attended = None
            for half in range(pair // head_size):
                mine = (lane >= half * head_size) & (lane < (half + 1) * head_size)
                qh = jnp.where(mine, q, jnp.zeros_like(q))
                sc = lax.dot_general(qh, ck, nt, preferred_element_type=jnp.float32) + bias_c
                sn = lax.dot_general(qh, k, nt, preferred_element_type=jnp.float32) + bias_n
                top = jnp.maximum(jnp.max(sc, axis=-1, keepdims=True),
                                  jnp.max(sn, axis=-1, keepdims=True))
                ec = jnp.exp(sc - top)
                en = jnp.exp(sn - top)
                total = jnp.sum(ec, axis=-1, keepdims=True) + jnp.sum(en, axis=-1, keepdims=True)
                pc = ec.astype(jnp.bfloat16)
                pn = en.astype(jnp.bfloat16)
                oh = (jnp.dot(pc, cv, preferred_element_type=jnp.float32) + jnp.dot(
                    pn, v, preferred_element_type=jnp.float32)) * (1.0 / total)
                attended = oh if attended is None else jnp.where(mine, oh, attended)
            qkv[0, rows, cols] = attended.astype(jnp.bfloat16)
            return carry

        lax.fori_loop(0, width // pair, head_pair, 0)

    for c in copies[1:]:
        c.wait()
    mixed = jnp.dot(qkv[0], wobuf[...], preferred_element_type=jnp.float32)
    residual = x_ref[...].astype(jnp.float32) + mixed
    res_ref[...] = residual
    rounded = residual.astype(jnp.bfloat16).astype(jnp.float32).reshape(streams, frames, width)
    origin = kept - kept_real
    if early:
        pad_ref[:, 0:kept, :] = jnp.zeros((streams, kept, width), jnp.float32)
        pad_ref[:, kept:, :] = rounded
        conv_ref[...] = conv_in_ref[...]
        conv_rows(conv_ref, pad_ref, cw_ref, new_taps(taps, kept_real, frames), frames, origin)
    else:
        pad_ref[:, 0:kept, :] = stv[:, pl.ds(2 * slot, kept), :].astype(jnp.float32)
        pad_ref[:, kept:, :] = rounded
        conv_ref[...] = jnp.zeros_like(conv_ref)
        every = [list(range(0, frames, 8))] * taps
        conv_rows(conv_ref, pad_ref, cw_ref, every, frames, origin)
    live = rlive_ref[...].reshape(streams, frames, 1)

    def finish(c, carry):
        cols = pl.ds(pl.multiple_of(c * chunk, chunk), chunk)
        conv = conv_ref[:, :, cols]
        res = res_ref[:, cols]
        silu = conv / (1.0 + jnp.exp(-conv))
        out = (res.reshape(streams, frames, chunk) + silu) * live
        out_ref[:, cols] = out.reshape(tokens, chunk).astype(out_ref.dtype)
        return carry

    lax.fori_loop(0, width // chunk, finish, 0)


def project(inputs, qkv_weight):
    streams, frames, width = inputs.shape
    tokens = streams * frames
    x = inputs.reshape(tokens, width)
    kernel = functools.partial(projection_kernel, head_size=width // HEADS)
    return pl.pallas_call(
        kernel,
        out_shape=jax.ShapeDtypeStruct((3, tokens, width), jnp.bfloat16),
        grid=(3,),
        in_specs=[pl.BlockSpec((tokens, width), lambda i: (0, 0)),
                  pl.BlockSpec((width, width), lambda i: (0, i))],
        out_specs=pl.BlockSpec((1, tokens, width), lambda i: (i, 0, 0)),
        scratch_shapes=[pltpu.VMEM((tokens, width), jnp.bfloat16)],
        compiler_params=pltpu.CompilerParams(dimension_semantics=("arbitrary",)),
    )(x, qkv_weight)


def encoder_layer(inputs, valid_counts, sel, state, recv, qkv_weight, out_weight, conv_weight,
                  ctx, kept_real, conv_in=None, projected=None):
    streams, frames, width = inputs.shape
    taps = conv_weight.shape[0]
    head_size = width // HEADS
    tokens = streams * frames
    slot = -(-ctx // 16) * 16
    live = (jnp.arange(frames, dtype=jnp.int32)[None, :] < valid_counts[:, None]).astype(jnp.float32)
    klive = live.reshape(1, tokens)
    rlive = live.reshape(tokens, 1)
    x = inputs.reshape(tokens, width)
    kept = state.shape[1] - 2 * slot
    early = conv_in is not None
    kernel = functools.partial(layer_kernel, streams=streams, frames=frames, ctx=ctx,
                               head_size=head_size, kept_real=kept_real, early=early)
    vmem = pl.BlockSpec(memory_space=pltpu.VMEM)
    hbm = pl.BlockSpec(memory_space=pl.ANY)
    extra = [conv_in] if early else []
    out = pl.pallas_call(
        kernel,
        out_shape=jax.ShapeDtypeStruct((tokens, width), jnp.bfloat16),
        in_specs=[pl.BlockSpec(memory_space=pltpu.SMEM), vmem, vmem, vmem, vmem,
                  hbm, hbm, hbm, hbm] + [vmem] * len(extra),
        out_specs=vmem,
        scratch_shapes=[
            pltpu.VMEM((width, width), jnp.bfloat16),
            pltpu.VMEM((streams,) + state.shape[1:], jnp.bfloat16),
            pltpu.VMEM((3, tokens, width), jnp.bfloat16),
            pltpu.VMEM((streams, frames, width), jnp.float32),
            pltpu.VMEM((streams, kept + frames, width), jnp.float32),
            pltpu.VMEM((tokens, width), jnp.float32),
            pltpu.SemaphoreType.DMA((2, width // CHUNK_ROWS)),
            pltpu.SemaphoreType.DMA((streams,)),
        ],
    )(sel, x, klive, rlive, conv_weight, project(inputs, qkv_weight) if projected is None else projected,
      out_weight, state, recv, *extra)
    return out.reshape(streams, frames, width)


def migrate(anchor, own, count, local_count, state):
    total = anchor.shape[0]
    every_slot = jnp.arange(total, dtype=jnp.int32)
    newpos = jnp.sum(jnp.where(anchor[None, :] == every_slot[:, None], every_slot[None, :], 0),
                     axis=1)
    mine_new = lax.dynamic_slice_in_dim(newpos, own * local_count, local_count)
    target = mine_new // local_count
    hosts = jnp.arange(count, dtype=jnp.int32)
    match = target[None, :] == hosts[:, None]
    send_slot = jnp.sum(jnp.where(match, jnp.arange(local_count, dtype=jnp.int32)[None, :], 0),
                        axis=1)
    send = jnp.take(state, jnp.clip(send_slot, 0, local_count - 1), axis=0, mode="clip")
    mine_old = lax.dynamic_slice_in_dim(anchor, own * local_count, local_count)
    source = mine_old // local_count
    staying = source == own
    local_idx = jnp.clip(mine_old - own * local_count, 0, local_count - 1)
    recv_idx = jnp.clip(source, 0, count - 1)
    sel = jnp.concatenate([jnp.where(staying, 0, 1), jnp.where(staying, local_idx, recv_idx)])
    return sel.astype(jnp.int32), send


def exchange(send):
    return lax.all_to_all(send, "stream", 0, 0, tiled=True)


def body(
    new_frames, valid_counts, anchor, context_cache, conv_state, qkv_weight, out_weight, conv_weight
):
    local_count = new_frames.shape[0]
    own = lax.axis_index("stream")
    count = lax.axis_size("stream")
    ctx = context_cache.shape[2]
    width = conv_state.shape[3]
    slot = -(-ctx // 16) * 16
    kept = conv_state.shape[2]
    lead = (-kept) % 16
    context = context_cache[0]
    state = jnp.concatenate([
        jnp.pad(context[:, :, :width], ((0, 0), (0, slot - ctx), (0, 0))),
        jnp.pad(context[:, :, width:], ((0, 0), (0, slot - ctx), (0, 0))),
        jnp.pad(conv_state[0], ((0, 0), (lead, 0), (0, 0))),
    ], axis=1)
    sel, send = migrate(anchor, own, count, local_count, state)
    valid_here = lax.dynamic_slice_in_dim(valid_counts, own * local_count, local_count)
    section_index = lax.axis_index("section")
    layer = functools.partial(encoder_layer, valid_counts=valid_here, sel=sel, state=state,
                              qkv_weight=qkv_weight[0], out_weight=out_weight[0],
                              conv_weight=conv_weight[0], ctx=ctx, kept_real=kept)
    on_first = section_index == 0
    frames = new_frames.shape[1]
    like = lambda shape, dtype: (lambda: jnp.zeros(shape, dtype))

    def early_branch():
        return exchange(send), project(new_frames, qkv_weight[0])

    recv0, projected = lax.cond(
        on_first, early_branch,
        lambda: (jnp.zeros_like(send), jnp.zeros((3, local_count * frames, width), jnp.bfloat16)))
    token = shifted(recv0[:1, :8], "section", 1)
    zero = jnp.where(on_first, 0.0, jnp.sum(token.astype(jnp.float32)) * 0.0)
    sel0 = sel + zero.astype(sel.dtype)
    first = lax.cond(on_first,
                     lambda: layer(new_frames, sel=sel0, recv=recv0, projected=projected),
                     like(new_frames.shape, new_frames.dtype))

    recv1 = lax.cond(on_first, lambda: jnp.zeros_like(send),
                     lambda: exchange(send + zero.astype(send.dtype)))
    inbound = shifted(first, "section", 1)
    result = lax.cond(on_first, lambda: first, lambda: layer(inbound, recv=recv1))
    return result[None]


def solution(mesh):
    return jax.shard_map(
        body,
        mesh=mesh,
        in_specs=(
            P(("groups", "stream"), None, None),
            P("groups"),
            P("groups"),
            P("section", ("groups", "stream"), None, None),
            P("section", ("groups", "stream"), None, None),
            P("section", None, None),
            P("section", None, None),
            P("section", None, None),
        ),
        out_specs=P("section", ("groups", "stream"), None, None),
        check_vma=False,
    )
```

```python
import functools

import jax
import jax.numpy as jnp
from jax import lax
from jax.experimental import pallas as pl
from jax.experimental.pallas import tpu as pltpu
from jax.sharding import PartitionSpec as P

HEADS = 16
GROUP = 16
CHUNK_ROWS = 128


def shifted(value, axis, steps):
    count = lax.axis_size(axis)
    leading, last = (max(0, -steps), min(count, count - steps))
    return lax.ppermute(value, axis, [(source, source + steps) for source in range(leading, last)])


def projection_kernel(x_ref, w_ref, out_ref, nrm_ref, *, head_size):
    step = pl.program_id(0)

    @pl.when(step == 0)
    def _():
        floats = x_ref[...].astype(jnp.float32)
        centred = floats - jnp.mean(floats, axis=-1, keepdims=True)
        variance = jnp.mean(centred * centred, axis=-1, keepdims=True)
        nrm_ref[...] = (centred * lax.rsqrt(variance + 1e-05)).astype(jnp.bfloat16)

    part = jnp.dot(nrm_ref[...], w_ref[...], preferred_element_type=jnp.float32)
    scale = jnp.where(step == 0, head_size ** -0.5, 1.0).astype(jnp.float32)
    out_ref[0] = (part * scale).astype(out_ref.dtype)


def conv_rows(conv_ref, pad_ref, cw_ref, tap_rows, frames, origin):
    width = cw_ref.shape[1]
    chunk = 128

    def conv_chunk(c, carry):
        cols = pl.ds(pl.multiple_of(c * chunk, chunk), chunk)
        for lo in range(0, frames, 8):
            conv = conv_ref[:, pl.ds(lo, 8), cols]
            for j, rows in enumerate(tap_rows):
                if lo in rows:
                    conv = conv + cw_ref[pl.ds(j, 1), cols].reshape(1, 1, chunk) * pad_ref[
                        :, pl.ds(origin + j + lo, 8), cols]
            conv_ref[:, pl.ds(lo, 8), cols] = conv
        return carry

    lax.fori_loop(0, width // chunk, conv_chunk, 0)


def kept_taps(taps, kept, frames):
    return [[lo for lo in range(0, frames, 8) if lo < kept - j] for j in range(taps)]


def new_taps(taps, kept, frames):
    return [[lo for lo in range(0, frames, 8) if lo + 7 >= kept - j] for j in range(taps)]


def kept_conv_kernel(sel_ref, cw_ref, state_hbm, recv_hbm, out_ref, stv, pad_ref, gsem, *,
                     streams, frames, slot, kept):
    width = cw_ref.shape[1]
    rows = pad_ref.shape[1] - frames
    for j in range(streams):
        kind = sel_ref[j]
        idx = sel_ref[streams + j]

        @pl.when(kind == 0)
        def _():
            pltpu.make_async_copy(state_hbm.at[idx, pl.ds(2 * slot, rows)], stv.at[j],
                                  gsem.at[j]).start()

        @pl.when(kind != 0)
        def _():
            pltpu.make_async_copy(recv_hbm.at[idx, pl.ds(2 * slot, rows)], stv.at[j],
                                  gsem.at[j]).start()

    for j in range(streams):
        pltpu.make_async_copy(state_hbm.at[0, pl.ds(2 * slot, rows)], stv.at[j], gsem.at[j]).wait()
    pad_ref[:, 0:rows, :] = stv[...].astype(jnp.float32)
    pad_ref[:, rows:, :] = jnp.zeros((streams, frames, width), jnp.float32)
    out_ref[...] = jnp.zeros_like(out_ref)
    taps = cw_ref.shape[0]
    conv_rows(out_ref, pad_ref, cw_ref, kept_taps(taps, kept, frames), frames, rows - kept)


def kept_conv(sel, state, recv, conv_weight, streams, frames, ctx, kept):
    slot = -(-ctx // 16) * 16
    rows = state.shape[1] - 2 * slot
    width = state.shape[2]
    kernel = functools.partial(kept_conv_kernel, streams=streams, frames=frames, slot=slot,
                               kept=kept)
    vmem = pl.BlockSpec(memory_space=pltpu.VMEM)
    hbm = pl.BlockSpec(memory_space=pl.ANY)
    return pl.pallas_call(
        kernel,
        out_shape=jax.ShapeDtypeStruct((streams, frames, width), jnp.float32),
        in_specs=[pl.BlockSpec(memory_space=pltpu.SMEM), vmem, hbm, hbm],
        out_specs=vmem,
        scratch_shapes=[
            pltpu.VMEM((streams, rows, width), jnp.bfloat16),
            pltpu.VMEM((streams, rows + frames, width), jnp.float32),
            pltpu.SemaphoreType.DMA((streams,)),
        ],
    )(sel, conv_weight, state, recv)


def layer_kernel(sel_ref, x_ref, klive_ref, rlive_ref, cw_ref, qkv_hbm, wo_hbm, state_hbm,
                 recv_hbm, *rest, streams, frames, ctx, head_size, kept_real, early):
    if early:
        conv_in_ref, out_ref, wobuf, stv, qkv, conv_ref, pad_ref, res_ref, wsem, gsem = rest
    else:
        out_ref, wobuf, stv, qkv, conv_ref, pad_ref, res_ref, wsem, gsem = rest
    tokens = streams * frames
    width = x_ref.shape[1]
    slot = -(-ctx // 16) * 16
    kept = pad_ref.shape[1] - frames
    taps = cw_ref.shape[0]
    chunk = 128

    keys_rows = pl.ds(0, 2 * slot)
    conv_part = pl.ds(2 * slot, stv.shape[1] - 2 * slot)

    def gather(part, which):
        for j in range(streams):
            kind = sel_ref[j]
            idx = sel_ref[streams + j]

            @pl.when(kind == 0)
            def _():
                pltpu.make_async_copy(state_hbm.at[idx, part], stv.at[j, part],
                                      gsem.at[which, j]).start()

            @pl.when(kind != 0)
            def _():
                pltpu.make_async_copy(recv_hbm.at[idx, part], stv.at[j, part],
                                      gsem.at[which, j]).start()

    def gather_wait(part, which):
        for j in range(streams):
            pltpu.make_async_copy(state_hbm.at[0, part], stv.at[j, part], gsem.at[which, j]).wait()

    rows_w = wo_hbm.shape[0]
    copies = [pltpu.make_async_copy(qkv_hbm, qkv, wsem.at[0, 0])]
    for r in range(rows_w // CHUNK_ROWS):
        part = pl.ds(r * CHUNK_ROWS, CHUNK_ROWS)
        copies.append(pltpu.make_async_copy(wo_hbm.at[part], wobuf.at[part], wsem.at[1, r]))
    copies[0].start()
    gather(keys_rows, 0)
    for c in copies[1:]:
        c.start()
    gather(conv_part, 1)

    copies[0].wait()
    gather_wait(keys_rows, 0)

    rows_g = GROUP * frames
    cols_g = GROUP * slot
    q_stream = lax.broadcasted_iota(jnp.int32, (rows_g, cols_g), 0) // frames
    c_col = lax.broadcasted_iota(jnp.int32, (rows_g, cols_g), 1)
    bias_c = jnp.where((c_col // slot == q_stream) & (c_col % slot < ctx), 0.0, -1e30)
    k_stream = lax.broadcasted_iota(jnp.int32, (rows_g, rows_g), 1) // frames
    q_stream_n = lax.broadcasted_iota(jnp.int32, (rows_g, rows_g), 0) // frames
    same_n = q_stream_n == k_stream
    pair = 2 * head_size
    lane = lax.broadcasted_iota(jnp.int32, (rows_g, pair), 1)
    nt = (((1,), (1,)), ((), ()))
    for g in range(streams // GROUP):
        rows = pl.ds(g * rows_g, rows_g)
        srow = pl.ds(g * GROUP, GROUP)
        bias_n = jnp.where(same_n & (klive_ref[:, pl.ds(g * rows_g, rows_g)] > 0.0), 0.0, -1e30)

        def head_pair(p, carry):
            cols = pl.ds(pl.multiple_of(p * pair, pair), pair)
            q = qkv[0, rows, cols]
            k = qkv[1, rows, cols]
            v = qkv[2, rows, cols]
            ck = stv[srow, pl.ds(0, slot), cols].reshape(cols_g, pair)
            cv = stv[srow, pl.ds(slot, slot), cols].reshape(cols_g, pair)
            attended = None
            for half in range(pair // head_size):
                mine = (lane >= half * head_size) & (lane < (half + 1) * head_size)
                qh = jnp.where(mine, q, jnp.zeros_like(q))
                sc = lax.dot_general(qh, ck, nt, preferred_element_type=jnp.float32) + bias_c
                sn = lax.dot_general(qh, k, nt, preferred_element_type=jnp.float32) + bias_n
                top = jnp.maximum(jnp.max(sc, axis=-1, keepdims=True),
                                  jnp.max(sn, axis=-1, keepdims=True))
                ec = jnp.exp(sc - top)
                en = jnp.exp(sn - top)
                total = jnp.sum(ec, axis=-1, keepdims=True) + jnp.sum(en, axis=-1, keepdims=True)
                pc = ec.astype(jnp.bfloat16)
                pn = en.astype(jnp.bfloat16)
                oh = (jnp.dot(pc, cv, preferred_element_type=jnp.float32) + jnp.dot(
                    pn, v, preferred_element_type=jnp.float32)) * (1.0 / total)
                attended = oh if attended is None else jnp.where(mine, oh, attended)
            qkv[0, rows, cols] = attended.astype(jnp.bfloat16)
            return carry

        lax.fori_loop(0, width // pair, head_pair, 0)

    for c in copies[1:]:
        c.wait()
    mixed = jnp.dot(qkv[0], wobuf[...], preferred_element_type=jnp.float32)
    residual = x_ref[...].astype(jnp.float32) + mixed
    res_ref[...] = residual
    rounded = residual.astype(jnp.bfloat16).astype(jnp.float32).reshape(streams, frames, width)
    gather_wait(conv_part, 1)
    origin = kept - kept_real
    if early:
        pad_ref[:, 0:kept, :] = jnp.zeros((streams, kept, width), jnp.float32)
        pad_ref[:, kept:, :] = rounded
        conv_ref[...] = conv_in_ref[...]
        conv_rows(conv_ref, pad_ref, cw_ref, new_taps(taps, kept_real, frames), frames, origin)
    else:
        pad_ref[:, 0:kept, :] = stv[:, pl.ds(2 * slot, kept), :].astype(jnp.float32)
        pad_ref[:, kept:, :] = rounded
        conv_ref[...] = jnp.zeros_like(conv_ref)
        every = [list(range(0, frames, 8))] * taps
        conv_rows(conv_ref, pad_ref, cw_ref, every, frames, origin)
    live = rlive_ref[...].reshape(streams, frames, 1)

    def finish(c, carry):
        cols = pl.ds(pl.multiple_of(c * chunk, chunk), chunk)
        conv = conv_ref[:, :, cols]
        res = res_ref[:, cols]
        silu = conv / (1.0 + jnp.exp(-conv))
        out = (res.reshape(streams, frames, chunk) + silu) * live
        out_ref[:, cols] = out.reshape(tokens, chunk).astype(out_ref.dtype)
        return carry

    lax.fori_loop(0, width // chunk, finish, 0)


def project(inputs, qkv_weight):
    streams, frames, width = inputs.shape
    tokens = streams * frames
    x = inputs.reshape(tokens, width)
    kernel = functools.partial(projection_kernel, head_size=width // HEADS)
    return pl.pallas_call(
        kernel,
        out_shape=jax.ShapeDtypeStruct((3, tokens, width), jnp.bfloat16),
        grid=(3,),
        in_specs=[pl.BlockSpec((tokens, width), lambda i: (0, 0)),
                  pl.BlockSpec((width, width), lambda i: (0, i))],
        out_specs=pl.BlockSpec((1, tokens, width), lambda i: (i, 0, 0)),
        scratch_shapes=[pltpu.VMEM((tokens, width), jnp.bfloat16)],
        compiler_params=pltpu.CompilerParams(dimension_semantics=("arbitrary",)),
    )(x, qkv_weight)


def encoder_layer(inputs, valid_counts, sel, state, recv, qkv_weight, out_weight, conv_weight,
                  ctx, kept_real, conv_in=None, projected=None):
    streams, frames, width = inputs.shape
    taps = conv_weight.shape[0]
    head_size = width // HEADS
    tokens = streams * frames
    slot = -(-ctx // 16) * 16
    live = (jnp.arange(frames, dtype=jnp.int32)[None, :] < valid_counts[:, None]).astype(jnp.float32)
    klive = live.reshape(1, tokens)
    rlive = live.reshape(tokens, 1)
    x = inputs.reshape(tokens, width)
    kept = state.shape[1] - 2 * slot
    early = conv_in is not None
    kernel = functools.partial(layer_kernel, streams=streams, frames=frames, ctx=ctx,
                               head_size=head_size, kept_real=kept_real, early=early)
    vmem = pl.BlockSpec(memory_space=pltpu.VMEM)
    hbm = pl.BlockSpec(memory_space=pl.ANY)
    extra = [conv_in] if early else []
    out = pl.pallas_call(
        kernel,
        out_shape=jax.ShapeDtypeStruct((tokens, width), jnp.bfloat16),
        in_specs=[pl.BlockSpec(memory_space=pltpu.SMEM), vmem, vmem, vmem, vmem,
                  hbm, hbm, hbm, hbm] + [vmem] * len(extra),
        out_specs=vmem,
        scratch_shapes=[
            pltpu.VMEM((width, width), jnp.bfloat16),
            pltpu.VMEM((streams,) + state.shape[1:], jnp.bfloat16),
            pltpu.VMEM((3, tokens, width), jnp.bfloat16),
            pltpu.VMEM((streams, frames, width), jnp.float32),
            pltpu.VMEM((streams, kept + frames, width), jnp.float32),
            pltpu.VMEM((tokens, width), jnp.float32),
            pltpu.SemaphoreType.DMA((2, width // CHUNK_ROWS)),
            pltpu.SemaphoreType.DMA((2, streams)),
        ],
    )(sel, x, klive, rlive, conv_weight, project(inputs, qkv_weight) if projected is None else projected,
      out_weight, state, recv, *extra)
    return out.reshape(streams, frames, width)


def migrate(anchor, own, count, local_count, state):
    total = anchor.shape[0]
    every_slot = jnp.arange(total, dtype=jnp.int32)
    newpos = jnp.sum(jnp.where(anchor[None, :] == every_slot[:, None], every_slot[None, :], 0),
                     axis=1)
    mine_new = lax.dynamic_slice_in_dim(newpos, own * local_count, local_count)
    target = mine_new // local_count
    hosts = jnp.arange(count, dtype=jnp.int32)
    match = target[None, :] == hosts[:, None]
    send_slot = jnp.sum(jnp.where(match, jnp.arange(local_count, dtype=jnp.int32)[None, :], 0),
                        axis=1)
    send = jnp.take(state, jnp.clip(send_slot, 0, local_count - 1), axis=0, mode="clip")
    mine_old = lax.dynamic_slice_in_dim(anchor, own * local_count, local_count)
    source = mine_old // local_count
    staying = source == own
    local_idx = jnp.clip(mine_old - own * local_count, 0, local_count - 1)
    recv_idx = jnp.clip(source, 0, count - 1)
    sel = jnp.concatenate([jnp.where(staying, 0, 1), jnp.where(staying, local_idx, recv_idx)])
    return sel.astype(jnp.int32), send


def exchange(send):
    return lax.all_to_all(send, "stream", 0, 0, tiled=True)


def body(
    new_frames, valid_counts, anchor, context_cache, conv_state, qkv_weight, out_weight, conv_weight
):
    local_count = new_frames.shape[0]
    own = lax.axis_index("stream")
    count = lax.axis_size("stream")
    ctx = context_cache.shape[2]
    width = conv_state.shape[3]
    slot = -(-ctx // 16) * 16
    kept = conv_state.shape[2]
    lead = (-kept) % 16
    context = context_cache[0]
    state = jnp.concatenate([
        jnp.pad(context[:, :, :width], ((0, 0), (0, slot - ctx), (0, 0))),
        jnp.pad(context[:, :, width:], ((0, 0), (0, slot - ctx), (0, 0))),
        jnp.pad(conv_state[0], ((0, 0), (lead, 0), (0, 0))),
    ], axis=1)
    sel, send = migrate(anchor, own, count, local_count, state)
    valid_here = lax.dynamic_slice_in_dim(valid_counts, own * local_count, local_count)
    section_index = lax.axis_index("section")
    layer = functools.partial(encoder_layer, valid_counts=valid_here, sel=sel, state=state,
                              qkv_weight=qkv_weight[0], out_weight=out_weight[0],
                              conv_weight=conv_weight[0], ctx=ctx, kept_real=kept)
    on_first = section_index == 0
    frames = new_frames.shape[1]
    like = lambda shape, dtype: (lambda: jnp.zeros(shape, dtype))

    def early_branch():
        return exchange(send), project(new_frames, qkv_weight[0])

    recv0, projected = lax.cond(
        on_first, early_branch,
        lambda: (jnp.zeros_like(send), jnp.zeros((3, local_count * frames, width), jnp.bfloat16)))
    token = shifted(recv0[:1, :8], "section", 1)
    zero = jnp.where(on_first, 0.0, jnp.sum(token.astype(jnp.float32)) * 0.0)
    sel0 = sel + zero.astype(sel.dtype)
    first = lax.cond(on_first,
                     lambda: layer(new_frames, sel=sel0, recv=recv0, projected=projected),
                     like(new_frames.shape, new_frames.dtype))

    recv1 = lax.cond(on_first, lambda: jnp.zeros_like(send),
                     lambda: exchange(send + zero.astype(send.dtype)))
    inbound = shifted(first, "section", 1)
    result = lax.cond(on_first, lambda: first, lambda: layer(inbound, recv=recv1))
    return result[None]


def solution(mesh):
    return jax.shard_map(
        body,
        mesh=mesh,
        in_specs=(
            P(("groups", "stream"), None, None),
            P("groups"),
            P("groups"),
            P("section", ("groups", "stream"), None, None),
            P("section", ("groups", "stream"), None, None),
            P("section", None, None),
            P("section", None, None),
            P("section", None, None),
        ),
        out_specs=P("section", ("groups", "stream"), None, None),
        check_vma=False,
    )
```

```python
import functools

import jax
import jax.numpy as jnp
from jax import lax
from jax.experimental import pallas as pl
from jax.experimental.pallas import tpu as pltpu
from jax.sharding import PartitionSpec as P

HEADS = 16
GROUP = 16
CHUNK_ROWS = 128


def shifted(value, axis, steps):
    count = lax.axis_size(axis)
    leading, last = (max(0, -steps), min(count, count - steps))
    return lax.ppermute(value, axis, [(source, source + steps) for source in range(leading, last)])


def projection_kernel(x_ref, w_ref, out_ref, nrm_ref, *, head_size):
    step = pl.program_id(0)

    @pl.when(step == 0)
    def _():
        floats = x_ref[...].astype(jnp.float32)
        centred = floats - jnp.mean(floats, axis=-1, keepdims=True)
        variance = jnp.mean(centred * centred, axis=-1, keepdims=True)
        nrm_ref[...] = (centred * lax.rsqrt(variance + 1e-05)).astype(jnp.bfloat16)

    part = jnp.dot(nrm_ref[...], w_ref[...], preferred_element_type=jnp.float32)
    scale = jnp.where(step == 0, head_size ** -0.5, 1.0).astype(jnp.float32)
    out_ref[0] = (part * scale).astype(out_ref.dtype)


def conv_rows(conv_ref, pad_ref, cw_ref, tap_rows, frames, origin):
    width = cw_ref.shape[1]
    chunk = 128

    def conv_chunk(c, carry):
        cols = pl.ds(pl.multiple_of(c * chunk, chunk), chunk)
        for lo in range(0, frames, 8):
            conv = conv_ref[:, pl.ds(lo, 8), cols]
            for j, rows in enumerate(tap_rows):
                if lo in rows:
                    conv = conv + cw_ref[pl.ds(j, 1), cols].reshape(1, 1, chunk) * pad_ref[
                        :, pl.ds(origin + j + lo, 8), cols]
            conv_ref[:, pl.ds(lo, 8), cols] = conv
        return carry

    lax.fori_loop(0, width // chunk, conv_chunk, 0)


def kept_taps(taps, kept, frames):
    return [[lo for lo in range(0, frames, 8) if lo < kept - j] for j in range(taps)]


def new_taps(taps, kept, frames):
    return [[lo for lo in range(0, frames, 8) if lo + 7 >= kept - j] for j in range(taps)]


def kept_conv_kernel(sel_ref, cw_ref, state_hbm, recv_hbm, out_ref, stv, pad_ref, gsem, *,
                     streams, frames, slot, kept):
    width = cw_ref.shape[1]
    rows = pad_ref.shape[1] - frames
    for j in range(streams):
        kind = sel_ref[j]
        idx = sel_ref[streams + j]

        @pl.when(kind == 0)
        def _():
            pltpu.make_async_copy(state_hbm.at[idx, pl.ds(2 * slot, rows)], stv.at[j],
                                  gsem.at[j]).start()

        @pl.when(kind != 0)
        def _():
            pltpu.make_async_copy(recv_hbm.at[idx, pl.ds(2 * slot, rows)], stv.at[j],
                                  gsem.at[j]).start()

    for j in range(streams):
        pltpu.make_async_copy(state_hbm.at[0, pl.ds(2 * slot, rows)], stv.at[j], gsem.at[j]).wait()
    pad_ref[:, 0:rows, :] = stv[...].astype(jnp.float32)
    pad_ref[:, rows:, :] = jnp.zeros((streams, frames, width), jnp.float32)
    out_ref[...] = jnp.zeros_like(out_ref)
    taps = cw_ref.shape[0]
    conv_rows(out_ref, pad_ref, cw_ref, kept_taps(taps, kept, frames), frames, rows - kept)


def kept_conv(sel, state, recv, conv_weight, streams, frames, ctx, kept):
    slot = -(-ctx // 16) * 16
    rows = state.shape[1] - 2 * slot
    width = state.shape[2]
    kernel = functools.partial(kept_conv_kernel, streams=streams, frames=frames, slot=slot,
                               kept=kept)
    vmem = pl.BlockSpec(memory_space=pltpu.VMEM)
    hbm = pl.BlockSpec(memory_space=pl.ANY)
    return pl.pallas_call(
        kernel,
        out_shape=jax.ShapeDtypeStruct((streams, frames, width), jnp.float32),
        in_specs=[pl.BlockSpec(memory_space=pltpu.SMEM), vmem, hbm, hbm],
        out_specs=vmem,
        scratch_shapes=[
            pltpu.VMEM((streams, rows, width), jnp.bfloat16),
            pltpu.VMEM((streams, rows + frames, width), jnp.float32),
            pltpu.SemaphoreType.DMA((streams,)),
        ],
    )(sel, conv_weight, state, recv)


def layer_kernel(sel_ref, x_ref, klive_ref, rlive_ref, cw_ref, qkv_hbm, wo_hbm, state_hbm,
                 recv_hbm, *rest, streams, frames, ctx, head_size, kept_real, early):
    if early:
        conv_in_ref, out_ref, wobuf, stv, qkv, conv_ref, pad_ref, res_ref, wsem, gsem = rest
    else:
        out_ref, wobuf, stv, qkv, conv_ref, pad_ref, res_ref, wsem, gsem = rest
    tokens = streams * frames
    width = x_ref.shape[1]
    slot = -(-ctx // 16) * 16
    kept = pad_ref.shape[1] - frames
    taps = cw_ref.shape[0]
    chunk = 128

    keys_rows = pl.ds(0, 2 * slot)
    conv_part = pl.ds(2 * slot, stv.shape[1] - 2 * slot)

    def gather(part, which):
        for j in range(streams):
            kind = sel_ref[j]
            idx = sel_ref[streams + j]

            @pl.when(kind == 0)
            def _():
                pltpu.make_async_copy(state_hbm.at[idx, part], stv.at[j, part],
                                      gsem.at[which, j]).start()

            @pl.when(kind != 0)
            def _():
                pltpu.make_async_copy(recv_hbm.at[idx, part], stv.at[j, part],
                                      gsem.at[which, j]).start()

    def gather_wait(part, which):
        for j in range(streams):
            pltpu.make_async_copy(state_hbm.at[0, part], stv.at[j, part], gsem.at[which, j]).wait()

    rows_w = wo_hbm.shape[0]
    copies = [pltpu.make_async_copy(qkv_hbm, qkv, wsem.at[0, 0])]
    for r in range(rows_w // CHUNK_ROWS):
        part = pl.ds(r * CHUNK_ROWS, CHUNK_ROWS)
        copies.append(pltpu.make_async_copy(wo_hbm.at[part], wobuf.at[part], wsem.at[1, r]))
    copies[0].start()
    gather(keys_rows, 0)
    for c in copies[1:]:
        c.start()
    gather(conv_part, 1)

    copies[0].wait()
    gather_wait(keys_rows, 0)

    rows_g = GROUP * frames
    cols_g = GROUP * slot
    q_stream = lax.broadcasted_iota(jnp.int32, (rows_g, cols_g), 0) // frames
    c_col = lax.broadcasted_iota(jnp.int32, (rows_g, cols_g), 1)
    bias_c = jnp.where((c_col // slot == q_stream) & (c_col % slot < ctx), 0.0, -1e30)
    k_stream = lax.broadcasted_iota(jnp.int32, (rows_g, rows_g), 1) // frames
    q_stream_n = lax.broadcasted_iota(jnp.int32, (rows_g, rows_g), 0) // frames
    same_n = q_stream_n == k_stream
    pair = 2 * head_size
    lane = lax.broadcasted_iota(jnp.int32, (rows_g, pair), 1)
    nt = (((1,), (1,)), ((), ()))
    for g in range(streams // GROUP):
        rows = pl.ds(g * rows_g, rows_g)
        srow = pl.ds(g * GROUP, GROUP)
        bias_n = jnp.where(same_n & (klive_ref[:, pl.ds(g * rows_g, rows_g)] > 0.0), 0.0, -1e30)

        def head_pair(p, carry):
            cols = pl.ds(pl.multiple_of(p * pair, pair), pair)
            q = qkv[0, rows, cols]
            k = qkv[1, rows, cols]
            v = qkv[2, rows, cols]
            ck = stv[srow, pl.ds(0, slot), cols].reshape(cols_g, pair)
            cv = stv[srow, pl.ds(slot, slot), cols].reshape(cols_g, pair)
            attended = None
            for half in range(pair // head_size):
                mine = (lane >= half * head_size) & (lane < (half + 1) * head_size)
                qh = jnp.where(mine, q, jnp.zeros_like(q))
                sc = lax.dot_general(qh, ck, nt, preferred_element_type=jnp.float32) + bias_c
                sn = lax.dot_general(qh, k, nt, preferred_element_type=jnp.float32) + bias_n
                top = jnp.maximum(jnp.max(sc, axis=-1, keepdims=True),
                                  jnp.max(sn, axis=-1, keepdims=True))
                ec = jnp.exp(sc - top)
                en = jnp.exp(sn - top)
                total = jnp.sum(ec, axis=-1, keepdims=True) + jnp.sum(en, axis=-1, keepdims=True)
                pc = ec.astype(jnp.bfloat16)
                pn = en.astype(jnp.bfloat16)
                oh = (jnp.dot(pc, cv, preferred_element_type=jnp.float32) + jnp.dot(
                    pn, v, preferred_element_type=jnp.float32)) * (1.0 / total)
                attended = oh if attended is None else jnp.where(mine, oh, attended)
            qkv[0, rows, cols] = attended.astype(jnp.bfloat16)
            return carry

        lax.fori_loop(0, width // pair, head_pair, 0)

    for c in copies[1:]:
        c.wait()
    mixed = jnp.dot(qkv[0], wobuf[...], preferred_element_type=jnp.float32)
    residual = x_ref[...].astype(jnp.float32) + mixed
    res_ref[...] = residual
    rounded = residual.astype(jnp.bfloat16).astype(jnp.float32).reshape(streams, frames, width)
    gather_wait(conv_part, 1)
    origin = kept - kept_real
    if early:
        pad_ref[:, 0:kept, :] = jnp.zeros((streams, kept, width), jnp.float32)
        pad_ref[:, kept:, :] = rounded
        conv_ref[...] = conv_in_ref[...]
        conv_rows(conv_ref, pad_ref, cw_ref, new_taps(taps, kept_real, frames), frames, origin)
    else:
        pad_ref[:, 0:kept, :] = stv[:, pl.ds(2 * slot, kept), :].astype(jnp.float32)
        pad_ref[:, kept:, :] = rounded
        conv_ref[...] = jnp.zeros_like(conv_ref)
        every = [list(range(0, frames, 8))] * taps
        conv_rows(conv_ref, pad_ref, cw_ref, every, frames, origin)
    live = rlive_ref[...].reshape(streams, frames, 1)

    def finish(c, carry):
        cols = pl.ds(pl.multiple_of(c * chunk, chunk), chunk)
        conv = conv_ref[:, :, cols]
        res = res_ref[:, cols]
        silu = conv / (1.0 + jnp.exp(-conv))
        out = (res.reshape(streams, frames, chunk) + silu) * live
        out_ref[:, cols] = out.reshape(tokens, chunk).astype(out_ref.dtype)
        return carry

    lax.fori_loop(0, width // chunk, finish, 0)


def project(inputs, qkv_weight):
    streams, frames, width = inputs.shape
    tokens = streams * frames
    x = inputs.reshape(tokens, width)
    kernel = functools.partial(projection_kernel, head_size=width // HEADS)
    return pl.pallas_call(
        kernel,
        out_shape=jax.ShapeDtypeStruct((3, tokens, width), jnp.bfloat16),
        grid=(3,),
        in_specs=[pl.BlockSpec((tokens, width), lambda i: (0, 0)),
                  pl.BlockSpec((width, width), lambda i: (0, i))],
        out_specs=pl.BlockSpec((1, tokens, width), lambda i: (i, 0, 0)),
        scratch_shapes=[pltpu.VMEM((tokens, width), jnp.bfloat16)],
        compiler_params=pltpu.CompilerParams(dimension_semantics=("arbitrary",)),
    )(x, qkv_weight)


def encoder_layer(inputs, valid_counts, sel, state, recv, qkv_weight, out_weight, conv_weight,
                  ctx, kept_real, conv_in=None, projected=None):
    streams, frames, width = inputs.shape
    taps = conv_weight.shape[0]
    head_size = width // HEADS
    tokens = streams * frames
    slot = -(-ctx // 16) * 16
    live = (jnp.arange(frames, dtype=jnp.int32)[None, :] < valid_counts[:, None]).astype(jnp.float32)
    klive = live.reshape(1, tokens)
    rlive = live.reshape(tokens, 1)
    x = inputs.reshape(tokens, width)
    kept = state.shape[1] - 2 * slot
    early = conv_in is not None
    kernel = functools.partial(layer_kernel, streams=streams, frames=frames, ctx=ctx,
                               head_size=head_size, kept_real=kept_real, early=early)
    vmem = pl.BlockSpec(memory_space=pltpu.VMEM)
    hbm = pl.BlockSpec(memory_space=pl.ANY)
    extra = [conv_in] if early else []
    out = pl.pallas_call(
        kernel,
        out_shape=jax.ShapeDtypeStruct((tokens, width), jnp.bfloat16),
        in_specs=[pl.BlockSpec(memory_space=pltpu.SMEM), vmem, vmem, vmem, vmem,
                  hbm, hbm, hbm, hbm] + [vmem] * len(extra),
        out_specs=vmem,
        scratch_shapes=[
            pltpu.VMEM((width, width), jnp.bfloat16),
            pltpu.VMEM((streams,) + state.shape[1:], jnp.bfloat16),
            pltpu.VMEM((3, tokens, width), jnp.bfloat16),
            pltpu.VMEM((streams, frames, width), jnp.float32),
            pltpu.VMEM((streams, kept + frames, width), jnp.float32),
            pltpu.VMEM((tokens, width), jnp.float32),
            pltpu.SemaphoreType.DMA((2, width // CHUNK_ROWS)),
            pltpu.SemaphoreType.DMA((2, streams)),
        ],
    )(sel, x, klive, rlive, conv_weight, project(inputs, qkv_weight) if projected is None else projected,
      out_weight, state, recv, *extra)
    return out.reshape(streams, frames, width)


def migrate(anchor, own, count, local_count, build):
    total = anchor.shape[0]
    every_slot = jnp.arange(total, dtype=jnp.int32)
    newpos = jnp.sum(jnp.where(anchor[None, :] == every_slot[:, None], every_slot[None, :], 0),
                     axis=1)
    mine_new = lax.dynamic_slice_in_dim(newpos, own * local_count, local_count)
    target = mine_new // local_count
    hosts = jnp.arange(count, dtype=jnp.int32)
    match = target[None, :] == hosts[:, None]
    send_slot = jnp.sum(jnp.where(match, jnp.arange(local_count, dtype=jnp.int32)[None, :], 0),
                        axis=1)
    send = build(jnp.clip(send_slot, 0, local_count - 1))
    mine_old = lax.dynamic_slice_in_dim(anchor, own * local_count, local_count)
    source = mine_old // local_count
    staying = source == own
    local_idx = jnp.clip(mine_old - own * local_count, 0, local_count - 1)
    recv_idx = jnp.clip(source, 0, count - 1)
    sel = jnp.concatenate([jnp.where(staying, 0, 1), jnp.where(staying, local_idx, recv_idx)])
    return sel.astype(jnp.int32), send


def exchange(send):
    return lax.all_to_all(send, "stream", 0, 0, tiled=True)


def body(
    new_frames, valid_counts, anchor, context_cache, conv_state, qkv_weight, out_weight, conv_weight
):
    local_count = new_frames.shape[0]
    own = lax.axis_index("stream")
    count = lax.axis_size("stream")
    ctx = context_cache.shape[2]
    width = conv_state.shape[3]
    slot = -(-ctx // 16) * 16
    kept = conv_state.shape[2]
    lead = (-kept) % 16
    context = context_cache[0]
    def slab(context, conv):
        return jnp.concatenate([
            jnp.pad(context[:, :, :width], ((0, 0), (0, slot - ctx), (0, 0))),
            jnp.pad(context[:, :, width:], ((0, 0), (0, slot - ctx), (0, 0))),
            jnp.pad(conv, ((0, 0), (lead, 0), (0, 0))),
        ], axis=1)

    state = slab(context, conv_state[0])
    build = lambda rows: slab(jnp.take(context, rows, axis=0, mode="clip"),
                              jnp.take(conv_state[0], rows, axis=0, mode="clip"))
    sel, send = migrate(anchor, own, count, local_count, build)
    valid_here = lax.dynamic_slice_in_dim(valid_counts, own * local_count, local_count)
    section_index = lax.axis_index("section")
    layer = functools.partial(encoder_layer, valid_counts=valid_here, sel=sel, state=state,
                              qkv_weight=qkv_weight[0], out_weight=out_weight[0],
                              conv_weight=conv_weight[0], ctx=ctx, kept_real=kept)
    on_first = section_index == 0
    frames = new_frames.shape[1]
    like = lambda shape, dtype: (lambda: jnp.zeros(shape, dtype))

    def early_branch():
        return exchange(send), project(new_frames, qkv_weight[0])

    recv0, projected = lax.cond(
        on_first, early_branch,
        lambda: (jnp.zeros_like(send), jnp.zeros((3, local_count * frames, width), jnp.bfloat16)))
    token = shifted(recv0[:1, :8], "section", 1)
    zero = jnp.where(on_first, 0.0, jnp.sum(token.astype(jnp.float32)) * 0.0)
    sel0 = sel + zero.astype(sel.dtype)
    first = lax.cond(on_first,
                     lambda: layer(new_frames, sel=sel0, recv=recv0, projected=projected),
                     like(new_frames.shape, new_frames.dtype))

    recv1 = lax.cond(on_first, lambda: jnp.zeros_like(send),
                     lambda: exchange(send + zero.astype(send.dtype)))
    inbound = shifted(first, "section", 1)
    result = lax.cond(on_first, lambda: first, lambda: layer(inbound, recv=recv1))
    return result[None]


def solution(mesh):
    return jax.shard_map(
        body,
        mesh=mesh,
        in_specs=(
            P(("groups", "stream"), None, None),
            P("groups"),
            P("groups"),
            P("section", ("groups", "stream"), None, None),
            P("section", ("groups", "stream"), None, None),
            P("section", None, None),
            P("section", None, None),
            P("section", None, None),
        ),
        out_specs=P("section", ("groups", "stream"), None, None),
        check_vma=False,
    )
```

```python
import functools

import jax
import jax.numpy as jnp
from jax import lax
from jax.experimental import pallas as pl
from jax.experimental.pallas import tpu as pltpu
from jax.sharding import PartitionSpec as P

HEADS = 16
GROUP = 16
CHUNK_ROWS = 128


def shifted(value, axis, steps):
    count = lax.axis_size(axis)
    leading, last = (max(0, -steps), min(count, count - steps))
    return lax.ppermute(value, axis, [(source, source + steps) for source in range(leading, last)])


def projection_kernel(x_ref, w_ref, out_ref, nrm_ref, *, head_size):
    step = pl.program_id(0)

    @pl.when(step == 0)
    def _():
        floats = x_ref[...].astype(jnp.float32)
        centred = floats - jnp.mean(floats, axis=-1, keepdims=True)
        variance = jnp.mean(centred * centred, axis=-1, keepdims=True)
        nrm_ref[...] = (centred * lax.rsqrt(variance + 1e-05)).astype(jnp.bfloat16)

    part = jnp.dot(nrm_ref[...], w_ref[...], preferred_element_type=jnp.float32)
    scale = jnp.where(step == 0, head_size ** -0.5, 1.0).astype(jnp.float32)
    out_ref[0] = (part * scale).astype(out_ref.dtype)


def conv_rows(conv_ref, pad_ref, cw_ref, tap_rows, frames, origin):
    width = cw_ref.shape[1]
    chunk = 128

    def conv_chunk(c, carry):
        cols = pl.ds(pl.multiple_of(c * chunk, chunk), chunk)
        for lo in range(0, frames, 8):
            conv = conv_ref[:, pl.ds(lo, 8), cols]
            for j, rows in enumerate(tap_rows):
                if lo in rows:
                    conv = conv + cw_ref[pl.ds(j, 1), cols].reshape(1, 1, chunk) * pad_ref[
                        :, pl.ds(origin + j + lo, 8), cols]
            conv_ref[:, pl.ds(lo, 8), cols] = conv
        return carry

    lax.fori_loop(0, width // chunk, conv_chunk, 0)


def kept_taps(taps, kept, frames):
    return [[lo for lo in range(0, frames, 8) if lo < kept - j] for j in range(taps)]


def new_taps(taps, kept, frames):
    return [[lo for lo in range(0, frames, 8) if lo + 7 >= kept - j] for j in range(taps)]


def kept_conv_kernel(sel_ref, cw_ref, state_hbm, recv_hbm, out_ref, stv, pad_ref, gsem, *,
                     streams, frames, slot, kept):
    width = cw_ref.shape[1]
    rows = pad_ref.shape[1] - frames
    for j in range(streams):
        kind = sel_ref[j]
        idx = sel_ref[streams + j]

        @pl.when(kind == 0)
        def _():
            pltpu.make_async_copy(state_hbm.at[idx, pl.ds(2 * slot, rows)], stv.at[j],
                                  gsem.at[j]).start()

        @pl.when(kind != 0)
        def _():
            pltpu.make_async_copy(recv_hbm.at[idx, pl.ds(2 * slot, rows)], stv.at[j],
                                  gsem.at[j]).start()

    for j in range(streams):
        pltpu.make_async_copy(state_hbm.at[0, pl.ds(2 * slot, rows)], stv.at[j], gsem.at[j]).wait()
    pad_ref[:, 0:rows, :] = stv[...].astype(jnp.float32)
    pad_ref[:, rows:, :] = jnp.zeros((streams, frames, width), jnp.float32)
    out_ref[...] = jnp.zeros_like(out_ref)
    taps = cw_ref.shape[0]
    conv_rows(out_ref, pad_ref, cw_ref, kept_taps(taps, kept, frames), frames, rows - kept)


def kept_conv(sel, state, recv, conv_weight, streams, frames, ctx, kept):
    slot = -(-ctx // 16) * 16
    rows = state.shape[1] - 2 * slot
    width = state.shape[2]
    kernel = functools.partial(kept_conv_kernel, streams=streams, frames=frames, slot=slot,
                               kept=kept)
    vmem = pl.BlockSpec(memory_space=pltpu.VMEM)
    hbm = pl.BlockSpec(memory_space=pl.ANY)
    return pl.pallas_call(
        kernel,
        out_shape=jax.ShapeDtypeStruct((streams, frames, width), jnp.float32),
        in_specs=[pl.BlockSpec(memory_space=pltpu.SMEM), vmem, hbm, hbm],
        out_specs=vmem,
        scratch_shapes=[
            pltpu.VMEM((streams, rows, width), jnp.bfloat16),
            pltpu.VMEM((streams, rows + frames, width), jnp.float32),
            pltpu.SemaphoreType.DMA((streams,)),
        ],
    )(sel, conv_weight, state, recv)


def layer_kernel(sel_ref, x_ref, klive_ref, rlive_ref, cw_ref, qkv_hbm, wo_hbm, state_hbm,
                 recv_hbm, *rest, streams, frames, ctx, head_size, kept_real, early, fused):
    if fused:
        wbuf = rest[-1]
        rest = rest[:-1]
    if early:
        conv_in_ref, out_ref, wobuf, stv, qkv, conv_ref, pad_ref, res_ref, wsem, gsem = rest
    else:
        out_ref, wobuf, stv, qkv, conv_ref, pad_ref, res_ref, wsem, gsem = rest
    tokens = streams * frames
    width = x_ref.shape[1]
    slot = -(-ctx // 16) * 16
    kept = pad_ref.shape[1] - frames
    taps = cw_ref.shape[0]
    chunk = 128

    keys_rows = pl.ds(0, 2 * slot)
    conv_part = pl.ds(2 * slot, stv.shape[1] - 2 * slot)

    def gather(part, which):
        for j in range(streams):
            kind = sel_ref[j]
            idx = sel_ref[streams + j]

            @pl.when(kind == 0)
            def _():
                pltpu.make_async_copy(state_hbm.at[idx, part], stv.at[j, part],
                                      gsem.at[which, j]).start()

            @pl.when(kind != 0)
            def _():
                pltpu.make_async_copy(recv_hbm.at[idx, part], stv.at[j, part],
                                      gsem.at[which, j]).start()

    def gather_wait(part, which):
        for j in range(streams):
            pltpu.make_async_copy(state_hbm.at[0, part], stv.at[j, part], gsem.at[which, j]).wait()

    rows_w = wo_hbm.shape[0]
    if fused:
        first = []
        for r in range(rows_w // CHUNK_ROWS):
            part = pl.ds(r * CHUNK_ROWS, CHUNK_ROWS)
            first.append(pltpu.make_async_copy(qkv_hbm.at[part], wbuf.at[part], wsem.at[0, r]))
    else:
        first = [pltpu.make_async_copy(qkv_hbm, qkv, wsem.at[0, 0])]
    copies = []
    for r in range(rows_w // CHUNK_ROWS):
        part = pl.ds(r * CHUNK_ROWS, CHUNK_ROWS)
        copies.append(pltpu.make_async_copy(wo_hbm.at[part], wobuf.at[part], wsem.at[1, r]))
    for c in first:
        c.start()
    gather(keys_rows, 0)
    for c in copies:
        c.start()
    gather(conv_part, 1)

    if fused:
        floats = x_ref[...].astype(jnp.float32)
        centred = floats - jnp.mean(floats, axis=-1, keepdims=True)
        variance = jnp.mean(centred * centred, axis=-1, keepdims=True)
        normed = (centred * lax.rsqrt(variance + 1e-05)).astype(jnp.bfloat16)
    for c in first:
        c.wait()
    if fused:
        for i in range(3):
            part = jnp.dot(normed, wbuf[:, pl.ds(i * width, width)],
                           preferred_element_type=jnp.float32)
            if i == 0:
                part = part * (head_size ** -0.5)
            qkv[i] = part.astype(jnp.bfloat16)
    gather_wait(keys_rows, 0)

    rows_g = GROUP * frames
    cols_g = GROUP * slot
    q_stream = lax.broadcasted_iota(jnp.int32, (rows_g, cols_g), 0) // frames
    c_col = lax.broadcasted_iota(jnp.int32, (rows_g, cols_g), 1)
    bias_c = jnp.where((c_col // slot == q_stream) & (c_col % slot < ctx), 0.0, -1e30)
    k_stream = lax.broadcasted_iota(jnp.int32, (rows_g, rows_g), 1) // frames
    q_stream_n = lax.broadcasted_iota(jnp.int32, (rows_g, rows_g), 0) // frames
    same_n = q_stream_n == k_stream
    pair = 2 * head_size
    lane = lax.broadcasted_iota(jnp.int32, (rows_g, pair), 1)
    nt = (((1,), (1,)), ((), ()))
    for g in range(streams // GROUP):
        rows = pl.ds(g * rows_g, rows_g)
        srow = pl.ds(g * GROUP, GROUP)
        bias_n = jnp.where(same_n & (klive_ref[:, pl.ds(g * rows_g, rows_g)] > 0.0), 0.0, -1e30)

        def head_pair(p, carry):
            cols = pl.ds(pl.multiple_of(p * pair, pair), pair)
            q = qkv[0, rows, cols]
            k = qkv[1, rows, cols]
            v = qkv[2, rows, cols]
            ck = stv[srow, pl.ds(0, slot), cols].reshape(cols_g, pair)
            cv = stv[srow, pl.ds(slot, slot), cols].reshape(cols_g, pair)
            attended = None
            for half in range(pair // head_size):
                mine = (lane >= half * head_size) & (lane < (half + 1) * head_size)
                qh = jnp.where(mine, q, jnp.zeros_like(q))
                sc = lax.dot_general(qh, ck, nt, preferred_element_type=jnp.float32) + bias_c
                sn = lax.dot_general(qh, k, nt, preferred_element_type=jnp.float32) + bias_n
                top = jnp.maximum(jnp.max(sc, axis=-1, keepdims=True),
                                  jnp.max(sn, axis=-1, keepdims=True))
                ec = jnp.exp(sc - top)
                en = jnp.exp(sn - top)
                total = jnp.sum(ec, axis=-1, keepdims=True) + jnp.sum(en, axis=-1, keepdims=True)
                pc = ec.astype(jnp.bfloat16)
                pn = en.astype(jnp.bfloat16)
                oh = (jnp.dot(pc, cv, preferred_element_type=jnp.float32) + jnp.dot(
                    pn, v, preferred_element_type=jnp.float32)) * (1.0 / total)
                attended = oh if attended is None else jnp.where(mine, oh, attended)
            qkv[0, rows, cols] = attended.astype(jnp.bfloat16)
            return carry

        lax.fori_loop(0, width // pair, head_pair, 0)

    for c in copies:
        c.wait()
    mixed = jnp.dot(qkv[0], wobuf[...], preferred_element_type=jnp.float32)
    residual = x_ref[...].astype(jnp.float32) + mixed
    res_ref[...] = residual
    rounded = residual.astype(jnp.bfloat16).astype(jnp.float32).reshape(streams, frames, width)
    gather_wait(conv_part, 1)
    origin = kept - kept_real
    if early:
        pad_ref[:, 0:kept, :] = jnp.zeros((streams, kept, width), jnp.float32)
        pad_ref[:, kept:, :] = rounded
        conv_ref[...] = conv_in_ref[...]
        conv_rows(conv_ref, pad_ref, cw_ref, new_taps(taps, kept_real, frames), frames, origin)
    else:
        pad_ref[:, 0:kept, :] = stv[:, pl.ds(2 * slot, kept), :].astype(jnp.float32)
        pad_ref[:, kept:, :] = rounded
        conv_ref[...] = jnp.zeros_like(conv_ref)
        every = [list(range(0, frames, 8))] * taps
        conv_rows(conv_ref, pad_ref, cw_ref, every, frames, origin)
    live = rlive_ref[...].reshape(streams, frames, 1)

    def finish(c, carry):
        cols = pl.ds(pl.multiple_of(c * chunk, chunk), chunk)
        conv = conv_ref[:, :, cols]
        res = res_ref[:, cols]
        silu = conv / (1.0 + jnp.exp(-conv))
        out = (res.reshape(streams, frames, chunk) + silu) * live
        out_ref[:, cols] = out.reshape(tokens, chunk).astype(out_ref.dtype)
        return carry

    lax.fori_loop(0, width // chunk, finish, 0)


def project(inputs, qkv_weight):
    streams, frames, width = inputs.shape
    tokens = streams * frames
    x = inputs.reshape(tokens, width)
    kernel = functools.partial(projection_kernel, head_size=width // HEADS)
    return pl.pallas_call(
        kernel,
        out_shape=jax.ShapeDtypeStruct((3, tokens, width), jnp.bfloat16),
        grid=(3,),
        in_specs=[pl.BlockSpec((tokens, width), lambda i: (0, 0)),
                  pl.BlockSpec((width, width), lambda i: (0, i))],
        out_specs=pl.BlockSpec((1, tokens, width), lambda i: (i, 0, 0)),
        scratch_shapes=[pltpu.VMEM((tokens, width), jnp.bfloat16)],
        compiler_params=pltpu.CompilerParams(dimension_semantics=("arbitrary",)),
    )(x, qkv_weight)


def encoder_layer(inputs, valid_counts, sel, state, recv, qkv_weight, out_weight, conv_weight,
                  ctx, kept_real, conv_in=None, projected=None, fused=False):
    streams, frames, width = inputs.shape
    taps = conv_weight.shape[0]
    head_size = width // HEADS
    tokens = streams * frames
    slot = -(-ctx // 16) * 16
    live = (jnp.arange(frames, dtype=jnp.int32)[None, :] < valid_counts[:, None]).astype(jnp.float32)
    klive = live.reshape(1, tokens)
    rlive = live.reshape(tokens, 1)
    x = inputs.reshape(tokens, width)
    kept = state.shape[1] - 2 * slot
    early = conv_in is not None
    kernel = functools.partial(layer_kernel, streams=streams, frames=frames, ctx=ctx,
                               head_size=head_size, kept_real=kept_real, early=early,
                               fused=fused)
    vmem = pl.BlockSpec(memory_space=pltpu.VMEM)
    hbm = pl.BlockSpec(memory_space=pl.ANY)
    extra = [conv_in] if early else []
    out = pl.pallas_call(
        kernel,
        out_shape=jax.ShapeDtypeStruct((tokens, width), jnp.bfloat16),
        in_specs=[pl.BlockSpec(memory_space=pltpu.SMEM), vmem, vmem, vmem, vmem,
                  hbm, hbm, hbm, hbm] + [vmem] * len(extra),
        out_specs=vmem,
        scratch_shapes=[
            pltpu.VMEM((width, width), jnp.bfloat16),
            pltpu.VMEM((streams,) + state.shape[1:], jnp.bfloat16),
            pltpu.VMEM((3, tokens, width), jnp.bfloat16),
            pltpu.VMEM((streams, frames, width), jnp.float32),
            pltpu.VMEM((streams, kept + frames, width), jnp.float32),
            pltpu.VMEM((tokens, width), jnp.float32),
            pltpu.SemaphoreType.DMA((2, width // CHUNK_ROWS)),
            pltpu.SemaphoreType.DMA((2, streams)),
        ] + ([pltpu.VMEM((width, 3 * width), jnp.bfloat16)] if fused else []),
    )(sel, x, klive, rlive, conv_weight,
      qkv_weight if fused else (project(inputs, qkv_weight) if projected is None else projected),
      out_weight, state, recv, *extra)
    return out.reshape(streams, frames, width)


def migrate(anchor, own, count, local_count, state):
    total = anchor.shape[0]
    every_slot = jnp.arange(total, dtype=jnp.int32)
    newpos = jnp.sum(jnp.where(anchor[None, :] == every_slot[:, None], every_slot[None, :], 0),
                     axis=1)
    mine_new = lax.dynamic_slice_in_dim(newpos, own * local_count, local_count)
    target = mine_new // local_count
    hosts = jnp.arange(count, dtype=jnp.int32)
    match = target[None, :] == hosts[:, None]
    send_slot = jnp.sum(jnp.where(match, jnp.arange(local_count, dtype=jnp.int32)[None, :], 0),
                        axis=1)
    send = jnp.take(state, jnp.clip(send_slot, 0, local_count - 1), axis=0, mode="clip")
    mine_old = lax.dynamic_slice_in_dim(anchor, own * local_count, local_count)
    source = mine_old // local_count
    staying = source == own
    local_idx = jnp.clip(mine_old - own * local_count, 0, local_count - 1)
    recv_idx = jnp.clip(source, 0, count - 1)
    sel = jnp.concatenate([jnp.where(staying, 0, 1), jnp.where(staying, local_idx, recv_idx)])
    return sel.astype(jnp.int32), send


def exchange(send):
    return lax.all_to_all(send, "stream", 0, 0, tiled=True)


def body(
    new_frames, valid_counts, anchor, context_cache, conv_state, qkv_weight, out_weight, conv_weight
):
    local_count = new_frames.shape[0]
    own = lax.axis_index("stream")
    count = lax.axis_size("stream")
    ctx = context_cache.shape[2]
    width = conv_state.shape[3]
    slot = -(-ctx // 16) * 16
    kept = conv_state.shape[2]
    lead = (-kept) % 16
    context = context_cache[0]
    state = jnp.concatenate([
        jnp.pad(context[:, :, :width], ((0, 0), (0, slot - ctx), (0, 0))),
        jnp.pad(context[:, :, width:], ((0, 0), (0, slot - ctx), (0, 0))),
        jnp.pad(conv_state[0], ((0, 0), (lead, 0), (0, 0))),
    ], axis=1)
    sel, send = migrate(anchor, own, count, local_count, state)
    valid_here = lax.dynamic_slice_in_dim(valid_counts, own * local_count, local_count)
    section_index = lax.axis_index("section")
    layer = functools.partial(encoder_layer, valid_counts=valid_here, sel=sel, state=state,
                              qkv_weight=qkv_weight[0], out_weight=out_weight[0],
                              conv_weight=conv_weight[0], ctx=ctx, kept_real=kept)
    on_first = section_index == 0
    frames = new_frames.shape[1]
    like = lambda shape, dtype: (lambda: jnp.zeros(shape, dtype))

    def early_branch():
        return exchange(send), project(new_frames, qkv_weight[0])

    recv0, projected = lax.cond(
        on_first, early_branch,
        lambda: (jnp.zeros_like(send), jnp.zeros((3, local_count * frames, width), jnp.bfloat16)))
    token = shifted(recv0[:1, :8], "section", 1)
    zero = jnp.where(on_first, 0.0, jnp.sum(token.astype(jnp.float32)) * 0.0)
    sel0 = sel + zero.astype(sel.dtype)
    first = lax.cond(on_first,
                     lambda: layer(new_frames, sel=sel0, recv=recv0, projected=projected),
                     like(new_frames.shape, new_frames.dtype))

    recv1 = lax.cond(on_first, lambda: jnp.zeros_like(send),
                     lambda: exchange(send + zero.astype(send.dtype)))
    inbound = shifted(first, "section", 1)
    result = lax.cond(on_first, lambda: first, lambda: layer(inbound, recv=recv1, fused=True))
    return result[None]


def solution(mesh):
    return jax.shard_map(
        body,
        mesh=mesh,
        in_specs=(
            P(("groups", "stream"), None, None),
            P("groups"),
            P("groups"),
            P("section", ("groups", "stream"), None, None),
            P("section", ("groups", "stream"), None, None),
            P("section", None, None),
            P("section", None, None),
            P("section", None, None),
        ),
        out_specs=P("section", ("groups", "stream"), None, None),
        check_vma=False,
    )
```

```python
import functools

import jax
import jax.numpy as jnp
from jax import lax
from jax.experimental import pallas as pl
from jax.experimental.pallas import tpu as pltpu
from jax.sharding import PartitionSpec as P

HEADS = 16
GROUP = 16
CHUNK_ROWS = 128


def shifted(value, axis, steps):
    count = lax.axis_size(axis)
    leading, last = (max(0, -steps), min(count, count - steps))
    return lax.ppermute(value, axis, [(source, source + steps) for source in range(leading, last)])


def projection_kernel(x_ref, w_ref, out_ref, nrm_ref, *, head_size):
    step = pl.program_id(0)

    @pl.when(step == 0)
    def _():
        floats = x_ref[...].astype(jnp.float32)
        centred = floats - jnp.mean(floats, axis=-1, keepdims=True)
        variance = jnp.mean(centred * centred, axis=-1, keepdims=True)
        nrm_ref[...] = (centred * lax.rsqrt(variance + 1e-05)).astype(jnp.bfloat16)

    part = jnp.dot(nrm_ref[...], w_ref[...], preferred_element_type=jnp.float32)
    scale = jnp.where(step == 0, head_size ** -0.5, 1.0).astype(jnp.float32)
    out_ref[0] = (part * scale).astype(out_ref.dtype)


def conv_rows(conv_ref, pad_ref, cw_ref, tap_rows, frames, origin):
    width = cw_ref.shape[1]
    chunk = 128

    def conv_chunk(c, carry):
        cols = pl.ds(pl.multiple_of(c * chunk, chunk), chunk)
        for lo in range(0, frames, 8):
            conv = conv_ref[:, pl.ds(lo, 8), cols]
            for j, rows in enumerate(tap_rows):
                if lo in rows:
                    conv = conv + cw_ref[pl.ds(j, 1), cols].reshape(1, 1, chunk) * pad_ref[
                        :, pl.ds(origin + j + lo, 8), cols]
            conv_ref[:, pl.ds(lo, 8), cols] = conv
        return carry

    lax.fori_loop(0, width // chunk, conv_chunk, 0)


def kept_taps(taps, kept, frames):
    return [[lo for lo in range(0, frames, 8) if lo < kept - j] for j in range(taps)]


def new_taps(taps, kept, frames):
    return [[lo for lo in range(0, frames, 8) if lo + 7 >= kept - j] for j in range(taps)]


def kept_conv_kernel(sel_ref, cw_ref, state_hbm, recv_hbm, out_ref, stv, pad_ref, gsem, *,
                     streams, frames, slot, kept):
    width = cw_ref.shape[1]
    rows = pad_ref.shape[1] - frames
    for j in range(streams):
        kind = sel_ref[j]
        idx = sel_ref[streams + j]

        @pl.when(kind == 0)
        def _():
            pltpu.make_async_copy(state_hbm.at[idx, pl.ds(2 * slot, rows)], stv.at[j],
                                  gsem.at[j]).start()

        @pl.when(kind != 0)
        def _():
            pltpu.make_async_copy(recv_hbm.at[idx, pl.ds(2 * slot, rows)], stv.at[j],
                                  gsem.at[j]).start()

    for j in range(streams):
        pltpu.make_async_copy(state_hbm.at[0, pl.ds(2 * slot, rows)], stv.at[j], gsem.at[j]).wait()
    pad_ref[:, 0:rows, :] = stv[...].astype(jnp.float32)
    pad_ref[:, rows:, :] = jnp.zeros((streams, frames, width), jnp.float32)
    out_ref[...] = jnp.zeros_like(out_ref)
    taps = cw_ref.shape[0]
    conv_rows(out_ref, pad_ref, cw_ref, kept_taps(taps, kept, frames), frames, rows - kept)


def kept_conv(sel, state, recv, conv_weight, streams, frames, ctx, kept):
    slot = -(-ctx // 16) * 16
    rows = state.shape[1] - 2 * slot
    width = state.shape[2]
    kernel = functools.partial(kept_conv_kernel, streams=streams, frames=frames, slot=slot,
                               kept=kept)
    vmem = pl.BlockSpec(memory_space=pltpu.VMEM)
    hbm = pl.BlockSpec(memory_space=pl.ANY)
    return pl.pallas_call(
        kernel,
        out_shape=jax.ShapeDtypeStruct((streams, frames, width), jnp.float32),
        in_specs=[pl.BlockSpec(memory_space=pltpu.SMEM), vmem, hbm, hbm],
        out_specs=vmem,
        scratch_shapes=[
            pltpu.VMEM((streams, rows, width), jnp.bfloat16),
            pltpu.VMEM((streams, rows + frames, width), jnp.float32),
            pltpu.SemaphoreType.DMA((streams,)),
        ],
    )(sel, conv_weight, state, recv)


def layer_kernel(sel_ref, x_ref, klive_ref, rlive_ref, cw_ref, qkv_hbm, wo_hbm, state_hbm,
                 recv_hbm, *rest, streams, frames, ctx, head_size, kept_real, early, fused):
    if fused:
        wbuf = rest[-1]
        rest = rest[:-1]
    if early:
        conv_in_ref, out_ref, wobuf, stv, qkv, conv_ref, pad_ref, res_ref, wsem, gsem = rest
    else:
        out_ref, wobuf, stv, qkv, conv_ref, pad_ref, res_ref, wsem, gsem = rest
    tokens = streams * frames
    width = x_ref.shape[1]
    slot = -(-ctx // 16) * 16
    kept = pad_ref.shape[1] - frames
    taps = cw_ref.shape[0]
    chunk = 128

    keys_rows = pl.ds(0, 2 * slot)
    conv_part = pl.ds(2 * slot, stv.shape[1] - 2 * slot)

    def gather(part, which):
        for j in range(streams):
            kind = sel_ref[j]
            idx = sel_ref[streams + j]

            @pl.when(kind == 0)
            def _():
                pltpu.make_async_copy(state_hbm.at[idx, part], stv.at[j, part],
                                      gsem.at[which, j]).start()

            @pl.when(kind != 0)
            def _():
                pltpu.make_async_copy(recv_hbm.at[idx, part], stv.at[j, part],
                                      gsem.at[which, j]).start()

    def gather_wait(part, which):
        for j in range(streams):
            pltpu.make_async_copy(state_hbm.at[0, part], stv.at[j, part], gsem.at[which, j]).wait()

    rows_w = wo_hbm.shape[0]
    if fused:
        first = []
        for r in range(rows_w // CHUNK_ROWS):
            part = pl.ds(r * CHUNK_ROWS, CHUNK_ROWS)
            first.append(pltpu.make_async_copy(qkv_hbm.at[part], wbuf.at[part], wsem.at[0, r]))
    else:
        first = [pltpu.make_async_copy(qkv_hbm, qkv, wsem.at[0, 0])]
    copies = []
    for r in range(rows_w // CHUNK_ROWS):
        part = pl.ds(r * CHUNK_ROWS, CHUNK_ROWS)
        copies.append(pltpu.make_async_copy(wo_hbm.at[part], wobuf.at[part], wsem.at[1, r]))
    origin = kept - kept_real
    if fused:
        gather(conv_part, 1)
        for c in first:
            c.start()
        gather(keys_rows, 0)
        for c in copies:
            c.start()
        floats = x_ref[...].astype(jnp.float32)
        centred = floats - jnp.mean(floats, axis=-1, keepdims=True)
        variance = jnp.mean(centred * centred, axis=-1, keepdims=True)
        normed = (centred * lax.rsqrt(variance + 1e-05)).astype(jnp.bfloat16)
        gather_wait(conv_part, 1)
        pad_ref[:, 0:kept, :] = stv[:, pl.ds(2 * slot, kept), :].astype(jnp.float32)
        pad_ref[:, kept:, :] = jnp.zeros((streams, frames, width), jnp.float32)
        conv_ref[...] = jnp.zeros_like(conv_ref)
        conv_rows(conv_ref, pad_ref, cw_ref, kept_taps(taps, kept_real, frames), frames, origin)
    else:
        for c in first:
            c.start()
        gather(keys_rows, 0)
        for c in copies:
            c.start()
        gather(conv_part, 1)
    for c in first:
        c.wait()
    if fused:
        for i in range(3):
            part = jnp.dot(normed, wbuf[:, pl.ds(i * width, width)],
                           preferred_element_type=jnp.float32)
            if i == 0:
                part = part * (head_size ** -0.5)
            qkv[i] = part.astype(jnp.bfloat16)
    gather_wait(keys_rows, 0)

    rows_g = GROUP * frames
    cols_g = GROUP * slot
    q_stream = lax.broadcasted_iota(jnp.int32, (rows_g, cols_g), 0) // frames
    c_col = lax.broadcasted_iota(jnp.int32, (rows_g, cols_g), 1)
    bias_c = jnp.where((c_col // slot == q_stream) & (c_col % slot < ctx), 0.0, -1e30)
    k_stream = lax.broadcasted_iota(jnp.int32, (rows_g, rows_g), 1) // frames
    q_stream_n = lax.broadcasted_iota(jnp.int32, (rows_g, rows_g), 0) // frames
    same_n = q_stream_n == k_stream
    pair = 2 * head_size
    lane = lax.broadcasted_iota(jnp.int32, (rows_g, pair), 1)
    nt = (((1,), (1,)), ((), ()))
    for g in range(streams // GROUP):
        rows = pl.ds(g * rows_g, rows_g)
        srow = pl.ds(g * GROUP, GROUP)
        bias_n = jnp.where(same_n & (klive_ref[:, pl.ds(g * rows_g, rows_g)] > 0.0), 0.0, -1e30)

        def head_pair(p, carry):
            cols = pl.ds(pl.multiple_of(p * pair, pair), pair)
            q = qkv[0, rows, cols]
            k = qkv[1, rows, cols]
            v = qkv[2, rows, cols]
            ck = stv[srow, pl.ds(0, slot), cols].reshape(cols_g, pair)
            cv = stv[srow, pl.ds(slot, slot), cols].reshape(cols_g, pair)
            attended = None
            for half in range(pair // head_size):
                mine = (lane >= half * head_size) & (lane < (half + 1) * head_size)
                qh = jnp.where(mine, q, jnp.zeros_like(q))
                sc = lax.dot_general(qh, ck, nt, preferred_element_type=jnp.float32) + bias_c
                sn = lax.dot_general(qh, k, nt, preferred_element_type=jnp.float32) + bias_n
                top = jnp.maximum(jnp.max(sc, axis=-1, keepdims=True),
                                  jnp.max(sn, axis=-1, keepdims=True))
                ec = jnp.exp(sc - top)
                en = jnp.exp(sn - top)
                total = jnp.sum(ec, axis=-1, keepdims=True) + jnp.sum(en, axis=-1, keepdims=True)
                pc = ec.astype(jnp.bfloat16)
                pn = en.astype(jnp.bfloat16)
                oh = (jnp.dot(pc, cv, preferred_element_type=jnp.float32) + jnp.dot(
                    pn, v, preferred_element_type=jnp.float32)) * (1.0 / total)
                attended = oh if attended is None else jnp.where(mine, oh, attended)
            qkv[0, rows, cols] = attended.astype(jnp.bfloat16)
            return carry

        lax.fori_loop(0, width // pair, head_pair, 0)

    for c in copies:
        c.wait()
    mixed = jnp.dot(qkv[0], wobuf[...], preferred_element_type=jnp.float32)
    residual = x_ref[...].astype(jnp.float32) + mixed
    res_ref[...] = residual
    rounded = residual.astype(jnp.bfloat16).astype(jnp.float32).reshape(streams, frames, width)
    if not fused:
        gather_wait(conv_part, 1)
    if fused:
        pad_ref[:, 0:kept, :] = jnp.zeros((streams, kept, width), jnp.float32)
        pad_ref[:, kept:, :] = rounded
        conv_rows(conv_ref, pad_ref, cw_ref, new_taps(taps, kept_real, frames), frames, origin)
    elif early:
        pad_ref[:, 0:kept, :] = jnp.zeros((streams, kept, width), jnp.float32)
        pad_ref[:, kept:, :] = rounded
        conv_ref[...] = conv_in_ref[...]
        conv_rows(conv_ref, pad_ref, cw_ref, new_taps(taps, kept_real, frames), frames, origin)
    else:
        pad_ref[:, 0:kept, :] = stv[:, pl.ds(2 * slot, kept), :].astype(jnp.float32)
        pad_ref[:, kept:, :] = rounded
        conv_ref[...] = jnp.zeros_like(conv_ref)
        every = [list(range(0, frames, 8))] * taps
        conv_rows(conv_ref, pad_ref, cw_ref, every, frames, origin)
    live = rlive_ref[...].reshape(streams, frames, 1)

    def finish(c, carry):
        cols = pl.ds(pl.multiple_of(c * chunk, chunk), chunk)
        conv = conv_ref[:, :, cols]
        res = res_ref[:, cols]
        silu = conv / (1.0 + jnp.exp(-conv))
        out = (res.reshape(streams, frames, chunk) + silu) * live
        out_ref[:, cols] = out.reshape(tokens, chunk).astype(out_ref.dtype)
        return carry

    lax.fori_loop(0, width // chunk, finish, 0)


def project(inputs, qkv_weight):
    streams, frames, width = inputs.shape
    tokens = streams * frames
    x = inputs.reshape(tokens, width)
    kernel = functools.partial(projection_kernel, head_size=width // HEADS)
    return pl.pallas_call(
        kernel,
        out_shape=jax.ShapeDtypeStruct((3, tokens, width), jnp.bfloat16),
        grid=(3,),
        in_specs=[pl.BlockSpec((tokens, width), lambda i: (0, 0)),
                  pl.BlockSpec((width, width), lambda i: (0, i))],
        out_specs=pl.BlockSpec((1, tokens, width), lambda i: (i, 0, 0)),
        scratch_shapes=[pltpu.VMEM((tokens, width), jnp.bfloat16)],
        compiler_params=pltpu.CompilerParams(dimension_semantics=("arbitrary",)),
    )(x, qkv_weight)


def encoder_layer(inputs, valid_counts, sel, state, recv, qkv_weight, out_weight, conv_weight,
                  ctx, kept_real, conv_in=None, projected=None, fused=False):
    streams, frames, width = inputs.shape
    taps = conv_weight.shape[0]
    head_size = width // HEADS
    tokens = streams * frames
    slot = -(-ctx // 16) * 16
    live = (jnp.arange(frames, dtype=jnp.int32)[None, :] < valid_counts[:, None]).astype(jnp.float32)
    klive = live.reshape(1, tokens)
    rlive = live.reshape(tokens, 1)
    x = inputs.reshape(tokens, width)
    kept = state.shape[1] - 2 * slot
    early = conv_in is not None
    kernel = functools.partial(layer_kernel, streams=streams, frames=frames, ctx=ctx,
                               head_size=head_size, kept_real=kept_real, early=early,
                               fused=fused)
    vmem = pl.BlockSpec(memory_space=pltpu.VMEM)
    hbm = pl.BlockSpec(memory_space=pl.ANY)
    extra = [conv_in] if early else []
    out = pl.pallas_call(
        kernel,
        out_shape=jax.ShapeDtypeStruct((tokens, width), jnp.bfloat16),
        in_specs=[pl.BlockSpec(memory_space=pltpu.SMEM), vmem, vmem, vmem, vmem,
                  hbm, hbm, hbm, hbm] + [vmem] * len(extra),
        out_specs=vmem,
        scratch_shapes=[
            pltpu.VMEM((width, width), jnp.bfloat16),
            pltpu.VMEM((streams,) + state.shape[1:], jnp.bfloat16),
            pltpu.VMEM((3, tokens, width), jnp.bfloat16),
            pltpu.VMEM((streams, frames, width), jnp.float32),
            pltpu.VMEM((streams, kept + frames, width), jnp.float32),
            pltpu.VMEM((tokens, width), jnp.float32),
            pltpu.SemaphoreType.DMA((2, width // CHUNK_ROWS)),
            pltpu.SemaphoreType.DMA((2, streams)),
        ] + ([pltpu.VMEM((width, 3 * width), jnp.bfloat16)] if fused else []),
    )(sel, x, klive, rlive, conv_weight,
      qkv_weight if fused else (project(inputs, qkv_weight) if projected is None else projected),
      out_weight, state, recv, *extra)
    return out.reshape(streams, frames, width)


def migrate(anchor, own, count, local_count, state):
    total = anchor.shape[0]
    every_slot = jnp.arange(total, dtype=jnp.int32)
    newpos = jnp.sum(jnp.where(anchor[None, :] == every_slot[:, None], every_slot[None, :], 0),
                     axis=1)
    mine_new = lax.dynamic_slice_in_dim(newpos, own * local_count, local_count)
    target = mine_new // local_count
    hosts = jnp.arange(count, dtype=jnp.int32)
    match = target[None, :] == hosts[:, None]
    send_slot = jnp.sum(jnp.where(match, jnp.arange(local_count, dtype=jnp.int32)[None, :], 0),
                        axis=1)
    send = jnp.take(state, jnp.clip(send_slot, 0, local_count - 1), axis=0, mode="clip")
    mine_old = lax.dynamic_slice_in_dim(anchor, own * local_count, local_count)
    source = mine_old // local_count
    staying = source == own
    local_idx = jnp.clip(mine_old - own * local_count, 0, local_count - 1)
    recv_idx = jnp.clip(source, 0, count - 1)
    sel = jnp.concatenate([jnp.where(staying, 0, 1), jnp.where(staying, local_idx, recv_idx)])
    return sel.astype(jnp.int32), send


def exchange(send):
    return lax.all_to_all(send, "stream", 0, 0, tiled=True)


def body(
    new_frames, valid_counts, anchor, context_cache, conv_state, qkv_weight, out_weight, conv_weight
):
    local_count = new_frames.shape[0]
    own = lax.axis_index("stream")
    count = lax.axis_size("stream")
    ctx = context_cache.shape[2]
    width = conv_state.shape[3]
    slot = -(-ctx // 16) * 16
    kept = conv_state.shape[2]
    lead = (-kept) % 16
    context = context_cache[0]
    state = jnp.concatenate([
        jnp.pad(context[:, :, :width], ((0, 0), (0, slot - ctx), (0, 0))),
        jnp.pad(context[:, :, width:], ((0, 0), (0, slot - ctx), (0, 0))),
        jnp.pad(conv_state[0], ((0, 0), (lead, 0), (0, 0))),
    ], axis=1)
    sel, send = migrate(anchor, own, count, local_count, state)
    valid_here = lax.dynamic_slice_in_dim(valid_counts, own * local_count, local_count)
    section_index = lax.axis_index("section")
    layer = functools.partial(encoder_layer, valid_counts=valid_here, sel=sel, state=state,
                              qkv_weight=qkv_weight[0], out_weight=out_weight[0],
                              conv_weight=conv_weight[0], ctx=ctx, kept_real=kept)
    on_first = section_index == 0
    frames = new_frames.shape[1]
    like = lambda shape, dtype: (lambda: jnp.zeros(shape, dtype))

    def early_branch():
        return exchange(send), project(new_frames, qkv_weight[0])

    recv0, projected = lax.cond(
        on_first, early_branch,
        lambda: (jnp.zeros_like(send), jnp.zeros((3, local_count * frames, width), jnp.bfloat16)))
    token = shifted(recv0[:1, :8], "section", 1)
    zero = jnp.where(on_first, 0.0, jnp.sum(token.astype(jnp.float32)) * 0.0)
    sel0 = sel + zero.astype(sel.dtype)
    first = lax.cond(on_first,
                     lambda: layer(new_frames, sel=sel0, recv=recv0, projected=projected),
                     like(new_frames.shape, new_frames.dtype))

    recv1 = lax.cond(on_first, lambda: jnp.zeros_like(send),
                     lambda: exchange(send + zero.astype(send.dtype)))
    inbound = shifted(first, "section", 1)
    result = lax.cond(on_first, lambda: first, lambda: layer(inbound, recv=recv1, fused=True))
    return result[None]


def solution(mesh):
    return jax.shard_map(
        body,
        mesh=mesh,
        in_specs=(
            P(("groups", "stream"), None, None),
            P("groups"),
            P("groups"),
            P("section", ("groups", "stream"), None, None),
            P("section", ("groups", "stream"), None, None),
            P("section", None, None),
            P("section", None, None),
            P("section", None, None),
        ),
        out_specs=P("section", ("groups", "stream"), None, None),
        check_vma=False,
    )
```

```python
import functools

import jax
import jax.numpy as jnp
from jax import lax
from jax.experimental import pallas as pl
from jax.experimental.pallas import tpu as pltpu
from jax.sharding import PartitionSpec as P

HEADS = 16
GROUP = 16
CHUNK_ROWS = 128


def shifted(value, axis, steps):
    count = lax.axis_size(axis)
    leading, last = (max(0, -steps), min(count, count - steps))
    return lax.ppermute(value, axis, [(source, source + steps) for source in range(leading, last)])


def projection_kernel(x_ref, w_ref, out_ref, nrm_ref, *, head_size):
    step = pl.program_id(0)

    @pl.when(step == 0)
    def _():
        floats = x_ref[...].astype(jnp.float32)
        centred = floats - jnp.mean(floats, axis=-1, keepdims=True)
        variance = jnp.mean(centred * centred, axis=-1, keepdims=True)
        nrm_ref[...] = (centred * lax.rsqrt(variance + 1e-05)).astype(jnp.bfloat16)

    part = jnp.dot(nrm_ref[...], w_ref[...], preferred_element_type=jnp.float32)
    scale = jnp.where(step == 0, head_size ** -0.5, 1.0).astype(jnp.float32)
    out_ref[0] = (part * scale).astype(out_ref.dtype)


def conv_rows(conv_ref, pad_ref, cw_ref, tap_rows, frames, origin):
    width = cw_ref.shape[1]
    chunk = 128

    def conv_chunk(c, carry):
        cols = pl.ds(pl.multiple_of(c * chunk, chunk), chunk)
        for lo in range(0, frames, 8):
            conv = conv_ref[:, pl.ds(lo, 8), cols]
            for j, rows in enumerate(tap_rows):
                if lo in rows:
                    conv = conv + cw_ref[pl.ds(j, 1), cols].reshape(1, 1, chunk) * pad_ref[
                        :, pl.ds(origin + j + lo, 8), cols]
            conv_ref[:, pl.ds(lo, 8), cols] = conv
        return carry

    lax.fori_loop(0, width // chunk, conv_chunk, 0)


def kept_taps(taps, kept, frames):
    return [[lo for lo in range(0, frames, 8) if lo < kept - j] for j in range(taps)]


def new_taps(taps, kept, frames):
    return [[lo for lo in range(0, frames, 8) if lo + 7 >= kept - j] for j in range(taps)]


def kept_conv_kernel(sel_ref, cw_ref, state_hbm, recv_hbm, out_ref, stv, pad_ref, gsem, *,
                     streams, frames, slot, kept):
    width = cw_ref.shape[1]
    rows = pad_ref.shape[1] - frames
    for j in range(streams):
        kind = sel_ref[j]
        idx = sel_ref[streams + j]

        @pl.when(kind == 0)
        def _():
            pltpu.make_async_copy(state_hbm.at[idx, pl.ds(2 * slot, rows)], stv.at[j],
                                  gsem.at[j]).start()

        @pl.when(kind != 0)
        def _():
            pltpu.make_async_copy(recv_hbm.at[idx, pl.ds(2 * slot, rows)], stv.at[j],
                                  gsem.at[j]).start()

    for j in range(streams):
        pltpu.make_async_copy(state_hbm.at[0, pl.ds(2 * slot, rows)], stv.at[j], gsem.at[j]).wait()
    pad_ref[:, 0:rows, :] = stv[...].astype(jnp.float32)
    pad_ref[:, rows:, :] = jnp.zeros((streams, frames, width), jnp.float32)
    out_ref[...] = jnp.zeros_like(out_ref)
    taps = cw_ref.shape[0]
    conv_rows(out_ref, pad_ref, cw_ref, kept_taps(taps, kept, frames), frames, rows - kept)


def kept_conv(sel, state, recv, conv_weight, streams, frames, ctx, kept):
    slot = -(-ctx // 16) * 16
    rows = state.shape[1] - 2 * slot
    width = state.shape[2]
    kernel = functools.partial(kept_conv_kernel, streams=streams, frames=frames, slot=slot,
                               kept=kept)
    vmem = pl.BlockSpec(memory_space=pltpu.VMEM)
    hbm = pl.BlockSpec(memory_space=pl.ANY)
    return pl.pallas_call(
        kernel,
        out_shape=jax.ShapeDtypeStruct((streams, frames, width), jnp.float32),
        in_specs=[pl.BlockSpec(memory_space=pltpu.SMEM), vmem, hbm, hbm],
        out_specs=vmem,
        scratch_shapes=[
            pltpu.VMEM((streams, rows, width), jnp.bfloat16),
            pltpu.VMEM((streams, rows + frames, width), jnp.float32),
            pltpu.SemaphoreType.DMA((streams,)),
        ],
    )(sel, conv_weight, state, recv)


def layer_kernel(sel_ref, x_ref, klive_ref, rlive_ref, cw_ref, qkv_hbm, wo_hbm, state_hbm,
                 recv_hbm, *rest, streams, frames, ctx, head_size, kept_real, early, fused):
    if fused:
        wbuf = rest[-1]
        rest = rest[:-1]
    if early:
        conv_in_ref, out_ref, wobuf, stv, qkv, conv_ref, pad_ref, res_ref, wsem, gsem = rest
    else:
        out_ref, wobuf, stv, qkv, conv_ref, pad_ref, res_ref, wsem, gsem = rest
    tokens = streams * frames
    width = x_ref.shape[1]
    slot = -(-ctx // 16) * 16
    kept = pad_ref.shape[1] - frames
    taps = cw_ref.shape[0]
    chunk = 128

    keys_rows = pl.ds(0, 2 * slot)
    conv_part = pl.ds(2 * slot, stv.shape[1] - 2 * slot)

    def gather(part, which):
        for j in range(streams):
            kind = sel_ref[j]
            idx = sel_ref[streams + j]

            @pl.when(kind == 0)
            def _():
                pltpu.make_async_copy(state_hbm.at[idx, part], stv.at[j, part],
                                      gsem.at[which, j]).start()

            @pl.when(kind != 0)
            def _():
                pltpu.make_async_copy(recv_hbm.at[idx, part], stv.at[j, part],
                                      gsem.at[which, j]).start()

    def gather_wait(part, which):
        for j in range(streams):
            pltpu.make_async_copy(state_hbm.at[0, part], stv.at[j, part], gsem.at[which, j]).wait()

    rows_w = wo_hbm.shape[0]
    if fused:
        first = []
        for r in range(rows_w // CHUNK_ROWS):
            part = pl.ds(r * CHUNK_ROWS, CHUNK_ROWS)
            first.append(pltpu.make_async_copy(qkv_hbm.at[part], wbuf.at[part], wsem.at[0, r]))
    else:
        first = [pltpu.make_async_copy(qkv_hbm, qkv, wsem.at[0, 0])]
    copies = []
    for r in range(rows_w // CHUNK_ROWS):
        part = pl.ds(r * CHUNK_ROWS, CHUNK_ROWS)
        copies.append(pltpu.make_async_copy(wo_hbm.at[part], wobuf.at[part], wsem.at[1, r]))
    for c in first:
        c.start()
    gather(keys_rows, 0)
    for c in copies:
        c.start()
    gather(conv_part, 1)

    if fused:
        floats = x_ref[...].astype(jnp.float32)
        centred = floats - jnp.mean(floats, axis=-1, keepdims=True)
        variance = jnp.mean(centred * centred, axis=-1, keepdims=True)
        normed = (centred * lax.rsqrt(variance + 1e-05)).astype(jnp.bfloat16)
    for c in first:
        c.wait()
    if fused:
        for i in range(3):
            part = jnp.dot(normed, wbuf[:, pl.ds(i * width, width)],
                           preferred_element_type=jnp.float32)
            if i == 0:
                part = part * (head_size ** -0.5)
            qkv[i] = part.astype(jnp.bfloat16)
    gather_wait(keys_rows, 0)

    rows_g = GROUP * frames
    cols_g = GROUP * slot
    q_stream = lax.broadcasted_iota(jnp.int32, (rows_g, cols_g), 0) // frames
    c_col = lax.broadcasted_iota(jnp.int32, (rows_g, cols_g), 1)
    bias_c = jnp.where((c_col // slot == q_stream) & (c_col % slot < ctx), 0.0, -1e30)
    k_stream = lax.broadcasted_iota(jnp.int32, (rows_g, rows_g), 1) // frames
    q_stream_n = lax.broadcasted_iota(jnp.int32, (rows_g, rows_g), 0) // frames
    same_n = q_stream_n == k_stream
    pair = 2 * head_size
    lane = lax.broadcasted_iota(jnp.int32, (rows_g, pair), 1)
    nt = (((1,), (1,)), ((), ()))
    for g in range(streams // GROUP):
        rows = pl.ds(g * rows_g, rows_g)
        srow = pl.ds(g * GROUP, GROUP)
        bias_n = jnp.where(same_n & (klive_ref[:, pl.ds(g * rows_g, rows_g)] > 0.0), 0.0, -1e30)

        def head_pair(p, carry):
            cols = pl.ds(pl.multiple_of(p * pair, pair), pair)
            q = qkv[0, rows, cols]
            k = qkv[1, rows, cols]
            v = qkv[2, rows, cols]
            ck = stv[srow, pl.ds(0, slot), cols].reshape(cols_g, pair)
            cv = stv[srow, pl.ds(slot, slot), cols].reshape(cols_g, pair)
            attended = None
            for half in range(pair // head_size):
                mine = (lane >= half * head_size) & (lane < (half + 1) * head_size)
                qh = jnp.where(mine, q, jnp.zeros_like(q))
                sc = lax.dot_general(qh, ck, nt, preferred_element_type=jnp.float32) + bias_c
                sn = lax.dot_general(qh, k, nt, preferred_element_type=jnp.float32) + bias_n
                top = jnp.maximum(jnp.max(sc, axis=-1, keepdims=True),
                                  jnp.max(sn, axis=-1, keepdims=True))
                ec = jnp.exp(sc - top)
                en = jnp.exp(sn - top)
                total = jnp.sum(ec, axis=-1, keepdims=True) + jnp.sum(en, axis=-1, keepdims=True)
                pc = ec.astype(jnp.bfloat16)
                pn = en.astype(jnp.bfloat16)
                oh = (jnp.dot(pc, cv, preferred_element_type=jnp.float32) + jnp.dot(
                    pn, v, preferred_element_type=jnp.float32)) * (1.0 / total)
                attended = oh if attended is None else jnp.where(mine, oh, attended)
            qkv[0, rows, cols] = attended.astype(jnp.bfloat16)
            return carry

        lax.fori_loop(0, width // pair, head_pair, 0)

    for c in copies:
        c.wait()
    mixed = jnp.dot(qkv[0], wobuf[...], preferred_element_type=jnp.float32)
    residual = x_ref[...].astype(jnp.float32) + mixed
    res_ref[...] = residual
    rounded = residual.astype(jnp.bfloat16).astype(jnp.float32).reshape(streams, frames, width)
    gather_wait(conv_part, 1)
    origin = kept - kept_real
    if early:
        pad_ref[:, 0:kept, :] = jnp.zeros((streams, kept, width), jnp.float32)
        pad_ref[:, kept:, :] = rounded
        conv_ref[...] = conv_in_ref[...]
        conv_rows(conv_ref, pad_ref, cw_ref, new_taps(taps, kept_real, frames), frames, origin)
    else:
        pad_ref[:, 0:kept, :] = stv[:, pl.ds(2 * slot, kept), :].astype(jnp.float32)
        pad_ref[:, kept:, :] = rounded
        conv_ref[...] = jnp.zeros_like(conv_ref)
        every = [list(range(0, frames, 8))] * taps
        conv_rows(conv_ref, pad_ref, cw_ref, every, frames, origin)
    live = rlive_ref[...].reshape(streams, frames, 1)

    def finish(c, carry):
        cols = pl.ds(pl.multiple_of(c * chunk, chunk), chunk)
        conv = conv_ref[:, :, cols]
        res = res_ref[:, cols]
        silu = conv / (1.0 + jnp.exp(-conv))
        out = (res.reshape(streams, frames, chunk) + silu) * live
        out_ref[:, cols] = out.reshape(tokens, chunk).astype(out_ref.dtype)
        return carry

    lax.fori_loop(0, width // chunk, finish, 0)


def project(inputs, qkv_weight):
    streams, frames, width = inputs.shape
    tokens = streams * frames
    x = inputs.reshape(tokens, width)
    kernel = functools.partial(projection_kernel, head_size=width // HEADS)
    return pl.pallas_call(
        kernel,
        out_shape=jax.ShapeDtypeStruct((3, tokens, width), jnp.bfloat16),
        grid=(3,),
        in_specs=[pl.BlockSpec((tokens, width), lambda i: (0, 0)),
                  pl.BlockSpec((width, width), lambda i: (0, i))],
        out_specs=pl.BlockSpec((1, tokens, width), lambda i: (i, 0, 0)),
        scratch_shapes=[pltpu.VMEM((tokens, width), jnp.bfloat16)],
        compiler_params=pltpu.CompilerParams(dimension_semantics=("arbitrary",)),
    )(x, qkv_weight)


def encoder_layer(inputs, valid_counts, sel, state, recv, qkv_weight, out_weight, conv_weight,
                  ctx, kept_real, conv_in=None, projected=None, fused=False):
    streams, frames, width = inputs.shape
    taps = conv_weight.shape[0]
    head_size = width // HEADS
    tokens = streams * frames
    slot = -(-ctx // 16) * 16
    live = (jnp.arange(frames, dtype=jnp.int32)[None, :] < valid_counts[:, None]).astype(jnp.float32)
    klive = live.reshape(1, tokens)
    rlive = live.reshape(tokens, 1)
    x = inputs.reshape(tokens, width)
    kept = state.shape[1] - 2 * slot
    early = conv_in is not None
    kernel = functools.partial(layer_kernel, streams=streams, frames=frames, ctx=ctx,
                               head_size=head_size, kept_real=kept_real, early=early,
                               fused=fused)
    vmem = pl.BlockSpec(memory_space=pltpu.VMEM)
    hbm = pl.BlockSpec(memory_space=pl.ANY)
    extra = [conv_in] if early else []
    out = pl.pallas_call(
        kernel,
        out_shape=jax.ShapeDtypeStruct((tokens, width), jnp.bfloat16),
        in_specs=[pl.BlockSpec(memory_space=pltpu.SMEM), vmem, vmem, vmem, vmem,
                  hbm, hbm, hbm, hbm] + [vmem] * len(extra),
        out_specs=vmem,
        scratch_shapes=[
            pltpu.VMEM((width, width), jnp.bfloat16),
            pltpu.VMEM((streams,) + state.shape[1:], jnp.bfloat16),
            pltpu.VMEM((3, tokens, width), jnp.bfloat16),
            pltpu.VMEM((streams, frames, width), jnp.float32),
            pltpu.VMEM((streams, kept + frames, width), jnp.float32),
            pltpu.VMEM((tokens, width), jnp.float32),
            pltpu.SemaphoreType.DMA((2, width // CHUNK_ROWS)),
            pltpu.SemaphoreType.DMA((2, streams)),
        ] + ([pltpu.VMEM((width, 3 * width), jnp.bfloat16)] if fused else []),
    )(sel, x, klive, rlive, conv_weight,
      qkv_weight if fused else (project(inputs, qkv_weight) if projected is None else projected),
      out_weight, state, recv, *extra)
    return out.reshape(streams, frames, width)


def migrate(anchor, own, count, local_count, state):
    total = anchor.shape[0]
    every_slot = jnp.arange(total, dtype=jnp.int32)
    mine = own * local_count + jnp.arange(local_count, dtype=jnp.int32)
    mine_new = jnp.sum(jnp.where(anchor[None, :] == mine[:, None], every_slot[None, :], 0), axis=1)
    target = mine_new // local_count
    hosts = jnp.arange(count, dtype=jnp.int32)
    match = target[None, :] == hosts[:, None]
    send_slot = jnp.sum(jnp.where(match, jnp.arange(local_count, dtype=jnp.int32)[None, :], 0),
                        axis=1)
    send = jnp.take(state, jnp.clip(send_slot, 0, local_count - 1), axis=0, mode="clip")
    mine_old = lax.dynamic_slice_in_dim(anchor, own * local_count, local_count)
    source = mine_old // local_count
    staying = source == own
    local_idx = jnp.clip(mine_old - own * local_count, 0, local_count - 1)
    recv_idx = jnp.clip(source, 0, count - 1)
    sel = jnp.concatenate([jnp.where(staying, 0, 1), jnp.where(staying, local_idx, recv_idx)])
    return sel.astype(jnp.int32), send


def exchange(send):
    return lax.all_to_all(send, "stream", 0, 0, tiled=True)


def body(
    new_frames, valid_counts, anchor, context_cache, conv_state, qkv_weight, out_weight, conv_weight
):
    local_count = new_frames.shape[0]
    own = lax.axis_index("stream")
    count = lax.axis_size("stream")
    ctx = context_cache.shape[2]
    width = conv_state.shape[3]
    slot = -(-ctx // 16) * 16
    kept = conv_state.shape[2]
    lead = (-kept) % 16
    context = context_cache[0]
    state = jnp.concatenate([
        jnp.pad(context[:, :, :width], ((0, 0), (0, slot - ctx), (0, 0))),
        jnp.pad(context[:, :, width:], ((0, 0), (0, slot - ctx), (0, 0))),
        jnp.pad(conv_state[0], ((0, 0), (lead, 0), (0, 0))),
    ], axis=1)
    sel, send = migrate(anchor, own, count, local_count, state)
    valid_here = lax.dynamic_slice_in_dim(valid_counts, own * local_count, local_count)
    section_index = lax.axis_index("section")
    layer = functools.partial(encoder_layer, valid_counts=valid_here, sel=sel, state=state,
                              qkv_weight=qkv_weight[0], out_weight=out_weight[0],
                              conv_weight=conv_weight[0], ctx=ctx, kept_real=kept)
    on_first = section_index == 0
    frames = new_frames.shape[1]
    like = lambda shape, dtype: (lambda: jnp.zeros(shape, dtype))

    def early_branch():
        return exchange(send), project(new_frames, qkv_weight[0])

    recv0, projected = lax.cond(
        on_first, early_branch,
        lambda: (jnp.zeros_like(send), jnp.zeros((3, local_count * frames, width), jnp.bfloat16)))
    token = shifted(recv0[:1, :8], "section", 1)
    zero = jnp.where(on_first, 0.0, jnp.sum(token.astype(jnp.float32)) * 0.0)
    sel0 = sel + zero.astype(sel.dtype)
    first = lax.cond(on_first,
                     lambda: layer(new_frames, sel=sel0, recv=recv0, projected=projected),
                     like(new_frames.shape, new_frames.dtype))

    recv1 = lax.cond(on_first, lambda: jnp.zeros_like(send),
                     lambda: exchange(send + zero.astype(send.dtype)))
    inbound = shifted(first, "section", 1)
    result = lax.cond(on_first, lambda: first, lambda: layer(inbound, recv=recv1, fused=True))
    return result[None]


def solution(mesh):
    return jax.shard_map(
        body,
        mesh=mesh,
        in_specs=(
            P(("groups", "stream"), None, None),
            P("groups"),
            P("groups"),
            P("section", ("groups", "stream"), None, None),
            P("section", ("groups", "stream"), None, None),
            P("section", None, None),
            P("section", None, None),
            P("section", None, None),
        ),
        out_specs=P("section", ("groups", "stream"), None, None),
        check_vma=False,
    )
```

```python
import functools

import jax
import jax.numpy as jnp
from jax import lax
from jax.experimental import pallas as pl
from jax.experimental.pallas import tpu as pltpu
from jax.sharding import PartitionSpec as P

HEADS = 16
GROUP = 16
CHUNK_ROWS = 128


def shifted(value, axis, steps):
    count = lax.axis_size(axis)
    leading, last = (max(0, -steps), min(count, count - steps))
    return lax.ppermute(value, axis, [(source, source + steps) for source in range(leading, last)])


def projection_kernel(x_ref, w_ref, out_ref, nrm_ref, *, head_size):
    step = pl.program_id(0)

    @pl.when(step == 0)
    def _():
        floats = x_ref[...].astype(jnp.float32)
        centred = floats - jnp.mean(floats, axis=-1, keepdims=True)
        variance = jnp.mean(centred * centred, axis=-1, keepdims=True)
        nrm_ref[...] = (centred * lax.rsqrt(variance + 1e-05)).astype(jnp.bfloat16)

    part = jnp.dot(nrm_ref[...], w_ref[...], preferred_element_type=jnp.float32)
    scale = jnp.where(step == 0, head_size ** -0.5, 1.0).astype(jnp.float32)
    out_ref[0] = (part * scale).astype(out_ref.dtype)


def conv_rows(conv_ref, pad_ref, cw_ref, tap_rows, frames, origin):
    width = cw_ref.shape[1]
    chunk = 128

    def conv_chunk(c, carry):
        cols = pl.ds(pl.multiple_of(c * chunk, chunk), chunk)
        for lo in range(0, frames, 8):
            conv = conv_ref[:, pl.ds(lo, 8), cols]
            for j, rows in enumerate(tap_rows):
                if lo in rows:
                    conv = conv + cw_ref[pl.ds(j, 1), cols].reshape(1, 1, chunk) * pad_ref[
                        :, pl.ds(origin + j + lo, 8), cols]
            conv_ref[:, pl.ds(lo, 8), cols] = conv
        return carry

    lax.fori_loop(0, width // chunk, conv_chunk, 0)


def kept_taps(taps, kept, frames):
    return [[lo for lo in range(0, frames, 8) if lo < kept - j] for j in range(taps)]


def new_taps(taps, kept, frames):
    return [[lo for lo in range(0, frames, 8) if lo + 7 >= kept - j] for j in range(taps)]


def kept_conv_kernel(sel_ref, cw_ref, state_hbm, recv_hbm, out_ref, stv, pad_ref, gsem, *,
                     streams, frames, slot, kept):
    width = cw_ref.shape[1]
    rows = pad_ref.shape[1] - frames
    for j in range(streams):
        kind = sel_ref[j]
        idx = sel_ref[streams + j]

        @pl.when(kind == 0)
        def _():
            pltpu.make_async_copy(state_hbm.at[idx, pl.ds(2 * slot, rows)], stv.at[j],
                                  gsem.at[j]).start()

        @pl.when(kind != 0)
        def _():
            pltpu.make_async_copy(recv_hbm.at[idx, pl.ds(2 * slot, rows)], stv.at[j],
                                  gsem.at[j]).start()

    for j in range(streams):
        pltpu.make_async_copy(state_hbm.at[0, pl.ds(2 * slot, rows)], stv.at[j], gsem.at[j]).wait()
    pad_ref[:, 0:rows, :] = stv[...].astype(jnp.float32)
    pad_ref[:, rows:, :] = jnp.zeros((streams, frames, width), jnp.float32)
    out_ref[...] = jnp.zeros_like(out_ref)
    taps = cw_ref.shape[0]
    conv_rows(out_ref, pad_ref, cw_ref, kept_taps(taps, kept, frames), frames, rows - kept)


def kept_conv(sel, state, recv, conv_weight, streams, frames, ctx, kept):
    slot = -(-ctx // 16) * 16
    rows = state.shape[1] - 2 * slot
    width = state.shape[2]
    kernel = functools.partial(kept_conv_kernel, streams=streams, frames=frames, slot=slot,
                               kept=kept)
    vmem = pl.BlockSpec(memory_space=pltpu.VMEM)
    hbm = pl.BlockSpec(memory_space=pl.ANY)
    return pl.pallas_call(
        kernel,
        out_shape=jax.ShapeDtypeStruct((streams, frames, width), jnp.float32),
        in_specs=[pl.BlockSpec(memory_space=pltpu.SMEM), vmem, hbm, hbm],
        out_specs=vmem,
        scratch_shapes=[
            pltpu.VMEM((streams, rows, width), jnp.bfloat16),
            pltpu.VMEM((streams, rows + frames, width), jnp.float32),
            pltpu.SemaphoreType.DMA((streams,)),
        ],
    )(sel, conv_weight, state, recv)


def layer_kernel(sel_ref, x_ref, klive_ref, rlive_ref, cw_ref, qkv_hbm, wo_hbm, state_hbm,
                 recv_hbm, *rest, streams, frames, ctx, head_size, kept_real, early, fused):
    if fused:
        wbuf = rest[-1]
        rest = rest[:-1]
    if early:
        conv_in_ref, out_ref, wobuf, stv, qkv, conv_ref, pad_ref, res_ref, wsem, gsem = rest
    else:
        out_ref, wobuf, stv, qkv, conv_ref, pad_ref, res_ref, wsem, gsem = rest
    tokens = streams * frames
    width = x_ref.shape[1]
    slot = -(-ctx // 16) * 16
    kept = pad_ref.shape[1] - frames
    taps = cw_ref.shape[0]
    chunk = 128

    keys_rows = pl.ds(0, 2 * slot)
    conv_part = pl.ds(2 * slot, stv.shape[1] - 2 * slot)

    def gather(part, which):
        for j in range(streams):
            kind = sel_ref[j]
            idx = sel_ref[streams + j]

            @pl.when(kind == 0)
            def _():
                pltpu.make_async_copy(state_hbm.at[idx, part], stv.at[j, part],
                                      gsem.at[which, j]).start()

            @pl.when(kind != 0)
            def _():
                pltpu.make_async_copy(recv_hbm.at[idx, part], stv.at[j, part],
                                      gsem.at[which, j]).start()

    def gather_wait(part, which):
        for j in range(streams):
            pltpu.make_async_copy(state_hbm.at[0, part], stv.at[j, part], gsem.at[which, j]).wait()

    rows_w = wo_hbm.shape[0]
    if fused:
        first = []
        for i in range(3):
            part = pl.ds(i * width, width)
            first.append(pltpu.make_async_copy(qkv_hbm.at[:, part], wbuf.at[:, part],
                                               wsem.at[0, i]))
    else:
        first = [pltpu.make_async_copy(qkv_hbm, qkv, wsem.at[0, 0])]
    copies = []
    for r in range(rows_w // CHUNK_ROWS):
        part = pl.ds(r * CHUNK_ROWS, CHUNK_ROWS)
        copies.append(pltpu.make_async_copy(wo_hbm.at[part], wobuf.at[part], wsem.at[1, r]))
    for c in first:
        c.start()
    gather(keys_rows, 0)
    for c in copies:
        c.start()
    gather(conv_part, 1)

    if fused:
        floats = x_ref[...].astype(jnp.float32)
        centred = floats - jnp.mean(floats, axis=-1, keepdims=True)
        variance = jnp.mean(centred * centred, axis=-1, keepdims=True)
        normed = (centred * lax.rsqrt(variance + 1e-05)).astype(jnp.bfloat16)
    if not fused:
        first[0].wait()
    if fused:
        for i in range(3):
            first[i].wait()
            part = jnp.dot(normed, wbuf[:, pl.ds(i * width, width)],
                           preferred_element_type=jnp.float32)
            if i == 0:
                part = part * (head_size ** -0.5)
            qkv[i] = part.astype(jnp.bfloat16)
    gather_wait(keys_rows, 0)

    rows_g = GROUP * frames
    cols_g = GROUP * slot
    q_stream = lax.broadcasted_iota(jnp.int32, (rows_g, cols_g), 0) // frames
    c_col = lax.broadcasted_iota(jnp.int32, (rows_g, cols_g), 1)
    bias_c = jnp.where((c_col // slot == q_stream) & (c_col % slot < ctx), 0.0, -1e30)
    k_stream = lax.broadcasted_iota(jnp.int32, (rows_g, rows_g), 1) // frames
    q_stream_n = lax.broadcasted_iota(jnp.int32, (rows_g, rows_g), 0) // frames
    same_n = q_stream_n == k_stream
    pair = 2 * head_size
    lane = lax.broadcasted_iota(jnp.int32, (rows_g, pair), 1)
    nt = (((1,), (1,)), ((), ()))
    for g in range(streams // GROUP):
        rows = pl.ds(g * rows_g, rows_g)
        srow = pl.ds(g * GROUP, GROUP)
        bias_n = jnp.where(same_n & (klive_ref[:, pl.ds(g * rows_g, rows_g)] > 0.0), 0.0, -1e30)

        def head_pair(p, carry):
            cols = pl.ds(pl.multiple_of(p * pair, pair), pair)
            q = qkv[0, rows, cols]
            k = qkv[1, rows, cols]
            v = qkv[2, rows, cols]
            ck = stv[srow, pl.ds(0, slot), cols].reshape(cols_g, pair)
            cv = stv[srow, pl.ds(slot, slot), cols].reshape(cols_g, pair)
            attended = None
            for half in range(pair // head_size):
                mine = (lane >= half * head_size) & (lane < (half + 1) * head_size)
                qh = jnp.where(mine, q, jnp.zeros_like(q))
                sc = lax.dot_general(qh, ck, nt, preferred_element_type=jnp.float32) + bias_c
                sn = lax.dot_general(qh, k, nt, preferred_element_type=jnp.float32) + bias_n
                top = jnp.maximum(jnp.max(sc, axis=-1, keepdims=True),
                                  jnp.max(sn, axis=-1, keepdims=True))
                ec = jnp.exp(sc - top)
                en = jnp.exp(sn - top)
                total = jnp.sum(ec, axis=-1, keepdims=True) + jnp.sum(en, axis=-1, keepdims=True)
                pc = ec.astype(jnp.bfloat16)
                pn = en.astype(jnp.bfloat16)
                oh = (jnp.dot(pc, cv, preferred_element_type=jnp.float32) + jnp.dot(
                    pn, v, preferred_element_type=jnp.float32)) * (1.0 / total)
                attended = oh if attended is None else jnp.where(mine, oh, attended)
            qkv[0, rows, cols] = attended.astype(jnp.bfloat16)
            return carry

        lax.fori_loop(0, width // pair, head_pair, 0)

    for c in copies:
        c.wait()
    mixed = jnp.dot(qkv[0], wobuf[...], preferred_element_type=jnp.float32)
    residual = x_ref[...].astype(jnp.float32) + mixed
    res_ref[...] = residual
    rounded = residual.astype(jnp.bfloat16).astype(jnp.float32).reshape(streams, frames, width)
    gather_wait(conv_part, 1)
    origin = kept - kept_real
    if early:
        pad_ref[:, 0:kept, :] = jnp.zeros((streams, kept, width), jnp.float32)
        pad_ref[:, kept:, :] = rounded
        conv_ref[...] = conv_in_ref[...]
        conv_rows(conv_ref, pad_ref, cw_ref, new_taps(taps, kept_real, frames), frames, origin)
    else:
        pad_ref[:, 0:kept, :] = stv[:, pl.ds(2 * slot, kept), :].astype(jnp.float32)
        pad_ref[:, kept:, :] = rounded
        conv_ref[...] = jnp.zeros_like(conv_ref)
        every = [list(range(0, frames, 8))] * taps
        conv_rows(conv_ref, pad_ref, cw_ref, every, frames, origin)
    live = rlive_ref[...].reshape(streams, frames, 1)

    def finish(c, carry):
        cols = pl.ds(pl.multiple_of(c * chunk, chunk), chunk)
        conv = conv_ref[:, :, cols]
        res = res_ref[:, cols]
        silu = conv / (1.0 + jnp.exp(-conv))
        out = (res.reshape(streams, frames, chunk) + silu) * live
        out_ref[:, cols] = out.reshape(tokens, chunk).astype(out_ref.dtype)
        return carry

    lax.fori_loop(0, width // chunk, finish, 0)


def project(inputs, qkv_weight):
    streams, frames, width = inputs.shape
    tokens = streams * frames
    x = inputs.reshape(tokens, width)
    kernel = functools.partial(projection_kernel, head_size=width // HEADS)
    return pl.pallas_call(
        kernel,
        out_shape=jax.ShapeDtypeStruct((3, tokens, width), jnp.bfloat16),
        grid=(3,),
        in_specs=[pl.BlockSpec((tokens, width), lambda i: (0, 0)),
                  pl.BlockSpec((width, width), lambda i: (0, i))],
        out_specs=pl.BlockSpec((1, tokens, width), lambda i: (i, 0, 0)),
        scratch_shapes=[pltpu.VMEM((tokens, width), jnp.bfloat16)],
        compiler_params=pltpu.CompilerParams(dimension_semantics=("arbitrary",)),
    )(x, qkv_weight)


def encoder_layer(inputs, valid_counts, sel, state, recv, qkv_weight, out_weight, conv_weight,
                  ctx, kept_real, conv_in=None, projected=None, fused=False):
    streams, frames, width = inputs.shape
    taps = conv_weight.shape[0]
    head_size = width // HEADS
    tokens = streams * frames
    slot = -(-ctx // 16) * 16
    live = (jnp.arange(frames, dtype=jnp.int32)[None, :] < valid_counts[:, None]).astype(jnp.float32)
    klive = live.reshape(1, tokens)
    rlive = live.reshape(tokens, 1)
    x = inputs.reshape(tokens, width)
    kept = state.shape[1] - 2 * slot
    early = conv_in is not None
    kernel = functools.partial(layer_kernel, streams=streams, frames=frames, ctx=ctx,
                               head_size=head_size, kept_real=kept_real, early=early,
                               fused=fused)
    vmem = pl.BlockSpec(memory_space=pltpu.VMEM)
    hbm = pl.BlockSpec(memory_space=pl.ANY)
    extra = [conv_in] if early else []
    out = pl.pallas_call(
        kernel,
        out_shape=jax.ShapeDtypeStruct((tokens, width), jnp.bfloat16),
        in_specs=[pl.BlockSpec(memory_space=pltpu.SMEM), vmem, vmem, vmem, vmem,
                  hbm, hbm, hbm, hbm] + [vmem] * len(extra),
        out_specs=vmem,
        scratch_shapes=[
            pltpu.VMEM((width, width), jnp.bfloat16),
            pltpu.VMEM((streams,) + state.shape[1:], jnp.bfloat16),
            pltpu.VMEM((3, tokens, width), jnp.bfloat16),
            pltpu.VMEM((streams, frames, width), jnp.float32),
            pltpu.VMEM((streams, kept + frames, width), jnp.float32),
            pltpu.VMEM((tokens, width), jnp.float32),
            pltpu.SemaphoreType.DMA((2, width // CHUNK_ROWS)),
            pltpu.SemaphoreType.DMA((2, streams)),
        ] + ([pltpu.VMEM((width, 3 * width), jnp.bfloat16)] if fused else []),
    )(sel, x, klive, rlive, conv_weight,
      qkv_weight if fused else (project(inputs, qkv_weight) if projected is None else projected),
      out_weight, state, recv, *extra)
    return out.reshape(streams, frames, width)


def migrate(anchor, own, count, local_count, state):
    total = anchor.shape[0]
    every_slot = jnp.arange(total, dtype=jnp.int32)
    mine = own * local_count + jnp.arange(local_count, dtype=jnp.int32)
    mine_new = jnp.sum(jnp.where(anchor[None, :] == mine[:, None], every_slot[None, :], 0), axis=1)
    target = mine_new // local_count
    hosts = jnp.arange(count, dtype=jnp.int32)
    match = target[None, :] == hosts[:, None]
    send_slot = jnp.sum(jnp.where(match, jnp.arange(local_count, dtype=jnp.int32)[None, :], 0),
                        axis=1)
    send = jnp.take(state, jnp.clip(send_slot, 0, local_count - 1), axis=0, mode="clip")
    mine_old = lax.dynamic_slice_in_dim(anchor, own * local_count, local_count)
    source = mine_old // local_count
    staying = source == own
    local_idx = jnp.clip(mine_old - own * local_count, 0, local_count - 1)
    recv_idx = jnp.clip(source, 0, count - 1)
    sel = jnp.concatenate([jnp.where(staying, 0, 1), jnp.where(staying, local_idx, recv_idx)])
    return sel.astype(jnp.int32), send


def exchange(send):
    return lax.all_to_all(send, "stream", 0, 0, tiled=True)


def body(
    new_frames, valid_counts, anchor, context_cache, conv_state, qkv_weight, out_weight, conv_weight
):
    local_count = new_frames.shape[0]
    own = lax.axis_index("stream")
    count = lax.axis_size("stream")
    ctx = context_cache.shape[2]
    width = conv_state.shape[3]
    slot = -(-ctx // 16) * 16
    kept = conv_state.shape[2]
    lead = (-kept) % 16
    context = context_cache[0]
    state = jnp.concatenate([
        jnp.pad(context[:, :, :width], ((0, 0), (0, slot - ctx), (0, 0))),
        jnp.pad(context[:, :, width:], ((0, 0), (0, slot - ctx), (0, 0))),
        jnp.pad(conv_state[0], ((0, 0), (lead, 0), (0, 0))),
    ], axis=1)
    sel, send = migrate(anchor, own, count, local_count, state)
    valid_here = lax.dynamic_slice_in_dim(valid_counts, own * local_count, local_count)
    section_index = lax.axis_index("section")
    layer = functools.partial(encoder_layer, valid_counts=valid_here, sel=sel, state=state,
                              qkv_weight=qkv_weight[0], out_weight=out_weight[0],
                              conv_weight=conv_weight[0], ctx=ctx, kept_real=kept)
    on_first = section_index == 0
    frames = new_frames.shape[1]
    like = lambda shape, dtype: (lambda: jnp.zeros(shape, dtype))

    def early_branch():
        return exchange(send), project(new_frames, qkv_weight[0])

    recv0, projected = lax.cond(
        on_first, early_branch,
        lambda: (jnp.zeros_like(send), jnp.zeros((3, local_count * frames, width), jnp.bfloat16)))
    token = shifted(recv0[:1, :8], "section", 1)
    zero = jnp.where(on_first, 0.0, jnp.sum(token.astype(jnp.float32)) * 0.0)
    sel0 = sel + zero.astype(sel.dtype)
    first = lax.cond(on_first,
                     lambda: layer(new_frames, sel=sel0, recv=recv0, projected=projected),
                     like(new_frames.shape, new_frames.dtype))

    recv1 = lax.cond(on_first, lambda: jnp.zeros_like(send),
                     lambda: exchange(send + zero.astype(send.dtype)))
    inbound = shifted(first, "section", 1)
    result = lax.cond(on_first, lambda: first, lambda: layer(inbound, recv=recv1, fused=True))
    return result[None]


def solution(mesh):
    return jax.shard_map(
        body,
        mesh=mesh,
        in_specs=(
            P(("groups", "stream"), None, None),
            P("groups"),
            P("groups"),
            P("section", ("groups", "stream"), None, None),
            P("section", ("groups", "stream"), None, None),
            P("section", None, None),
            P("section", None, None),
            P("section", None, None),
        ),
        out_specs=P("section", ("groups", "stream"), None, None),
        check_vma=False,
    )
```

```python
import functools

import jax
import jax.numpy as jnp
from jax import lax
from jax.experimental import pallas as pl
from jax.experimental.pallas import tpu as pltpu
from jax.sharding import PartitionSpec as P

HEADS = 16
GROUP = 16
CHUNK_ROWS = 128


def shifted(value, axis, steps):
    count = lax.axis_size(axis)
    leading, last = (max(0, -steps), min(count, count - steps))
    return lax.ppermute(value, axis, [(source, source + steps) for source in range(leading, last)])


def projection_kernel(x_ref, w_ref, out_ref, nrm_ref, *, head_size):
    step = pl.program_id(0)

    @pl.when(step == 0)
    def _():
        floats = x_ref[...].astype(jnp.float32)
        centred = floats - jnp.mean(floats, axis=-1, keepdims=True)
        variance = jnp.mean(centred * centred, axis=-1, keepdims=True)
        nrm_ref[...] = (centred * lax.rsqrt(variance + 1e-05)).astype(jnp.bfloat16)

    part = jnp.dot(nrm_ref[...], w_ref[...], preferred_element_type=jnp.float32)
    scale = jnp.where(step == 0, head_size ** -0.5, 1.0).astype(jnp.float32)
    out_ref[0] = (part * scale).astype(out_ref.dtype)


def conv_rows(conv_ref, pad_ref, cw_ref, tap_rows, frames, origin):
    width = cw_ref.shape[1]
    chunk = 128

    def conv_chunk(c, carry):
        cols = pl.ds(pl.multiple_of(c * chunk, chunk), chunk)
        for lo in range(0, frames, 8):
            conv = conv_ref[:, pl.ds(lo, 8), cols]
            for j, rows in enumerate(tap_rows):
                if lo in rows:
                    conv = conv + cw_ref[pl.ds(j, 1), cols].reshape(1, 1, chunk) * pad_ref[
                        :, pl.ds(origin + j + lo, 8), cols]
            conv_ref[:, pl.ds(lo, 8), cols] = conv
        return carry

    lax.fori_loop(0, width // chunk, conv_chunk, 0)


def kept_taps(taps, kept, frames):
    return [[lo for lo in range(0, frames, 8) if lo < kept - j] for j in range(taps)]


def new_taps(taps, kept, frames):
    return [[lo for lo in range(0, frames, 8) if lo + 7 >= kept - j] for j in range(taps)]


def kept_conv_kernel(sel_ref, cw_ref, state_hbm, recv_hbm, out_ref, stv, pad_ref, gsem, *,
                     streams, frames, slot, kept):
    width = cw_ref.shape[1]
    rows = pad_ref.shape[1] - frames
    for j in range(streams):
        kind = sel_ref[j]
        idx = sel_ref[streams + j]

        @pl.when(kind == 0)
        def _():
            pltpu.make_async_copy(state_hbm.at[idx, pl.ds(2 * slot, rows)], stv.at[j],
                                  gsem.at[j]).start()

        @pl.when(kind != 0)
        def _():
            pltpu.make_async_copy(recv_hbm.at[idx, pl.ds(2 * slot, rows)], stv.at[j],
                                  gsem.at[j]).start()

    for j in range(streams):
        pltpu.make_async_copy(state_hbm.at[0, pl.ds(2 * slot, rows)], stv.at[j], gsem.at[j]).wait()
    pad_ref[:, 0:rows, :] = stv[...].astype(jnp.float32)
    pad_ref[:, rows:, :] = jnp.zeros((streams, frames, width), jnp.float32)
    out_ref[...] = jnp.zeros_like(out_ref)
    taps = cw_ref.shape[0]
    conv_rows(out_ref, pad_ref, cw_ref, kept_taps(taps, kept, frames), frames, rows - kept)


def kept_conv(sel, state, recv, conv_weight, streams, frames, ctx, kept):
    slot = -(-ctx // 16) * 16
    rows = state.shape[1] - 2 * slot
    width = state.shape[2]
    kernel = functools.partial(kept_conv_kernel, streams=streams, frames=frames, slot=slot,
                               kept=kept)
    vmem = pl.BlockSpec(memory_space=pltpu.VMEM)
    hbm = pl.BlockSpec(memory_space=pl.ANY)
    return pl.pallas_call(
        kernel,
        out_shape=jax.ShapeDtypeStruct((streams, frames, width), jnp.float32),
        in_specs=[pl.BlockSpec(memory_space=pltpu.SMEM), vmem, hbm, hbm],
        out_specs=vmem,
        scratch_shapes=[
            pltpu.VMEM((streams, rows, width), jnp.bfloat16),
            pltpu.VMEM((streams, rows + frames, width), jnp.float32),
            pltpu.SemaphoreType.DMA((streams,)),
        ],
    )(sel, conv_weight, state, recv)


def layer_kernel(sel_ref, x_ref, klive_ref, rlive_ref, cw_ref, qkv_hbm, wo_hbm, state_hbm,
                 recv_hbm, *rest, streams, frames, ctx, head_size, kept_real, early, fused):
    if fused:
        wbuf = rest[-1]
        rest = rest[:-1]
    if early:
        conv_in_ref, out_ref, wobuf, stv, qkv, conv_ref, pad_ref, res_ref, wsem, gsem = rest
    else:
        out_ref, wobuf, stv, qkv, conv_ref, pad_ref, res_ref, wsem, gsem = rest
    tokens = streams * frames
    width = x_ref.shape[1]
    slot = -(-ctx // 16) * 16
    kept = pad_ref.shape[1] - frames
    taps = cw_ref.shape[0]
    chunk = 128

    keys_rows = pl.ds(0, 2 * slot)
    conv_part = pl.ds(2 * slot, stv.shape[1] - 2 * slot)

    def gather(part, which):
        for j in range(streams):
            kind = sel_ref[j]
            idx = sel_ref[streams + j]

            @pl.when(kind == 0)
            def _():
                pltpu.make_async_copy(state_hbm.at[idx, part], stv.at[j, part],
                                      gsem.at[which, j]).start()

            @pl.when(kind != 0)
            def _():
                pltpu.make_async_copy(recv_hbm.at[idx, part], stv.at[j, part],
                                      gsem.at[which, j]).start()

    def gather_wait(part, which):
        for j in range(streams):
            pltpu.make_async_copy(state_hbm.at[0, part], stv.at[j, part], gsem.at[which, j]).wait()

    rows_w = wo_hbm.shape[0]
    if fused:
        first = []
        for r in range(rows_w // CHUNK_ROWS):
            part = pl.ds(r * CHUNK_ROWS, CHUNK_ROWS)
            first.append(pltpu.make_async_copy(qkv_hbm.at[part], wbuf.at[part], wsem.at[0, r]))
    else:
        first = [pltpu.make_async_copy(qkv_hbm, qkv, wsem.at[0, 0])]
    copies = []
    for r in range(rows_w // CHUNK_ROWS):
        part = pl.ds(r * CHUNK_ROWS, CHUNK_ROWS)
        copies.append(pltpu.make_async_copy(wo_hbm.at[part], wobuf.at[part], wsem.at[1, r]))
    for c in first:
        c.start()
    gather(keys_rows, 0)
    for c in copies:
        c.start()
    gather(conv_part, 1)

    if fused:
        floats = x_ref[...].astype(jnp.float32)
        centred = floats - jnp.mean(floats, axis=-1, keepdims=True)
        variance = jnp.mean(centred * centred, axis=-1, keepdims=True)
        normed = (centred * lax.rsqrt(variance + 1e-05)).astype(jnp.bfloat16)
    for c in first:
        c.wait()
    if fused:
        for i in range(3):
            part = jnp.dot(normed, wbuf[:, pl.ds(i * width, width)],
                           preferred_element_type=jnp.float32)
            if i == 0:
                part = part * (head_size ** -0.5)
            qkv[i] = part.astype(jnp.bfloat16)
    gather_wait(keys_rows, 0)

    rows_g = GROUP * frames
    cols_g = GROUP * slot
    q_stream = lax.broadcasted_iota(jnp.int32, (rows_g, cols_g), 0) // frames
    c_col = lax.broadcasted_iota(jnp.int32, (rows_g, cols_g), 1)
    bias_c = jnp.where((c_col // slot == q_stream) & (c_col % slot < ctx), 0.0, -1e30)
    k_stream = lax.broadcasted_iota(jnp.int32, (rows_g, rows_g), 1) // frames
    q_stream_n = lax.broadcasted_iota(jnp.int32, (rows_g, rows_g), 0) // frames
    same_n = q_stream_n == k_stream
    pair = 2 * head_size
    lane = lax.broadcasted_iota(jnp.int32, (rows_g, pair), 1)
    nt = (((1,), (1,)), ((), ()))
    for g in range(streams // GROUP):
        rows = pl.ds(g * rows_g, rows_g)
        srow = pl.ds(g * GROUP, GROUP)
        bias_n = jnp.where(same_n & (klive_ref[:, pl.ds(g * rows_g, rows_g)] > 0.0), 0.0, -1e30)

        def head_pair(p, carry):
            cols = pl.ds(pl.multiple_of(p * pair, pair), pair)
            q = qkv[0, rows, cols]
            k = qkv[1, rows, cols]
            v = qkv[2, rows, cols]
            ck = stv[srow, pl.ds(0, slot), cols].reshape(cols_g, pair)
            cv = stv[srow, pl.ds(slot, slot), cols].reshape(cols_g, pair)
            attended = None
            for half in range(pair // head_size):
                mine = (lane >= half * head_size) & (lane < (half + 1) * head_size)
                qh = jnp.where(mine, q, jnp.zeros_like(q))
                sc = lax.dot_general(qh, ck, nt, preferred_element_type=jnp.float32) + bias_c
                sn = lax.dot_general(qh, k, nt, preferred_element_type=jnp.float32) + bias_n
                top = jnp.maximum(jnp.max(sc, axis=-1, keepdims=True),
                                  jnp.max(sn, axis=-1, keepdims=True))
                ec = jnp.exp(sc - top)
                en = jnp.exp(sn - top)
                total = jnp.sum(ec, axis=-1, keepdims=True) + jnp.sum(en, axis=-1, keepdims=True)
                pc = ec.astype(jnp.bfloat16)
                pn = en.astype(jnp.bfloat16)
                oh = (jnp.dot(pc, cv, preferred_element_type=jnp.float32) + jnp.dot(
                    pn, v, preferred_element_type=jnp.float32)) * (1.0 / total)
                attended = oh if attended is None else jnp.where(mine, oh, attended)
            qkv[0, rows, cols] = attended.astype(jnp.bfloat16)
            return carry

        lax.fori_loop(0, width // pair, head_pair, 0, unroll=2)

    for c in copies:
        c.wait()
    mixed = jnp.dot(qkv[0], wobuf[...], preferred_element_type=jnp.float32)
    residual = x_ref[...].astype(jnp.float32) + mixed
    res_ref[...] = residual
    rounded = residual.astype(jnp.bfloat16).astype(jnp.float32).reshape(streams, frames, width)
    gather_wait(conv_part, 1)
    origin = kept - kept_real
    if early:
        pad_ref[:, 0:kept, :] = jnp.zeros((streams, kept, width), jnp.float32)
        pad_ref[:, kept:, :] = rounded
        conv_ref[...] = conv_in_ref[...]
        conv_rows(conv_ref, pad_ref, cw_ref, new_taps(taps, kept_real, frames), frames, origin)
    else:
        pad_ref[:, 0:kept, :] = stv[:, pl.ds(2 * slot, kept), :].astype(jnp.float32)
        pad_ref[:, kept:, :] = rounded
        conv_ref[...] = jnp.zeros_like(conv_ref)
        every = [list(range(0, frames, 8))] * taps
        conv_rows(conv_ref, pad_ref, cw_ref, every, frames, origin)
    live = rlive_ref[...].reshape(streams, frames, 1)

    def finish(c, carry):
        cols = pl.ds(pl.multiple_of(c * chunk, chunk), chunk)
        conv = conv_ref[:, :, cols]
        res = res_ref[:, cols]
        silu = conv / (1.0 + jnp.exp(-conv))
        out = (res.reshape(streams, frames, chunk) + silu) * live
        out_ref[:, cols] = out.reshape(tokens, chunk).astype(out_ref.dtype)
        return carry

    lax.fori_loop(0, width // chunk, finish, 0)


def project(inputs, qkv_weight):
    streams, frames, width = inputs.shape
    tokens = streams * frames
    x = inputs.reshape(tokens, width)
    kernel = functools.partial(projection_kernel, head_size=width // HEADS)
    return pl.pallas_call(
        kernel,
        out_shape=jax.ShapeDtypeStruct((3, tokens, width), jnp.bfloat16),
        grid=(3,),
        in_specs=[pl.BlockSpec((tokens, width), lambda i: (0, 0)),
                  pl.BlockSpec((width, width), lambda i: (0, i))],
        out_specs=pl.BlockSpec((1, tokens, width), lambda i: (i, 0, 0)),
        scratch_shapes=[pltpu.VMEM((tokens, width), jnp.bfloat16)],
        compiler_params=pltpu.CompilerParams(dimension_semantics=("arbitrary",)),
    )(x, qkv_weight)


def encoder_layer(inputs, valid_counts, sel, state, recv, qkv_weight, out_weight, conv_weight,
                  ctx, kept_real, conv_in=None, projected=None, fused=False):
    streams, frames, width = inputs.shape
    taps = conv_weight.shape[0]
    head_size = width // HEADS
    tokens = streams * frames
    slot = -(-ctx // 16) * 16
    live = (jnp.arange(frames, dtype=jnp.int32)[None, :] < valid_counts[:, None]).astype(jnp.float32)
    klive = live.reshape(1, tokens)
    rlive = live.reshape(tokens, 1)
    x = inputs.reshape(tokens, width)
    kept = state.shape[1] - 2 * slot
    early = conv_in is not None
    kernel = functools.partial(layer_kernel, streams=streams, frames=frames, ctx=ctx,
                               head_size=head_size, kept_real=kept_real, early=early,
                               fused=fused)
    vmem = pl.BlockSpec(memory_space=pltpu.VMEM)
    hbm = pl.BlockSpec(memory_space=pl.ANY)
    extra = [conv_in] if early else []
    out = pl.pallas_call(
        kernel,
        out_shape=jax.ShapeDtypeStruct((tokens, width), jnp.bfloat16),
        in_specs=[pl.BlockSpec(memory_space=pltpu.SMEM), vmem, vmem, vmem, vmem,
                  hbm, hbm, hbm, hbm] + [vmem] * len(extra),
        out_specs=vmem,
        scratch_shapes=[
            pltpu.VMEM((width, width), jnp.bfloat16),
            pltpu.VMEM((streams,) + state.shape[1:], jnp.bfloat16),
            pltpu.VMEM((3, tokens, width), jnp.bfloat16),
            pltpu.VMEM((streams, frames, width), jnp.float32),
            pltpu.VMEM((streams, kept + frames, width), jnp.float32),
            pltpu.VMEM((tokens, width), jnp.float32),
            pltpu.SemaphoreType.DMA((2, width // CHUNK_ROWS)),
            pltpu.SemaphoreType.DMA((2, streams)),
        ] + ([pltpu.VMEM((width, 3 * width), jnp.bfloat16)] if fused else []),
    )(sel, x, klive, rlive, conv_weight,
      qkv_weight if fused else (project(inputs, qkv_weight) if projected is None else projected),
      out_weight, state, recv, *extra)
    return out.reshape(streams, frames, width)


def migrate(anchor, own, count, local_count, state):
    total = anchor.shape[0]
    every_slot = jnp.arange(total, dtype=jnp.int32)
    mine = own * local_count + jnp.arange(local_count, dtype=jnp.int32)
    mine_new = jnp.sum(jnp.where(anchor[None, :] == mine[:, None], every_slot[None, :], 0), axis=1)
    target = mine_new // local_count
    hosts = jnp.arange(count, dtype=jnp.int32)
    match = target[None, :] == hosts[:, None]
    send_slot = jnp.sum(jnp.where(match, jnp.arange(local_count, dtype=jnp.int32)[None, :], 0),
                        axis=1)
    send = jnp.take(state, jnp.clip(send_slot, 0, local_count - 1), axis=0, mode="clip")
    mine_old = lax.dynamic_slice_in_dim(anchor, own * local_count, local_count)
    source = mine_old // local_count
    staying = source == own
    local_idx = jnp.clip(mine_old - own * local_count, 0, local_count - 1)
    recv_idx = jnp.clip(source, 0, count - 1)
    sel = jnp.concatenate([jnp.where(staying, 0, 1), jnp.where(staying, local_idx, recv_idx)])
    return sel.astype(jnp.int32), send


def exchange(send):
    return lax.all_to_all(send, "stream", 0, 0, tiled=True)


def body(
    new_frames, valid_counts, anchor, context_cache, conv_state, qkv_weight, out_weight, conv_weight
):
    local_count = new_frames.shape[0]
    own = lax.axis_index("stream")
    count = lax.axis_size("stream")
    ctx = context_cache.shape[2]
    width = conv_state.shape[3]
    slot = -(-ctx // 16) * 16
    kept = conv_state.shape[2]
    lead = (-kept) % 16
    context = context_cache[0]
    state = jnp.concatenate([
        jnp.pad(context[:, :, :width], ((0, 0), (0, slot - ctx), (0, 0))),
        jnp.pad(context[:, :, width:], ((0, 0), (0, slot - ctx), (0, 0))),
        jnp.pad(conv_state[0], ((0, 0), (lead, 0), (0, 0))),
    ], axis=1)
    sel, send = migrate(anchor, own, count, local_count, state)
    valid_here = lax.dynamic_slice_in_dim(valid_counts, own * local_count, local_count)
    section_index = lax.axis_index("section")
    layer = functools.partial(encoder_layer, valid_counts=valid_here, sel=sel, state=state,
                              qkv_weight=qkv_weight[0], out_weight=out_weight[0],
                              conv_weight=conv_weight[0], ctx=ctx, kept_real=kept)
    on_first = section_index == 0
    frames = new_frames.shape[1]
    like = lambda shape, dtype: (lambda: jnp.zeros(shape, dtype))

    def early_branch():
        return exchange(send), project(new_frames, qkv_weight[0])

    recv0, projected = lax.cond(
        on_first, early_branch,
        lambda: (jnp.zeros_like(send), jnp.zeros((3, local_count * frames, width), jnp.bfloat16)))
    token = shifted(recv0[:1, :8], "section", 1)
    zero = jnp.where(on_first, 0.0, jnp.sum(token.astype(jnp.float32)) * 0.0)
    sel0 = sel + zero.astype(sel.dtype)
    first = lax.cond(on_first,
                     lambda: layer(new_frames, sel=sel0, recv=recv0, projected=projected),
                     like(new_frames.shape, new_frames.dtype))

    recv1 = lax.cond(on_first, lambda: jnp.zeros_like(send),
                     lambda: exchange(send + zero.astype(send.dtype)))
    inbound = shifted(first, "section", 1)
    result = lax.cond(on_first, lambda: first, lambda: layer(inbound, recv=recv1, fused=True))
    return result[None]


def solution(mesh):
    return jax.shard_map(
        body,
        mesh=mesh,
        in_specs=(
            P(("groups", "stream"), None, None),
            P("groups"),
            P("groups"),
            P("section", ("groups", "stream"), None, None),
            P("section", ("groups", "stream"), None, None),
            P("section", None, None),
            P("section", None, None),
            P("section", None, None),
        ),
        out_specs=P("section", ("groups", "stream"), None, None),
        check_vma=False,
    )
```

```python
import functools

import jax
import jax.numpy as jnp
from jax import lax
from jax.experimental import pallas as pl
from jax.experimental.pallas import tpu as pltpu
from jax.sharding import PartitionSpec as P

HEADS = 16
GROUP = 16
CHUNK_ROWS = 128


def shifted(value, axis, steps):
    count = lax.axis_size(axis)
    leading, last = (max(0, -steps), min(count, count - steps))
    return lax.ppermute(value, axis, [(source, source + steps) for source in range(leading, last)])


def projection_kernel(x_ref, w_ref, out_ref, nrm_ref, *, head_size):
    step = pl.program_id(0)

    @pl.when(step == 0)
    def _():
        floats = x_ref[...].astype(jnp.float32)
        centred = floats - jnp.mean(floats, axis=-1, keepdims=True)
        variance = jnp.mean(centred * centred, axis=-1, keepdims=True)
        nrm_ref[...] = (centred * lax.rsqrt(variance + 1e-05)).astype(jnp.bfloat16)

    part = jnp.dot(nrm_ref[...], w_ref[...], preferred_element_type=jnp.float32)
    scale = jnp.where(step == 0, head_size ** -0.5, 1.0).astype(jnp.float32)
    out_ref[0] = (part * scale).astype(out_ref.dtype)


def conv_rows(conv_ref, pad_ref, cw_ref, tap_rows, frames, origin):
    width = cw_ref.shape[1]
    chunk = 128

    def conv_chunk(c, carry):
        cols = pl.ds(pl.multiple_of(c * chunk, chunk), chunk)
        for lo in range(0, frames, 8):
            conv = conv_ref[:, pl.ds(lo, 8), cols]
            for j, rows in enumerate(tap_rows):
                if lo in rows:
                    conv = conv + cw_ref[pl.ds(j, 1), cols].reshape(1, 1, chunk) * pad_ref[
                        :, pl.ds(origin + j + lo, 8), cols]
            conv_ref[:, pl.ds(lo, 8), cols] = conv
        return carry

    lax.fori_loop(0, width // chunk, conv_chunk, 0)


def kept_taps(taps, kept, frames):
    return [[lo for lo in range(0, frames, 8) if lo < kept - j] for j in range(taps)]


def new_taps(taps, kept, frames):
    return [[lo for lo in range(0, frames, 8) if lo + 7 >= kept - j] for j in range(taps)]


def kept_conv_kernel(sel_ref, cw_ref, state_hbm, recv_hbm, out_ref, stv, pad_ref, gsem, *,
                     streams, frames, slot, kept):
    width = cw_ref.shape[1]
    rows = pad_ref.shape[1] - frames
    for j in range(streams):
        kind = sel_ref[j]
        idx = sel_ref[streams + j]

        @pl.when(kind == 0)
        def _():
            pltpu.make_async_copy(state_hbm.at[idx, pl.ds(2 * slot, rows)], stv.at[j],
                                  gsem.at[j]).start()

        @pl.when(kind != 0)
        def _():
            pltpu.make_async_copy(recv_hbm.at[idx, pl.ds(2 * slot, rows)], stv.at[j],
                                  gsem.at[j]).start()

    for j in range(streams):
        pltpu.make_async_copy(state_hbm.at[0, pl.ds(2 * slot, rows)], stv.at[j], gsem.at[j]).wait()
    pad_ref[:, 0:rows, :] = stv[...].astype(jnp.float32)
    pad_ref[:, rows:, :] = jnp.zeros((streams, frames, width), jnp.float32)
    out_ref[...] = jnp.zeros_like(out_ref)
    taps = cw_ref.shape[0]
    conv_rows(out_ref, pad_ref, cw_ref, kept_taps(taps, kept, frames), frames, rows - kept)


def kept_conv(sel, state, recv, conv_weight, streams, frames, ctx, kept):
    slot = -(-ctx // 16) * 16
    rows = state.shape[1] - 2 * slot
    width = state.shape[2]
    kernel = functools.partial(kept_conv_kernel, streams=streams, frames=frames, slot=slot,
                               kept=kept)
    vmem = pl.BlockSpec(memory_space=pltpu.VMEM)
    hbm = pl.BlockSpec(memory_space=pl.ANY)
    return pl.pallas_call(
        kernel,
        out_shape=jax.ShapeDtypeStruct((streams, frames, width), jnp.float32),
        in_specs=[pl.BlockSpec(memory_space=pltpu.SMEM), vmem, hbm, hbm],
        out_specs=vmem,
        scratch_shapes=[
            pltpu.VMEM((streams, rows, width), jnp.bfloat16),
            pltpu.VMEM((streams, rows + frames, width), jnp.float32),
            pltpu.SemaphoreType.DMA((streams,)),
        ],
    )(sel, conv_weight, state, recv)


def layer_kernel(sel_ref, x_ref, klive_ref, rlive_ref, cw_ref, qkv_hbm, wo_hbm, state_hbm,
                 recv_hbm, *rest, streams, frames, ctx, head_size, kept_real, early, fused):
    if fused:
        wbuf = rest[-1]
        rest = rest[:-1]
    if early:
        conv_in_ref, out_ref, wobuf, stv, qkv, conv_ref, pad_ref, res_ref, wsem, gsem = rest
    else:
        out_ref, wobuf, stv, qkv, conv_ref, pad_ref, res_ref, wsem, gsem = rest
    tokens = streams * frames
    width = x_ref.shape[1]
    slot = -(-ctx // 16) * 16
    kept = pad_ref.shape[1] - frames
    taps = cw_ref.shape[0]
    chunk = 128

    keys_rows = pl.ds(0, 2 * slot)
    conv_part = pl.ds(2 * slot, stv.shape[1] - 2 * slot)

    def gather(part, which):
        for j in range(streams):
            kind = sel_ref[j]
            idx = sel_ref[streams + j]

            @pl.when(kind == 0)
            def _():
                pltpu.make_async_copy(state_hbm.at[idx, part], stv.at[j, part],
                                      gsem.at[which, j]).start()

            @pl.when(kind != 0)
            def _():
                pltpu.make_async_copy(recv_hbm.at[idx, part], stv.at[j, part],
                                      gsem.at[which, j]).start()

    def gather_wait(part, which):
        for j in range(streams):
            pltpu.make_async_copy(state_hbm.at[0, part], stv.at[j, part], gsem.at[which, j]).wait()

    rows_w = wo_hbm.shape[0]
    if fused:
        first = []
        for r in range(rows_w // CHUNK_ROWS):
            part = pl.ds(r * CHUNK_ROWS, CHUNK_ROWS)
            first.append(pltpu.make_async_copy(qkv_hbm.at[part], wbuf.at[part], wsem.at[0, r]))
    else:
        first = [pltpu.make_async_copy(qkv_hbm, qkv, wsem.at[0, 0])]
    copies = []
    for r in range(rows_w // CHUNK_ROWS):
        part = pl.ds(r * CHUNK_ROWS, CHUNK_ROWS)
        copies.append(pltpu.make_async_copy(wo_hbm.at[part], wobuf.at[part], wsem.at[1, r]))
    for c in first:
        c.start()
    gather(keys_rows, 0)
    for c in copies:
        c.start()
    gather(conv_part, 1)

    if fused:
        floats = x_ref[...].astype(jnp.float32)
        centred = floats - jnp.mean(floats, axis=-1, keepdims=True)
        variance = jnp.mean(centred * centred, axis=-1, keepdims=True)
        normed = (centred * lax.rsqrt(variance + 1e-05)).astype(jnp.bfloat16)
    for c in first:
        c.wait()
    if fused:
        for i in range(3):
            part = jnp.dot(normed, wbuf[:, pl.ds(i * width, width)],
                           preferred_element_type=jnp.float32)
            if i == 0:
                part = part * (head_size ** -0.5)
            qkv[i] = part.astype(jnp.bfloat16)
    gather_wait(keys_rows, 0)

    rows_g = GROUP * frames
    cols_g = GROUP * slot
    q_stream = lax.broadcasted_iota(jnp.int32, (rows_g, cols_g), 0) // frames
    c_col = lax.broadcasted_iota(jnp.int32, (rows_g, cols_g), 1)
    bias_c = jnp.where((c_col // slot == q_stream) & (c_col % slot < ctx), 0.0, -1e30)
    k_stream = lax.broadcasted_iota(jnp.int32, (rows_g, rows_g), 1) // frames
    q_stream_n = lax.broadcasted_iota(jnp.int32, (rows_g, rows_g), 0) // frames
    same_n = q_stream_n == k_stream
    pair = 2 * head_size
    lane = lax.broadcasted_iota(jnp.int32, (rows_g, pair), 1)
    nt = (((1,), (1,)), ((), ()))
    for g in range(streams // GROUP):
        rows = pl.ds(g * rows_g, rows_g)
        srow = pl.ds(g * GROUP, GROUP)
        bias_n = jnp.where(same_n & (klive_ref[:, pl.ds(g * rows_g, rows_g)] > 0.0), 0.0, -1e30)

        def head_pair(p, carry):
            cols = pl.ds(pl.multiple_of(p * pair, pair), pair)
            q = qkv[0, rows, cols]
            k = qkv[1, rows, cols]
            v = qkv[2, rows, cols]
            ck = stv[srow, pl.ds(0, slot), cols].reshape(cols_g, pair)
            cv = stv[srow, pl.ds(slot, slot), cols].reshape(cols_g, pair)
            attended = None
            for half in range(pair // head_size):
                mine = (lane >= half * head_size) & (lane < (half + 1) * head_size)
                qh = jnp.where(mine, q, jnp.zeros_like(q))
                sc = lax.dot_general(qh, ck, nt, preferred_element_type=jnp.float32) + bias_c
                sn = lax.dot_general(qh, k, nt, preferred_element_type=jnp.float32) + bias_n
                top = jnp.maximum(jnp.max(sc, axis=-1, keepdims=True),
                                  jnp.max(sn, axis=-1, keepdims=True))
                ec = jnp.exp(sc - top)
                en = jnp.exp(sn - top)
                total = jnp.sum(ec, axis=-1, keepdims=True) + jnp.sum(en, axis=-1, keepdims=True)
                pc = ec.astype(jnp.bfloat16)
                pn = en.astype(jnp.bfloat16)
                oh = (jnp.dot(pc, cv, preferred_element_type=jnp.float32) + jnp.dot(
                    pn, v, preferred_element_type=jnp.float32)) * (1.0 / total)
                attended = oh if attended is None else jnp.where(mine, oh, attended)
            qkv[0, rows, cols] = attended.astype(jnp.bfloat16)
            return carry

        lax.fori_loop(0, width // pair, head_pair, 0)

    for c in copies:
        c.wait()
    mixed = jnp.dot(qkv[0], wobuf[...], preferred_element_type=jnp.float32)
    residual = x_ref[...].astype(jnp.float32) + mixed
    res_ref[...] = residual
    rounded = residual.astype(jnp.bfloat16).astype(jnp.float32).reshape(streams, frames, width)
    gather_wait(conv_part, 1)
    origin = kept - kept_real
    if early:
        pad_ref[:, 0:kept, :] = jnp.zeros((streams, kept, width), jnp.float32)
        pad_ref[:, kept:, :] = rounded
        conv_ref[...] = conv_in_ref[...]
        conv_rows(conv_ref, pad_ref, cw_ref, new_taps(taps, kept_real, frames), frames, origin)
    else:
        pad_ref[:, 0:kept, :] = stv[:, pl.ds(2 * slot, kept), :].astype(jnp.float32)
        pad_ref[:, kept:, :] = rounded
        conv_ref[...] = jnp.zeros_like(conv_ref)
        every = [list(range(0, frames, 8))] * taps
        conv_rows(conv_ref, pad_ref, cw_ref, every, frames, origin)
    live = rlive_ref[...].reshape(streams, frames, 1)

    def finish(c, carry):
        cols = pl.ds(pl.multiple_of(c * chunk, chunk), chunk)
        conv = conv_ref[:, :, cols]
        res = res_ref[:, cols]
        silu = conv / (1.0 + jnp.exp(-conv))
        out = (res.reshape(streams, frames, chunk) + silu) * live
        out_ref[:, cols] = out.reshape(tokens, chunk).astype(out_ref.dtype)
        return carry

    lax.fori_loop(0, width // chunk, finish, 0)


def project(inputs, qkv_weight):
    streams, frames, width = inputs.shape
    tokens = streams * frames
    x = inputs.reshape(tokens, width)
    kernel = functools.partial(projection_kernel, head_size=width // HEADS)
    return pl.pallas_call(
        kernel,
        out_shape=jax.ShapeDtypeStruct((3, tokens, width), jnp.bfloat16),
        grid=(3,),
        in_specs=[pl.BlockSpec((tokens, width), lambda i: (0, 0)),
                  pl.BlockSpec((width, width), lambda i: (0, i))],
        out_specs=pl.BlockSpec((1, tokens, width), lambda i: (i, 0, 0)),
        scratch_shapes=[pltpu.VMEM((tokens, width), jnp.bfloat16)],
        compiler_params=pltpu.CompilerParams(dimension_semantics=("arbitrary",)),
    )(x, qkv_weight)


def encoder_layer(inputs, valid_counts, sel, state, recv, qkv_weight, out_weight, conv_weight,
                  ctx, kept_real, conv_in=None, projected=None, fused=False):
    streams, frames, width = inputs.shape
    taps = conv_weight.shape[0]
    head_size = width // HEADS
    tokens = streams * frames
    slot = -(-ctx // 16) * 16
    live = (jnp.arange(frames, dtype=jnp.int32)[None, :] < valid_counts[:, None]).astype(jnp.float32)
    klive = live.reshape(1, tokens)
    rlive = live.reshape(tokens, 1)
    x = inputs.reshape(tokens, width)
    kept = state.shape[1] - 2 * slot
    early = conv_in is not None
    kernel = functools.partial(layer_kernel, streams=streams, frames=frames, ctx=ctx,
                               head_size=head_size, kept_real=kept_real, early=early,
                               fused=fused)
    vmem = pl.BlockSpec(memory_space=pltpu.VMEM)
    hbm = pl.BlockSpec(memory_space=pl.ANY)
    extra = [conv_in] if early else []
    out = pl.pallas_call(
        kernel,
        out_shape=jax.ShapeDtypeStruct((tokens, width), jnp.bfloat16),
        in_specs=[pl.BlockSpec(memory_space=pltpu.SMEM), vmem, vmem, vmem, vmem,
                  hbm, hbm, hbm, hbm] + [vmem] * len(extra),
        out_specs=vmem,
        scratch_shapes=[
            pltpu.VMEM((width, width), jnp.bfloat16),
            pltpu.VMEM((streams,) + state.shape[1:], jnp.bfloat16),
            pltpu.VMEM((3, tokens, width), jnp.bfloat16),
            pltpu.VMEM((streams, frames, width), jnp.float32),
            pltpu.VMEM((streams, kept + frames, width), jnp.float32),
            pltpu.VMEM((tokens, width), jnp.float32),
            pltpu.SemaphoreType.DMA((2, width // CHUNK_ROWS)),
            pltpu.SemaphoreType.DMA((2, streams)),
        ] + ([pltpu.VMEM((width, 3 * width), jnp.bfloat16)] if fused else []),
    )(sel, x, klive, rlive, conv_weight,
      qkv_weight if fused else (project(inputs, qkv_weight) if projected is None else projected),
      out_weight, state, recv, *extra)
    return out.reshape(streams, frames, width)


def migrate(anchor, own, count, local_count, state):
    total = anchor.shape[0]
    every_slot = jnp.arange(total, dtype=jnp.int32)
    mine = own * local_count + jnp.arange(local_count, dtype=jnp.int32)
    mine_new = jnp.sum(jnp.where(anchor[None, :] == mine[:, None], every_slot[None, :], 0), axis=1)
    target = mine_new // local_count
    hosts = jnp.arange(count, dtype=jnp.int32)
    match = target[None, :] == hosts[:, None]
    send_slot = jnp.sum(jnp.where(match, jnp.arange(local_count, dtype=jnp.int32)[None, :], 0),
                        axis=1)
    send = jnp.take(state, jnp.clip(send_slot, 0, local_count - 1), axis=0, mode="clip")
    mine_old = lax.dynamic_slice_in_dim(anchor, own * local_count, local_count)
    source = mine_old // local_count
    staying = source == own
    local_idx = jnp.clip(mine_old - own * local_count, 0, local_count - 1)
    recv_idx = jnp.clip(source, 0, count - 1)
    sel = jnp.concatenate([jnp.where(staying, 0, 1), jnp.where(staying, local_idx, recv_idx)])
    return sel.astype(jnp.int32), send


def exchange(send):
    return lax.all_to_all(send, "stream", 0, 0, tiled=True)


def body(
    new_frames, valid_counts, anchor, context_cache, conv_state, qkv_weight, out_weight, conv_weight
):
    local_count = new_frames.shape[0]
    own = lax.axis_index("stream")
    count = lax.axis_size("stream")
    ctx = context_cache.shape[2]
    width = conv_state.shape[3]
    slot = -(-ctx // 16) * 16
    kept = conv_state.shape[2]
    lead = (-kept) % 16
    context = context_cache[0]
    state = jnp.concatenate([
        jnp.pad(context[:, :, :width], ((0, 0), (0, slot - ctx), (0, 0))),
        jnp.pad(context[:, :, width:], ((0, 0), (0, slot - ctx), (0, 0))),
        jnp.pad(conv_state[0], ((0, 0), (lead, 0), (0, 0))),
    ], axis=1)
    sel, send = migrate(anchor, own, count, local_count, state)
    valid_here = lax.dynamic_slice_in_dim(valid_counts, own * local_count, local_count)
    section_index = lax.axis_index("section")
    layer = functools.partial(encoder_layer, valid_counts=valid_here, sel=sel, state=state,
                              qkv_weight=qkv_weight[0], out_weight=out_weight[0],
                              conv_weight=conv_weight[0], ctx=ctx, kept_real=kept)
    on_first = section_index == 0
    frames = new_frames.shape[1]
    like = lambda shape, dtype: (lambda: jnp.zeros(shape, dtype))

    def early_branch():
        return exchange(send), project(new_frames, qkv_weight[0])

    recv0, projected = lax.cond(
        on_first, early_branch,
        lambda: (jnp.zeros_like(send), jnp.zeros((3, local_count * frames, width), jnp.bfloat16)))
    token = shifted(recv0[:1, :8, :128], "section", 1)
    zero = jnp.where(on_first, 0.0, jnp.sum(token.astype(jnp.float32)) * 0.0)
    sel0 = sel + zero.astype(sel.dtype)
    first = lax.cond(on_first,
                     lambda: layer(new_frames, sel=sel0, recv=recv0, projected=projected),
                     like(new_frames.shape, new_frames.dtype))

    recv1 = lax.cond(on_first, lambda: jnp.zeros_like(send),
                     lambda: exchange(send + zero.astype(send.dtype)))
    inbound = shifted(first, "section", 1)
    result = lax.cond(on_first, lambda: first, lambda: layer(inbound, recv=recv1, fused=True))
    return result[None]


def solution(mesh):
    return jax.shard_map(
        body,
        mesh=mesh,
        in_specs=(
            P(("groups", "stream"), None, None),
            P("groups"),
            P("groups"),
            P("section", ("groups", "stream"), None, None),
            P("section", ("groups", "stream"), None, None),
            P("section", None, None),
            P("section", None, None),
            P("section", None, None),
        ),
        out_specs=P("section", ("groups", "stream"), None, None),
        check_vma=False,
    )
```

```python
import functools

import jax
import jax.numpy as jnp
from jax import lax
from jax.experimental import pallas as pl
from jax.experimental.pallas import tpu as pltpu
from jax.sharding import PartitionSpec as P

HEADS = 16
GROUP = 16
CHUNK_ROWS = 128


def shifted(value, axis, steps):
    count = lax.axis_size(axis)
    leading, last = (max(0, -steps), min(count, count - steps))
    return lax.ppermute(value, axis, [(source, source + steps) for source in range(leading, last)])


def projection_kernel(x_ref, w_ref, out_ref, nrm_ref, *, head_size):
    step = pl.program_id(0)

    @pl.when(step == 0)
    def _():
        floats = x_ref[...].astype(jnp.float32)
        centred = floats - jnp.mean(floats, axis=-1, keepdims=True)
        variance = jnp.mean(centred * centred, axis=-1, keepdims=True)
        nrm_ref[...] = (centred * lax.rsqrt(variance + 1e-05)).astype(jnp.bfloat16)

    part = jnp.dot(nrm_ref[...], w_ref[...], preferred_element_type=jnp.float32)
    scale = jnp.where(step == 0, head_size ** -0.5, 1.0).astype(jnp.float32)
    out_ref[0] = (part * scale).astype(out_ref.dtype)


def conv_rows(conv_ref, pad_ref, cw_ref, tap_rows, frames, origin):
    width = cw_ref.shape[1]
    chunk = 256

    def conv_chunk(c, carry):
        cols = pl.ds(pl.multiple_of(c * chunk, chunk), chunk)
        for lo in range(0, frames, 8):
            conv = conv_ref[:, pl.ds(lo, 8), cols]
            for j, rows in enumerate(tap_rows):
                if lo in rows:
                    conv = conv + cw_ref[pl.ds(j, 1), cols].reshape(1, 1, chunk) * pad_ref[
                        :, pl.ds(origin + j + lo, 8), cols]
            conv_ref[:, pl.ds(lo, 8), cols] = conv
        return carry

    lax.fori_loop(0, width // chunk, conv_chunk, 0)


def kept_taps(taps, kept, frames):
    return [[lo for lo in range(0, frames, 8) if lo < kept - j] for j in range(taps)]


def new_taps(taps, kept, frames):
    return [[lo for lo in range(0, frames, 8) if lo + 7 >= kept - j] for j in range(taps)]


def kept_conv_kernel(sel_ref, cw_ref, state_hbm, recv_hbm, out_ref, stv, pad_ref, gsem, *,
                     streams, frames, slot, kept):
    width = cw_ref.shape[1]
    rows = pad_ref.shape[1] - frames
    for j in range(streams):
        kind = sel_ref[j]
        idx = sel_ref[streams + j]

        @pl.when(kind == 0)
        def _():
            pltpu.make_async_copy(state_hbm.at[idx, pl.ds(2 * slot, rows)], stv.at[j],
                                  gsem.at[j]).start()

        @pl.when(kind != 0)
        def _():
            pltpu.make_async_copy(recv_hbm.at[idx, pl.ds(2 * slot, rows)], stv.at[j],
                                  gsem.at[j]).start()

    for j in range(streams):
        pltpu.make_async_copy(state_hbm.at[0, pl.ds(2 * slot, rows)], stv.at[j], gsem.at[j]).wait()
    pad_ref[:, 0:rows, :] = stv[...].astype(jnp.float32)
    pad_ref[:, rows:, :] = jnp.zeros((streams, frames, width), jnp.float32)
    out_ref[...] = jnp.zeros_like(out_ref)
    taps = cw_ref.shape[0]
    conv_rows(out_ref, pad_ref, cw_ref, kept_taps(taps, kept, frames), frames, rows - kept)


def kept_conv(sel, state, recv, conv_weight, streams, frames, ctx, kept):
    slot = -(-ctx // 16) * 16
    rows = state.shape[1] - 2 * slot
    width = state.shape[2]
    kernel = functools.partial(kept_conv_kernel, streams=streams, frames=frames, slot=slot,
                               kept=kept)
    vmem = pl.BlockSpec(memory_space=pltpu.VMEM)
    hbm = pl.BlockSpec(memory_space=pl.ANY)
    return pl.pallas_call(
        kernel,
        out_shape=jax.ShapeDtypeStruct((streams, frames, width), jnp.float32),
        in_specs=[pl.BlockSpec(memory_space=pltpu.SMEM), vmem, hbm, hbm],
        out_specs=vmem,
        scratch_shapes=[
            pltpu.VMEM((streams, rows, width), jnp.bfloat16),
            pltpu.VMEM((streams, rows + frames, width), jnp.float32),
            pltpu.SemaphoreType.DMA((streams,)),
        ],
    )(sel, conv_weight, state, recv)


def layer_kernel(sel_ref, x_ref, klive_ref, rlive_ref, cw_ref, qkv_hbm, wo_hbm, state_hbm,
                 recv_hbm, *rest, streams, frames, ctx, head_size, kept_real, early, fused):
    if fused:
        wbuf = rest[-1]
        rest = rest[:-1]
    if early:
        conv_in_ref, out_ref, wobuf, stv, qkv, conv_ref, pad_ref, res_ref, wsem, gsem = rest
    else:
        out_ref, wobuf, stv, qkv, conv_ref, pad_ref, res_ref, wsem, gsem = rest
    tokens = streams * frames
    width = x_ref.shape[1]
    slot = -(-ctx // 16) * 16
    kept = pad_ref.shape[1] - frames
    taps = cw_ref.shape[0]
    chunk = 128

    keys_rows = pl.ds(0, 2 * slot)
    conv_part = pl.ds(2 * slot, stv.shape[1] - 2 * slot)

    def gather(part, which):
        for j in range(streams):
            kind = sel_ref[j]
            idx = sel_ref[streams + j]

            @pl.when(kind == 0)
            def _():
                pltpu.make_async_copy(state_hbm.at[idx, part], stv.at[j, part],
                                      gsem.at[which, j]).start()

            @pl.when(kind != 0)
            def _():
                pltpu.make_async_copy(recv_hbm.at[idx, part], stv.at[j, part],
                                      gsem.at[which, j]).start()

    def gather_wait(part, which):
        for j in range(streams):
            pltpu.make_async_copy(state_hbm.at[0, part], stv.at[j, part], gsem.at[which, j]).wait()

    rows_w = wo_hbm.shape[0]
    if fused:
        first = []
        for r in range(rows_w // CHUNK_ROWS):
            part = pl.ds(r * CHUNK_ROWS, CHUNK_ROWS)
            first.append(pltpu.make_async_copy(qkv_hbm.at[part], wbuf.at[part], wsem.at[0, r]))
    else:
        first = [pltpu.make_async_copy(qkv_hbm, qkv, wsem.at[0, 0])]
    copies = []
    for r in range(rows_w // CHUNK_ROWS):
        part = pl.ds(r * CHUNK_ROWS, CHUNK_ROWS)
        copies.append(pltpu.make_async_copy(wo_hbm.at[part], wobuf.at[part], wsem.at[1, r]))
    for c in first:
        c.start()
    gather(keys_rows, 0)
    for c in copies:
        c.start()
    gather(conv_part, 1)

    if fused:
        floats = x_ref[...].astype(jnp.float32)
        centred = floats - jnp.mean(floats, axis=-1, keepdims=True)
        variance = jnp.mean(centred * centred, axis=-1, keepdims=True)
        normed = (centred * lax.rsqrt(variance + 1e-05)).astype(jnp.bfloat16)
    for c in first:
        c.wait()
    if fused:
        for i in range(3):
            part = jnp.dot(normed, wbuf[:, pl.ds(i * width, width)],
                           preferred_element_type=jnp.float32)
            if i == 0:
                part = part * (head_size ** -0.5)
            qkv[i] = part.astype(jnp.bfloat16)
    gather_wait(keys_rows, 0)

    rows_g = GROUP * frames
    cols_g = GROUP * slot
    q_stream = lax.broadcasted_iota(jnp.int32, (rows_g, cols_g), 0) // frames
    c_col = lax.broadcasted_iota(jnp.int32, (rows_g, cols_g), 1)
    bias_c = jnp.where((c_col // slot == q_stream) & (c_col % slot < ctx), 0.0, -1e30)
    k_stream = lax.broadcasted_iota(jnp.int32, (rows_g, rows_g), 1) // frames
    q_stream_n = lax.broadcasted_iota(jnp.int32, (rows_g, rows_g), 0) // frames
    same_n = q_stream_n == k_stream
    pair = 2 * head_size
    lane = lax.broadcasted_iota(jnp.int32, (rows_g, pair), 1)
    nt = (((1,), (1,)), ((), ()))
    for g in range(streams // GROUP):
        rows = pl.ds(g * rows_g, rows_g)
        srow = pl.ds(g * GROUP, GROUP)
        bias_n = jnp.where(same_n & (klive_ref[:, pl.ds(g * rows_g, rows_g)] > 0.0), 0.0, -1e30)

        def head_pair(p, carry):
            cols = pl.ds(pl.multiple_of(p * pair, pair), pair)
            q = qkv[0, rows, cols]
            k = qkv[1, rows, cols]
            v = qkv[2, rows, cols]
            ck = stv[srow, pl.ds(0, slot), cols].reshape(cols_g, pair)
            cv = stv[srow, pl.ds(slot, slot), cols].reshape(cols_g, pair)
            attended = None
            for half in range(pair // head_size):
                mine = (lane >= half * head_size) & (lane < (half + 1) * head_size)
                qh = jnp.where(mine, q, jnp.zeros_like(q))
                sc = lax.dot_general(qh, ck, nt, preferred_element_type=jnp.float32) + bias_c
                sn = lax.dot_general(qh, k, nt, preferred_element_type=jnp.float32) + bias_n
                top = jnp.maximum(jnp.max(sc, axis=-1, keepdims=True),
                                  jnp.max(sn, axis=-1, keepdims=True))
                ec = jnp.exp(sc - top)
                en = jnp.exp(sn - top)
                total = jnp.sum(ec, axis=-1, keepdims=True) + jnp.sum(en, axis=-1, keepdims=True)
                pc = ec.astype(jnp.bfloat16)
                pn = en.astype(jnp.bfloat16)
                oh = (jnp.dot(pc, cv, preferred_element_type=jnp.float32) + jnp.dot(
                    pn, v, preferred_element_type=jnp.float32)) * (1.0 / total)
                attended = oh if attended is None else jnp.where(mine, oh, attended)
            qkv[0, rows, cols] = attended.astype(jnp.bfloat16)
            return carry

        lax.fori_loop(0, width // pair, head_pair, 0)

    for c in copies:
        c.wait()
    mixed = jnp.dot(qkv[0], wobuf[...], preferred_element_type=jnp.float32)
    residual = x_ref[...].astype(jnp.float32) + mixed
    res_ref[...] = residual
    rounded = residual.astype(jnp.bfloat16).astype(jnp.float32).reshape(streams, frames, width)
    gather_wait(conv_part, 1)
    origin = kept - kept_real
    if early:
        pad_ref[:, 0:kept, :] = jnp.zeros((streams, kept, width), jnp.float32)
        pad_ref[:, kept:, :] = rounded
        conv_ref[...] = conv_in_ref[...]
        conv_rows(conv_ref, pad_ref, cw_ref, new_taps(taps, kept_real, frames), frames, origin)
    else:
        pad_ref[:, 0:kept, :] = stv[:, pl.ds(2 * slot, kept), :].astype(jnp.float32)
        pad_ref[:, kept:, :] = rounded
        conv_ref[...] = jnp.zeros_like(conv_ref)
        every = [list(range(0, frames, 8))] * taps
        conv_rows(conv_ref, pad_ref, cw_ref, every, frames, origin)
    live = rlive_ref[...].reshape(streams, frames, 1)

    def finish(c, carry):
        cols = pl.ds(pl.multiple_of(c * chunk, chunk), chunk)
        conv = conv_ref[:, :, cols]
        res = res_ref[:, cols]
        silu = conv / (1.0 + jnp.exp(-conv))
        out = (res.reshape(streams, frames, chunk) + silu) * live
        out_ref[:, cols] = out.reshape(tokens, chunk).astype(out_ref.dtype)
        return carry

    lax.fori_loop(0, width // chunk, finish, 0)


def project(inputs, qkv_weight):
    streams, frames, width = inputs.shape
    tokens = streams * frames
    x = inputs.reshape(tokens, width)
    kernel = functools.partial(projection_kernel, head_size=width // HEADS)
    return pl.pallas_call(
        kernel,
        out_shape=jax.ShapeDtypeStruct((3, tokens, width), jnp.bfloat16),
        grid=(3,),
        in_specs=[pl.BlockSpec((tokens, width), lambda i: (0, 0)),
                  pl.BlockSpec((width, width), lambda i: (0, i))],
        out_specs=pl.BlockSpec((1, tokens, width), lambda i: (i, 0, 0)),
        scratch_shapes=[pltpu.VMEM((tokens, width), jnp.bfloat16)],
        compiler_params=pltpu.CompilerParams(dimension_semantics=("arbitrary",)),
    )(x, qkv_weight)


def encoder_layer(inputs, valid_counts, sel, state, recv, qkv_weight, out_weight, conv_weight,
                  ctx, kept_real, conv_in=None, projected=None, fused=False):
    streams, frames, width = inputs.shape
    taps = conv_weight.shape[0]
    head_size = width // HEADS
    tokens = streams * frames
    slot = -(-ctx // 16) * 16
    live = (jnp.arange(frames, dtype=jnp.int32)[None, :] < valid_counts[:, None]).astype(jnp.float32)
    klive = live.reshape(1, tokens)
    rlive = live.reshape(tokens, 1)
    x = inputs.reshape(tokens, width)
    kept = state.shape[1] - 2 * slot
    early = conv_in is not None
    kernel = functools.partial(layer_kernel, streams=streams, frames=frames, ctx=ctx,
                               head_size=head_size, kept_real=kept_real, early=early,
                               fused=fused)
    vmem = pl.BlockSpec(memory_space=pltpu.VMEM)
    hbm = pl.BlockSpec(memory_space=pl.ANY)
    extra = [conv_in] if early else []
    out = pl.pallas_call(
        kernel,
        out_shape=jax.ShapeDtypeStruct((tokens, width), jnp.bfloat16),
        in_specs=[pl.BlockSpec(memory_space=pltpu.SMEM), vmem, vmem, vmem, vmem,
                  hbm, hbm, hbm, hbm] + [vmem] * len(extra),
        out_specs=vmem,
        scratch_shapes=[
            pltpu.VMEM((width, width), jnp.bfloat16),
            pltpu.VMEM((streams,) + state.shape[1:], jnp.bfloat16),
            pltpu.VMEM((3, tokens, width), jnp.bfloat16),
            pltpu.VMEM((streams, frames, width), jnp.float32),
            pltpu.VMEM((streams, kept + frames, width), jnp.float32),
            pltpu.VMEM((tokens, width), jnp.float32),
            pltpu.SemaphoreType.DMA((2, width // CHUNK_ROWS)),
            pltpu.SemaphoreType.DMA((2, streams)),
        ] + ([pltpu.VMEM((width, 3 * width), jnp.bfloat16)] if fused else []),
    )(sel, x, klive, rlive, conv_weight,
      qkv_weight if fused else (project(inputs, qkv_weight) if projected is None else projected),
      out_weight, state, recv, *extra)
    return out.reshape(streams, frames, width)


def migrate(anchor, own, count, local_count, state):
    total = anchor.shape[0]
    every_slot = jnp.arange(total, dtype=jnp.int32)
    mine = own * local_count + jnp.arange(local_count, dtype=jnp.int32)
    mine_new = jnp.sum(jnp.where(anchor[None, :] == mine[:, None], every_slot[None, :], 0), axis=1)
    target = mine_new // local_count
    hosts = jnp.arange(count, dtype=jnp.int32)
    match = target[None, :] == hosts[:, None]
    send_slot = jnp.sum(jnp.where(match, jnp.arange(local_count, dtype=jnp.int32)[None, :], 0),
                        axis=1)
    send = jnp.take(state, jnp.clip(send_slot, 0, local_count - 1), axis=0, mode="clip")
    mine_old = lax.dynamic_slice_in_dim(anchor, own * local_count, local_count)
    source = mine_old // local_count
    staying = source == own
    local_idx = jnp.clip(mine_old - own * local_count, 0, local_count - 1)
    recv_idx = jnp.clip(source, 0, count - 1)
    sel = jnp.concatenate([jnp.where(staying, 0, 1), jnp.where(staying, local_idx, recv_idx)])
    return sel.astype(jnp.int32), send


def exchange(send):
    return lax.all_to_all(send, "stream", 0, 0, tiled=True)


def body(
    new_frames, valid_counts, anchor, context_cache, conv_state, qkv_weight, out_weight, conv_weight
):
    local_count = new_frames.shape[0]
    own = lax.axis_index("stream")
    count = lax.axis_size("stream")
    ctx = context_cache.shape[2]
    width = conv_state.shape[3]
    slot = -(-ctx // 16) * 16
    kept = conv_state.shape[2]
    lead = (-kept) % 16
    context = context_cache[0]
    state = jnp.concatenate([
        jnp.pad(context[:, :, :width], ((0, 0), (0, slot - ctx), (0, 0))),
        jnp.pad(context[:, :, width:], ((0, 0), (0, slot - ctx), (0, 0))),
        jnp.pad(conv_state[0], ((0, 0), (lead, 0), (0, 0))),
    ], axis=1)
    sel, send = migrate(anchor, own, count, local_count, state)
    valid_here = lax.dynamic_slice_in_dim(valid_counts, own * local_count, local_count)
    section_index = lax.axis_index("section")
    layer = functools.partial(encoder_layer, valid_counts=valid_here, sel=sel, state=state,
                              qkv_weight=qkv_weight[0], out_weight=out_weight[0],
                              conv_weight=conv_weight[0], ctx=ctx, kept_real=kept)
    on_first = section_index == 0
    frames = new_frames.shape[1]
    like = lambda shape, dtype: (lambda: jnp.zeros(shape, dtype))

    def early_branch():
        return exchange(send), project(new_frames, qkv_weight[0])

    recv0, projected = lax.cond(
        on_first, early_branch,
        lambda: (jnp.zeros_like(send), jnp.zeros((3, local_count * frames, width), jnp.bfloat16)))
    token = shifted(recv0[:1, :8], "section", 1)
    zero = jnp.where(on_first, 0.0, jnp.sum(token.astype(jnp.float32)) * 0.0)
    sel0 = sel + zero.astype(sel.dtype)
    first = lax.cond(on_first,
                     lambda: layer(new_frames, sel=sel0, recv=recv0, projected=projected),
                     like(new_frames.shape, new_frames.dtype))

    recv1 = lax.cond(on_first, lambda: jnp.zeros_like(send),
                     lambda: exchange(send + zero.astype(send.dtype)))
    inbound = shifted(first, "section", 1)
    result = lax.cond(on_first, lambda: first, lambda: layer(inbound, recv=recv1, fused=True))
    return result[None]


def solution(mesh):
    return jax.shard_map(
        body,
        mesh=mesh,
        in_specs=(
            P(("groups", "stream"), None, None),
            P("groups"),
            P("groups"),
            P("section", ("groups", "stream"), None, None),
            P("section", ("groups", "stream"), None, None),
            P("section", None, None),
            P("section", None, None),
            P("section", None, None),
        ),
        out_specs=P("section", ("groups", "stream"), None, None),
        check_vma=False,
    )
```

```python
import functools

import jax
import jax.numpy as jnp
from jax import lax
from jax.experimental import pallas as pl
from jax.experimental.pallas import tpu as pltpu
from jax.sharding import PartitionSpec as P

HEADS = 16
GROUP = 16
CHUNK_ROWS = 512


def shifted(value, axis, steps):
    count = lax.axis_size(axis)
    leading, last = (max(0, -steps), min(count, count - steps))
    return lax.ppermute(value, axis, [(source, source + steps) for source in range(leading, last)])


def projection_kernel(x_ref, w_ref, out_ref, nrm_ref, *, head_size):
    step = pl.program_id(0)

    @pl.when(step == 0)
    def _():
        floats = x_ref[...].astype(jnp.float32)
        centred = floats - jnp.mean(floats, axis=-1, keepdims=True)
        variance = jnp.mean(centred * centred, axis=-1, keepdims=True)
        nrm_ref[...] = (centred * lax.rsqrt(variance + 1e-05)).astype(jnp.bfloat16)

    part = jnp.dot(nrm_ref[...], w_ref[...], preferred_element_type=jnp.float32)
    scale = jnp.where(step == 0, head_size ** -0.5, 1.0).astype(jnp.float32)
    out_ref[0] = (part * scale).astype(out_ref.dtype)


def conv_rows(conv_ref, pad_ref, cw_ref, tap_rows, frames, origin):
    width = cw_ref.shape[1]
    chunk = 128

    def conv_chunk(c, carry):
        cols = pl.ds(pl.multiple_of(c * chunk, chunk), chunk)
        for lo in range(0, frames, 8):
            conv = conv_ref[:, pl.ds(lo, 8), cols]
            for j, rows in enumerate(tap_rows):
                if lo in rows:
                    conv = conv + cw_ref[pl.ds(j, 1), cols].reshape(1, 1, chunk) * pad_ref[
                        :, pl.ds(origin + j + lo, 8), cols]
            conv_ref[:, pl.ds(lo, 8), cols] = conv
        return carry

    lax.fori_loop(0, width // chunk, conv_chunk, 0)


def kept_taps(taps, kept, frames):
    return [[lo for lo in range(0, frames, 8) if lo < kept - j] for j in range(taps)]


def new_taps(taps, kept, frames):
    return [[lo for lo in range(0, frames, 8) if lo + 7 >= kept - j] for j in range(taps)]


def kept_conv_kernel(sel_ref, cw_ref, state_hbm, recv_hbm, out_ref, stv, pad_ref, gsem, *,
                     streams, frames, slot, kept):
    width = cw_ref.shape[1]
    rows = pad_ref.shape[1] - frames
    for j in range(streams):
        kind = sel_ref[j]
        idx = sel_ref[streams + j]

        @pl.when(kind == 0)
        def _():
            pltpu.make_async_copy(state_hbm.at[idx, pl.ds(2 * slot, rows)], stv.at[j],
                                  gsem.at[j]).start()

        @pl.when(kind != 0)
        def _():
            pltpu.make_async_copy(recv_hbm.at[idx, pl.ds(2 * slot, rows)], stv.at[j],
                                  gsem.at[j]).start()

    for j in range(streams):
        pltpu.make_async_copy(state_hbm.at[0, pl.ds(2 * slot, rows)], stv.at[j], gsem.at[j]).wait()
    pad_ref[:, 0:rows, :] = stv[...].astype(jnp.float32)
    pad_ref[:, rows:, :] = jnp.zeros((streams, frames, width), jnp.float32)
    out_ref[...] = jnp.zeros_like(out_ref)
    taps = cw_ref.shape[0]
    conv_rows(out_ref, pad_ref, cw_ref, kept_taps(taps, kept, frames), frames, rows - kept)


def kept_conv(sel, state, recv, conv_weight, streams, frames, ctx, kept):
    slot = -(-ctx // 16) * 16
    rows = state.shape[1] - 2 * slot
    width = state.shape[2]
    kernel = functools.partial(kept_conv_kernel, streams=streams, frames=frames, slot=slot,
                               kept=kept)
    vmem = pl.BlockSpec(memory_space=pltpu.VMEM)
    hbm = pl.BlockSpec(memory_space=pl.ANY)
    return pl.pallas_call(
        kernel,
        out_shape=jax.ShapeDtypeStruct((streams, frames, width), jnp.float32),
        in_specs=[pl.BlockSpec(memory_space=pltpu.SMEM), vmem, hbm, hbm],
        out_specs=vmem,
        scratch_shapes=[
            pltpu.VMEM((streams, rows, width), jnp.bfloat16),
            pltpu.VMEM((streams, rows + frames, width), jnp.float32),
            pltpu.SemaphoreType.DMA((streams,)),
        ],
    )(sel, conv_weight, state, recv)


def layer_kernel(sel_ref, x_ref, klive_ref, rlive_ref, cw_ref, qkv_hbm, wo_hbm, state_hbm,
                 recv_hbm, *rest, streams, frames, ctx, head_size, kept_real, early, fused):
    if fused:
        wbuf = rest[-1]
        rest = rest[:-1]
    if early:
        conv_in_ref, out_ref, wobuf, stv, qkv, conv_ref, pad_ref, res_ref, wsem, gsem = rest
    else:
        out_ref, wobuf, stv, qkv, conv_ref, pad_ref, res_ref, wsem, gsem = rest
    tokens = streams * frames
    width = x_ref.shape[1]
    slot = -(-ctx // 16) * 16
    kept = pad_ref.shape[1] - frames
    taps = cw_ref.shape[0]
    chunk = 128

    keys_rows = pl.ds(0, 2 * slot)
    conv_part = pl.ds(2 * slot, stv.shape[1] - 2 * slot)

    def gather(part, which):
        for j in range(streams):
            kind = sel_ref[j]
            idx = sel_ref[streams + j]

            @pl.when(kind == 0)
            def _():
                pltpu.make_async_copy(state_hbm.at[idx, part], stv.at[j, part],
                                      gsem.at[which, j]).start()

            @pl.when(kind != 0)
            def _():
                pltpu.make_async_copy(recv_hbm.at[idx, part], stv.at[j, part],
                                      gsem.at[which, j]).start()

    def gather_wait(part, which):
        for j in range(streams):
            pltpu.make_async_copy(state_hbm.at[0, part], stv.at[j, part], gsem.at[which, j]).wait()

    rows_w = wo_hbm.shape[0]
    if fused:
        first = []
        for r in range(rows_w // CHUNK_ROWS):
            part = pl.ds(r * CHUNK_ROWS, CHUNK_ROWS)
            first.append(pltpu.make_async_copy(qkv_hbm.at[part], wbuf.at[part], wsem.at[0, r]))
    else:
        first = [pltpu.make_async_copy(qkv_hbm, qkv, wsem.at[0, 0])]
    copies = []
    for r in range(rows_w // CHUNK_ROWS):
        part = pl.ds(r * CHUNK_ROWS, CHUNK_ROWS)
        copies.append(pltpu.make_async_copy(wo_hbm.at[part], wobuf.at[part], wsem.at[1, r]))
    for c in first:
        c.start()
    gather(keys_rows, 0)
    for c in copies:
        c.start()
    gather(conv_part, 1)

    if fused:
        floats = x_ref[...].astype(jnp.float32)
        centred = floats - jnp.mean(floats, axis=-1, keepdims=True)
        variance = jnp.mean(centred * centred, axis=-1, keepdims=True)
        normed = (centred * lax.rsqrt(variance + 1e-05)).astype(jnp.bfloat16)
    for c in first:
        c.wait()
    if fused:
        for i in range(3):
            part = jnp.dot(normed, wbuf[:, pl.ds(i * width, width)],
                           preferred_element_type=jnp.float32)
            if i == 0:
                part = part * (head_size ** -0.5)
            qkv[i] = part.astype(jnp.bfloat16)
    gather_wait(keys_rows, 0)

    rows_g = GROUP * frames
    cols_g = GROUP * slot
    q_stream = lax.broadcasted_iota(jnp.int32, (rows_g, cols_g), 0) // frames
    c_col = lax.broadcasted_iota(jnp.int32, (rows_g, cols_g), 1)
    bias_c = jnp.where((c_col // slot == q_stream) & (c_col % slot < ctx), 0.0, -1e30)
    k_stream = lax.broadcasted_iota(jnp.int32, (rows_g, rows_g), 1) // frames
    q_stream_n = lax.broadcasted_iota(jnp.int32, (rows_g, rows_g), 0) // frames
    same_n = q_stream_n == k_stream
    pair = 2 * head_size
    lane = lax.broadcasted_iota(jnp.int32, (rows_g, pair), 1)
    nt = (((1,), (1,)), ((), ()))
    for g in range(streams // GROUP):
        rows = pl.ds(g * rows_g, rows_g)
        srow = pl.ds(g * GROUP, GROUP)
        bias_n = jnp.where(same_n & (klive_ref[:, pl.ds(g * rows_g, rows_g)] > 0.0), 0.0, -1e30)

        def head_pair(p, carry):
            cols = pl.ds(pl.multiple_of(p * pair, pair), pair)
            q = qkv[0, rows, cols]
            k = qkv[1, rows, cols]
            v = qkv[2, rows, cols]
            ck = stv[srow, pl.ds(0, slot), cols].reshape(cols_g, pair)
            cv = stv[srow, pl.ds(slot, slot), cols].reshape(cols_g, pair)
            attended = None
            for half in range(pair // head_size):
                mine = (lane >= half * head_size) & (lane < (half + 1) * head_size)
                qh = jnp.where(mine, q, jnp.zeros_like(q))
                sc = lax.dot_general(qh, ck, nt, preferred_element_type=jnp.float32) + bias_c
                sn = lax.dot_general(qh, k, nt, preferred_element_type=jnp.float32) + bias_n
                top = jnp.maximum(jnp.max(sc, axis=-1, keepdims=True),
                                  jnp.max(sn, axis=-1, keepdims=True))
                ec = jnp.exp(sc - top)
                en = jnp.exp(sn - top)
                total = jnp.sum(ec, axis=-1, keepdims=True) + jnp.sum(en, axis=-1, keepdims=True)
                pc = ec.astype(jnp.bfloat16)
                pn = en.astype(jnp.bfloat16)
                oh = (jnp.dot(pc, cv, preferred_element_type=jnp.float32) + jnp.dot(
                    pn, v, preferred_element_type=jnp.float32)) * (1.0 / total)
                attended = oh if attended is None else jnp.where(mine, oh, attended)
            qkv[0, rows, cols] = attended.astype(jnp.bfloat16)
            return carry

        lax.fori_loop(0, width // pair, head_pair, 0)

    for c in copies:
        c.wait()
    mixed = jnp.dot(qkv[0], wobuf[...], preferred_element_type=jnp.float32)
    residual = x_ref[...].astype(jnp.float32) + mixed
    res_ref[...] = residual
    rounded = residual.astype(jnp.bfloat16).astype(jnp.float32).reshape(streams, frames, width)
    gather_wait(conv_part, 1)
    origin = kept - kept_real
    if early:
        pad_ref[:, 0:kept, :] = jnp.zeros((streams, kept, width), jnp.float32)
        pad_ref[:, kept:, :] = rounded
        conv_ref[...] = conv_in_ref[...]
        conv_rows(conv_ref, pad_ref, cw_ref, new_taps(taps, kept_real, frames), frames, origin)
    else:
        pad_ref[:, 0:kept, :] = stv[:, pl.ds(2 * slot, kept), :].astype(jnp.float32)
        pad_ref[:, kept:, :] = rounded
        conv_ref[...] = jnp.zeros_like(conv_ref)
        every = [list(range(0, frames, 8))] * taps
        conv_rows(conv_ref, pad_ref, cw_ref, every, frames, origin)
    live = rlive_ref[...].reshape(streams, frames, 1)

    def finish(c, carry):
        cols = pl.ds(pl.multiple_of(c * chunk, chunk), chunk)
        conv = conv_ref[:, :, cols]
        res = res_ref[:, cols]
        silu = conv / (1.0 + jnp.exp(-conv))
        out = (res.reshape(streams, frames, chunk) + silu) * live
        out_ref[:, cols] = out.reshape(tokens, chunk).astype(out_ref.dtype)
        return carry

    lax.fori_loop(0, width // chunk, finish, 0)


def project(inputs, qkv_weight):
    streams, frames, width = inputs.shape
    tokens = streams * frames
    x = inputs.reshape(tokens, width)
    kernel = functools.partial(projection_kernel, head_size=width // HEADS)
    return pl.pallas_call(
        kernel,
        out_shape=jax.ShapeDtypeStruct((3, tokens, width), jnp.bfloat16),
        grid=(3,),
        in_specs=[pl.BlockSpec((tokens, width), lambda i: (0, 0)),
                  pl.BlockSpec((width, width), lambda i: (0, i))],
        out_specs=pl.BlockSpec((1, tokens, width), lambda i: (i, 0, 0)),
        scratch_shapes=[pltpu.VMEM((tokens, width), jnp.bfloat16)],
        compiler_params=pltpu.CompilerParams(dimension_semantics=("arbitrary",)),
    )(x, qkv_weight)


def encoder_layer(inputs, valid_counts, sel, state, recv, qkv_weight, out_weight, conv_weight,
                  ctx, kept_real, conv_in=None, projected=None, fused=False):
    streams, frames, width = inputs.shape
    taps = conv_weight.shape[0]
    head_size = width // HEADS
    tokens = streams * frames
    slot = -(-ctx // 16) * 16
    live = (jnp.arange(frames, dtype=jnp.int32)[None, :] < valid_counts[:, None]).astype(jnp.float32)
    klive = live.reshape(1, tokens)
    rlive = live.reshape(tokens, 1)
    x = inputs.reshape(tokens, width)
    kept = state.shape[1] - 2 * slot
    early = conv_in is not None
    kernel = functools.partial(layer_kernel, streams=streams, frames=frames, ctx=ctx,
                               head_size=head_size, kept_real=kept_real, early=early,
                               fused=fused)
    vmem = pl.BlockSpec(memory_space=pltpu.VMEM)
    hbm = pl.BlockSpec(memory_space=pl.ANY)
    extra = [conv_in] if early else []
    out = pl.pallas_call(
        kernel,
        out_shape=jax.ShapeDtypeStruct((tokens, width), jnp.bfloat16),
        in_specs=[pl.BlockSpec(memory_space=pltpu.SMEM), vmem, vmem, vmem, vmem,
                  hbm, hbm, hbm, hbm] + [vmem] * len(extra),
        out_specs=vmem,
        scratch_shapes=[
            pltpu.VMEM((width, width), jnp.bfloat16),
            pltpu.VMEM((streams,) + state.shape[1:], jnp.bfloat16),
            pltpu.VMEM((3, tokens, width), jnp.bfloat16),
            pltpu.VMEM((streams, frames, width), jnp.float32),
            pltpu.VMEM((streams, kept + frames, width), jnp.float32),
            pltpu.VMEM((tokens, width), jnp.float32),
            pltpu.SemaphoreType.DMA((2, width // CHUNK_ROWS)),
            pltpu.SemaphoreType.DMA((2, streams)),
        ] + ([pltpu.VMEM((width, 3 * width), jnp.bfloat16)] if fused else []),
    )(sel, x, klive, rlive, conv_weight,
      qkv_weight if fused else (project(inputs, qkv_weight) if projected is None else projected),
      out_weight, state, recv, *extra)
    return out.reshape(streams, frames, width)


def migrate(anchor, own, count, local_count, state):
    total = anchor.shape[0]
    every_slot = jnp.arange(total, dtype=jnp.int32)
    mine = own * local_count + jnp.arange(local_count, dtype=jnp.int32)
    mine_new = jnp.sum(jnp.where(anchor[None, :] == mine[:, None], every_slot[None, :], 0), axis=1)
    target = mine_new // local_count
    hosts = jnp.arange(count, dtype=jnp.int32)
    match = target[None, :] == hosts[:, None]
    send_slot = jnp.sum(jnp.where(match, jnp.arange(local_count, dtype=jnp.int32)[None, :], 0),
                        axis=1)
    send = jnp.take(state, jnp.clip(send_slot, 0, local_count - 1), axis=0, mode="clip")
    mine_old = lax.dynamic_slice_in_dim(anchor, own * local_count, local_count)
    source = mine_old // local_count
    staying = source == own
    local_idx = jnp.clip(mine_old - own * local_count, 0, local_count - 1)
    recv_idx = jnp.clip(source, 0, count - 1)
    sel = jnp.concatenate([jnp.where(staying, 0, 1), jnp.where(staying, local_idx, recv_idx)])
    return sel.astype(jnp.int32), send


def exchange(send):
    return lax.all_to_all(send, "stream", 0, 0, tiled=True)


def body(
    new_frames, valid_counts, anchor, context_cache, conv_state, qkv_weight, out_weight, conv_weight
):
    local_count = new_frames.shape[0]
    own = lax.axis_index("stream")
    count = lax.axis_size("stream")
    ctx = context_cache.shape[2]
    width = conv_state.shape[3]
    slot = -(-ctx // 16) * 16
    kept = conv_state.shape[2]
    lead = (-kept) % 16
    context = context_cache[0]
    state = jnp.concatenate([
        jnp.pad(context[:, :, :width], ((0, 0), (0, slot - ctx), (0, 0))),
        jnp.pad(context[:, :, width:], ((0, 0), (0, slot - ctx), (0, 0))),
        jnp.pad(conv_state[0], ((0, 0), (lead, 0), (0, 0))),
    ], axis=1)
    sel, send = migrate(anchor, own, count, local_count, state)
    valid_here = lax.dynamic_slice_in_dim(valid_counts, own * local_count, local_count)
    section_index = lax.axis_index("section")
    layer = functools.partial(encoder_layer, valid_counts=valid_here, sel=sel, state=state,
                              qkv_weight=qkv_weight[0], out_weight=out_weight[0],
                              conv_weight=conv_weight[0], ctx=ctx, kept_real=kept)
    on_first = section_index == 0
    frames = new_frames.shape[1]
    like = lambda shape, dtype: (lambda: jnp.zeros(shape, dtype))

    def early_branch():
        return exchange(send), project(new_frames, qkv_weight[0])

    recv0, projected = lax.cond(
        on_first, early_branch,
        lambda: (jnp.zeros_like(send), jnp.zeros((3, local_count * frames, width), jnp.bfloat16)))
    token = shifted(recv0[:1, :8], "section", 1)
    zero = jnp.where(on_first, 0.0, jnp.sum(token.astype(jnp.float32)) * 0.0)
    sel0 = sel + zero.astype(sel.dtype)
    first = lax.cond(on_first,
                     lambda: layer(new_frames, sel=sel0, recv=recv0, projected=projected),
                     like(new_frames.shape, new_frames.dtype))

    recv1 = lax.cond(on_first, lambda: jnp.zeros_like(send),
                     lambda: exchange(send + zero.astype(send.dtype)))
    inbound = shifted(first, "section", 1)
    result = lax.cond(on_first, lambda: first, lambda: layer(inbound, recv=recv1, fused=True))
    return result[None]


def solution(mesh):
    return jax.shard_map(
        body,
        mesh=mesh,
        in_specs=(
            P(("groups", "stream"), None, None),
            P("groups"),
            P("groups"),
            P("section", ("groups", "stream"), None, None),
            P("section", ("groups", "stream"), None, None),
            P("section", None, None),
            P("section", None, None),
            P("section", None, None),
        ),
        out_specs=P("section", ("groups", "stream"), None, None),
        check_vma=False,
    )
```
